32 devices in a mesh: ctx: 16 (over z, x, core), head: 2 (over y).
Axes of the slice: x: 2, y: 2, z: 4, core: 2. Of those that a mesh axis runs over, the one named last changes fastest.
Arguments:
- queries: bfloat16 [8192, 1024], P('ctx', 'head'), may hold values from -6 to 6
- key_rows: bfloat16 [8192, 1024], P('ctx', 'head'), may hold values from -6 to 6
- values: bfloat16 [8192, 1024], P('ctx', 'head'), may hold values from -6 to 6
- outputs: bfloat16 [8192, 1024], P('ctx', 'head'), may hold values from -6 to 6
- out_grad: bfloat16 [8192, 1024], P('ctx', 'head'), may hold values from -48 to 48
- log_norm: bfloat16 [8, 8192], P('head', 'ctx'), may hold values from 4.5 to 7.5
- rand_blocks: int32 [64, 3], P('ctx'), may hold values from -1 to 61, as said below
Outputs:
- query_grad: bfloat16 [8192, 1024], P('ctx', 'head')
- key_grad: bfloat16 [8192, 1024], P('ctx', 'head')
- value_grad: bfloat16 [8192, 1024], P('ctx', 'head')
The draws below stay inside these ranges and needn't reach their ends.
Inputs may be any that keep to these rules, and one draw needn't show every extreme that they name: `rand_blocks`: an entry of row j is a sequence block index of a key block for the query block of row j, or -1 for none. A named block lies between 1 and that query block's sequence index minus 2; the blocks named in the 4 rows of one index of ctx lie on distinct indices of ctx, none of them index 0.
All inputs are finite; a program needn't handle non-finite values.
Results may differ from the reference program's by a relative error of at most 0.0065.
Values may be sent and summed in bfloat16 or wider, within the bound.
No kernel may reach another device: no remote copies, remote signals or barrier semaphores. Data moves between devices by JAX's collectives and lax.ppermute only.
A program may use at most 128 MiB of HBM per device.

```python
import jax
import jax.numpy as jnp
import numpy as np
from jax import lax

HEAD_DEV = 4
HD = 128
BLOCK = 128
PAIR = 2
WINDOW = 2
GLOBAL = 1
RANDOM = 3
HEADS = 8
TOKENS = 8192
N_CTX = 16


def draw_rand_blocks(key, part):
    slot_count = 2 * PAIR
    block_total = slot_count * N_CTX
    devices = jnp.arange(N_CTX, dtype=jnp.int32)
    perm_keys = jax.random.split(jax.random.fold_in(key, 11), N_CTX)
    owners = jax.vmap(lambda one_key: jax.random.permutation(one_key, N_CTX - 1))(perm_keys).astype(jnp.int32) + 1
    owners = owners[:, :slot_count * RANDOM].reshape(N_CTX, slot_count, RANDOM)
    within = jnp.arange(slot_count, dtype=jnp.int32)
    query_blk = jnp.where(within[None, :] < PAIR, PAIR * devices[:, None] + within[None, :], block_total - 1 - PAIR * devices[:, None] - (within[None, :] - PAIR))
    candidate = jnp.where(within < PAIR, PAIR * owners[..., None] + within, block_total - 1 - PAIR * owners[..., None] - (within - PAIR))
    allowed = (candidate >= GLOBAL) & (candidate <= query_blk[:, :, None, None] - WINDOW)
    scores = jax.random.randint(jax.random.fold_in(key, 12), candidate.shape, 0, 1 << 20) * slot_count + within
    scores = jnp.where(allowed, scores, -1)
    best = jnp.argmax(scores, axis=-1)
    chosen = jnp.take_along_axis(candidate, best[..., None], axis=-1)[..., 0]
    chosen = jnp.where(jnp.max(scores, axis=-1) >= 0, chosen, -1)
    return chosen.reshape(block_total, RANDOM).astype(jnp.int32)


def level_of(stream_key, shape, shards, least, top_value):
    factor_of, own = 1.0, jax.random.fold_in(stream_key, 6)
    for dim, shards_of in shards:
        heights = jnp.exp(jax.random.uniform(jax.random.fold_in(own, dim), (shards_of,), jnp.float32, least / len(shards), top_value / len(shards)))
        factor_of = factor_of * jnp.repeat(heights, shape[dim] // shards_of).reshape([-1 if axis == dim else 1 for axis in range(len(shape))])
    return factor_of


def gaussian(key, shape, width, reach, pieces=(), held_as=jnp.bfloat16):
    drawn = width * jax.random.normal(key, shape, jnp.float32)
    if pieces:
        drawn = drawn * level_of(key, shape, pieces, -0.22, 0.18)
    return jnp.clip(drawn, -reach, reach).astype(held_as)


def setup_inputs(seed: int = 0) -> dict:
    streams_of = jax.random.split(jax.random.key(seed), 8)
    return {
        "queries": gaussian(streams_of[0], (TOKENS, HEADS * HD), 1.0, 6.0, ((0, 16), (1, 2))),
        "key_rows": gaussian(streams_of[1], (TOKENS, HEADS * HD), 1.0, 6.0, ((0, 16), (1, 2))),
        "values": gaussian(streams_of[2], (TOKENS, HEADS * HD), 1.0, 6.0, ((0, 16), (1, 2))),
        "outputs": gaussian(streams_of[3], (TOKENS, HEADS * HD), 1.0, 6.0, ((0, 16), (1, 2))),
        "out_grad": gaussian(streams_of[4], (TOKENS, HEADS * HD), 8.0, 48.0, ((0, 16), (1, 2))),
        "log_norm": jnp.clip(4.5 + 3.0 * jax.random.uniform(streams_of[5], (HEADS, TOKENS), jnp.float32) ** level_of(streams_of[5], (HEADS, TOKENS), ((0, 2), (1, 16)), -0.2, 0.2), 4.5, 7.5).astype(jnp.bfloat16),
        "rand_blocks": draw_rand_blocks(jax.random.fold_in(streams_of[7], 71), 0),
    }


def layout_tables():
    slot_count = 2 * PAIR
    block_total = slot_count * N_CTX
    seq_of_layout = np.zeros(block_total, np.int32)
    for position in range(block_total):
        device, within = divmod(position, slot_count)
        if within < PAIR:
            seq_of_layout[position] = PAIR * device + within
        else:
            seq_of_layout[position] = block_total - 1 - PAIR * device - (within - PAIR)
    layout_of_seq = np.argsort(seq_of_layout).astype(np.int32)
    return seq_of_layout, layout_of_seq


def pair_terms(query_heads, grad_heads, norm_rows, delta_rows, key_heads, value_heads, visible):
    scaling = HD ** -0.5
    scores = jnp.einsum('ihd,njhd->nhij', query_heads, key_heads) * scaling
    attn_prob = jnp.exp(scores - norm_rows[None, :, :, None]) * visible[:, None]
    prob_low = lax.optimization_barrier(attn_prob.astype(jnp.bfloat16)).astype(jnp.float32)
    value_term = jnp.einsum('nhij,ihd->njhd', prob_low, grad_heads)
    grad_prob = jnp.einsum('ihd,njhd->nhij', grad_heads, value_heads)
    grad_score = attn_prob * (grad_prob - delta_rows[None, :, :, None])
    score_low = lax.optimization_barrier(grad_score.astype(jnp.bfloat16)).astype(jnp.float32)
    query_term = jnp.einsum('nhij,njhd->nihd', score_low, key_heads) * scaling
    key_term = jnp.einsum('nhij,ihd->njhd', score_low, query_heads) * scaling
    return query_term, key_term, value_term


def reference(queries, key_rows, values, outputs, out_grad, log_norm, rand_blocks):
    slot_count = 2 * PAIR
    block_total = slot_count * N_CTX
    group_count = HEADS // HEAD_DEV
    seq_of_layout, layout_of_seq = layout_tables()

    def in_sequence(array):
        array = array.reshape(block_total, BLOCK, group_count, HEAD_DEV, HD)[layout_of_seq]
        return jnp.transpose(array, (2, 0, 1, 3, 4))

    query_seq = in_sequence(queries)
    key_seq = in_sequence(key_rows)
    value_seq = in_sequence(values)
    output_seq = in_sequence(outputs)
    grad_seq = in_sequence(out_grad)
    norm_seq = log_norm.reshape(group_count, HEAD_DEV, block_total, BLOCK)[:, :, layout_of_seq]
    norm_seq = jnp.transpose(norm_seq, (0, 2, 1, 3)).astype(jnp.float32)
    delta_seq = jnp.sum(grad_seq.astype(jnp.float32) * output_seq.astype(jnp.float32), axis=-1)
    delta_seq = lax.optimization_barrier(delta_seq.astype(jnp.bfloat16)).astype(jnp.float32)
    delta_seq = jnp.transpose(delta_seq, (0, 1, 3, 2))

    rand_seq = rand_blocks[layout_of_seq]
    block_ids = jnp.arange(block_total, dtype=jnp.int32)
    fixed_ids = [block_ids, jnp.maximum(block_ids - 1, 0)]
    fixed_ok = [jnp.ones((block_total,), jnp.float32), (block_ids >= 1).astype(jnp.float32)]
    for glob_id in range(GLOBAL):
        fixed_ids.append(jnp.full((block_total,), glob_id, jnp.int32))
        fixed_ok.append((block_ids >= glob_id + WINDOW).astype(jnp.float32))
    fixed_count = 2 + GLOBAL
    key_ids = jnp.concatenate([jnp.stack(fixed_ids, axis=1), jnp.maximum(rand_seq, 0).astype(jnp.int32)], axis=1)
    key_ok = jnp.concatenate([jnp.stack(fixed_ok, axis=1), (rand_seq >= 0).astype(jnp.float32)], axis=1)
    causal = jnp.asarray(np.tril(np.ones((BLOCK, BLOCK))), jnp.float32)
    first_kind = np.zeros(fixed_count + RANDOM)
    first_kind[0] = 1.0
    kind_first = jnp.asarray(first_kind, jnp.float32)[:, None, None]

    def one_group(operands):
        query_g, key_g, value_g, grad_g, norm_g, delta_g = operands

        def step(carry, block_id):
            key_acc, value_acc = carry
            chosen = key_ids[block_id]
            visible = key_ok[block_id][:, None, None] * (kind_first * causal[None] + (1.0 - kind_first))
            query_term, key_term, value_term = pair_terms(
                query_g[block_id].astype(jnp.float32), grad_g[block_id].astype(jnp.float32),
                norm_g[block_id], delta_g[block_id],
                key_g[chosen].astype(jnp.float32), value_g[chosen].astype(jnp.float32), visible)
            rounded = lax.optimization_barrier(query_term[fixed_count:].astype(jnp.bfloat16)).astype(jnp.float32)
            query_total = jnp.sum(query_term[:fixed_count], axis=0) + jnp.sum(rounded, axis=0)
            key_acc = key_acc.at[chosen].add(key_term)
            value_acc = value_acc.at[chosen].add(value_term)
            return (key_acc, value_acc), query_total

        zeros_acc = jnp.zeros((block_total, BLOCK, HEAD_DEV, HD), jnp.float32)
        (key_acc, value_acc), query_acc = lax.scan(step, (zeros_acc, zeros_acc), block_ids)
        return query_acc, key_acc, value_acc

    query_acc, key_acc, value_acc = lax.map(one_group, (query_seq, key_seq, value_seq, grad_seq, norm_seq, delta_seq))

    def in_layout(array):
        array = jnp.transpose(array, (1, 2, 0, 3, 4))[seq_of_layout]
        return array.reshape(block_total * BLOCK, HEADS * HD).astype(jnp.bfloat16)

    return (in_layout(query_acc), in_layout(key_acc), in_layout(value_acc))
```

```python
import jax
import jax.numpy as jnp
from jax import lax
from jax.sharding import PartitionSpec as P

PAIR = 2
WINDOW = 2
GLOBAL = 1
RANDOM = 3


def padded(cells, sides, width):
    for axis, dim in sides:
        count = lax.axis_size(axis)
        ends = count - 1
        head = lax.slice_in_dim(cells, 0, width, axis=dim)
        tail = lax.slice_in_dim(cells, cells.shape[dim] - width, cells.shape[dim], axis=dim)
        cells = jnp.concatenate(
            [
                lax.ppermute(tail, axis, [(i, (i + 1) % count) for i in range(ends)]),
                cells,
                lax.ppermute(head, axis, [((i + 1) % count, i) for i in range(ends)]),
            ],
            axis=dim,
        )
    return cells


def spread_2(array, axis, root):
    count = lax.axis_size(axis)
    mine = lax.axis_index(axis) == root
    array = jnp.where(mine, array, jnp.zeros_like(array))
    step = 1
    while step < count:
        pairs = [(i, i + step) for i in range(step) if i + step < count]
        array = array + lax.ppermute(array, axis, pairs)
        step *= 2
    return array


def gather_to_root(array, axis):
    count = lax.axis_size(axis)
    step = 1
    while step * 2 < count:
        step *= 2
    while step >= 1:
        pairs = [(i + step, i) for i in range(step) if i + step < count]
        array = array + lax.ppermute(array, axis, pairs)
        step //= 2
    return array


def pair_grads(query_heads, grad_heads, norm_blk, delta_blk, key_heads, value_heads, visible):
    head_size = query_heads.shape[-1]
    scaling = head_size ** (-0.5)
    scores = (
        jnp.einsum("nhid,nhjd->nhij", query_heads, key_heads, preferred_element_type=jnp.float32)
        * scaling
    )
    attn_prob = jnp.exp(scores - norm_blk.astype(jnp.float32)[:, :, :, None]) * visible[:, None]
    prob_low = attn_prob.astype(jnp.bfloat16)
    value_term = jnp.einsum(
        "nhij,nhid->nhjd", prob_low, grad_heads, preferred_element_type=jnp.float32
    )
    grad_prob = jnp.einsum(
        "nhid,nhjd->nhij", grad_heads, value_heads, preferred_element_type=jnp.float32
    )
    score_low = (attn_prob * (grad_prob - delta_blk.astype(jnp.float32)[:, :, :, None])).astype(
        jnp.bfloat16
    )
    query_term = (
        jnp.einsum("nhij,nhjd->nhid", score_low, key_heads, preferred_element_type=jnp.float32)
        * scaling
    )
    key_term = (
        jnp.einsum("nhij,nhid->nhjd", score_low, query_heads, preferred_element_type=jnp.float32)
        * scaling
    )
    return (query_term, key_term, value_term)


def shards(queries, key_rows, values, outputs, out_grad, log_norm, rand_blocks):
    ctx_size = lax.axis_size("ctx")
    my_index = lax.axis_index("ctx")
    row_count, features = queries.shape
    head_count = log_norm.shape[0]
    head_size = features // head_count
    slot_count = 2 * PAIR
    height = row_count // slot_count
    block_total = slot_count * ctx_size
    block_shape = (slot_count, head_count, height, head_size)

    def heads_major(array):
        return jnp.transpose(array.reshape(slot_count, height, head_count, head_size), (0, 2, 1, 3))

    query_blk = heads_major(queries)
    key_blk = heads_major(key_rows)
    value_blk = heads_major(values)
    output_blk = heads_major(outputs)
    grad_blk = heads_major(out_grad)
    norm_blk = jnp.transpose(log_norm.reshape(head_count, slot_count, height), (1, 0, 2))
    delta_blk = jnp.sum(
        grad_blk.astype(jnp.float32) * output_blk.astype(jnp.float32), axis=-1
    ).astype(jnp.bfloat16)
    within = jnp.arange(slot_count, dtype=jnp.int32)
    seq_blk = jnp.where(
        within < PAIR, PAIR * my_index + within, block_total - 1 - PAIR * my_index - (within - PAIR)
    )
    last_dev = my_index == ctx_size - 1
    first_dev = my_index == 0
    causal = jnp.tril(jnp.ones((height, height), jnp.float32))
    self_query, self_key, self_value = pair_grads(
        query_blk,
        grad_blk,
        norm_blk,
        delta_blk,
        key_blk,
        value_blk,
        jnp.broadcast_to(causal, (slot_count, height, height)),
    )
    rim_keys = jnp.stack(
        [
            jnp.stack([key_blk[PAIR], key_blk[PAIR - 1]]),
            jnp.stack([value_blk[PAIR], value_blk[PAIR - 1]]),
        ]
    )
    widened = padded(rim_keys, (("ctx", 1),), 1)
    tail_key = jnp.where(last_dev, key_blk[PAIR - 1], widened[0, 3])
    tail_value = jnp.where(last_dev, value_blk[PAIR - 1], widened[1, 3])
    prev_keys = jnp.concatenate(
        [widened[0, 0][None], key_blk[0 : PAIR - 1], key_blk[PAIR + 1 : slot_count], tail_key[None]]
    )
    prev_values = jnp.concatenate(
        [
            widened[1, 0][None],
            value_blk[0 : PAIR - 1],
            value_blk[PAIR + 1 : slot_count],
            tail_value[None],
        ]
    )
    visible = jnp.where((within == 0) & first_dev, 0.0, 1.0).astype(jnp.float32)[:, None, None]
    window_query, term_key, term_value = pair_grads(
        query_blk, grad_blk, norm_blk, delta_blk, prev_keys, prev_values, visible
    )
    out_rim = jnp.stack(
        [
            jnp.stack([term_key[0], term_key[slot_count - 1]]),
            jnp.stack([term_value[0], term_value[slot_count - 1]]),
        ]
    )
    came_back = padded(out_rim.astype(jnp.bfloat16), (("ctx", 1),), 1).astype(out_rim.dtype)
    own_tail = jnp.where(last_dev, 1.0, 0.0).astype(jnp.float32)

    def spread(term, returned):
        return jnp.concatenate(
            [
                term[1:PAIR],
                (term[slot_count - 1] * own_tail + returned[3])[None],
                returned[0][None],
                term[PAIR : slot_count - 1],
            ]
        )

    window_key = spread(term_key, came_back[0])
    window_value = spread(term_value, came_back[1])
    global_kv = spread_2(jnp.stack([key_blk[0:GLOBAL], value_blk[0:GLOBAL]]), "ctx", 0)
    target = jnp.repeat(jnp.arange(GLOBAL, dtype=jnp.int32), slot_count)
    visible_glob = (jnp.tile(seq_blk, GLOBAL) >= target + WINDOW).astype(jnp.float32)[:, None, None]
    glob_query, glob_key, glob_value = pair_grads(
        jnp.tile(query_blk, (GLOBAL, 1, 1, 1)),
        jnp.tile(grad_blk, (GLOBAL, 1, 1, 1)),
        jnp.tile(norm_blk, (GLOBAL, 1, 1)),
        jnp.tile(delta_blk, (GLOBAL, 1, 1)),
        jnp.repeat(global_kv[0], slot_count, axis=0),
        jnp.repeat(global_kv[1], slot_count, axis=0),
        visible_glob,
    )
    glob_query = jnp.sum(glob_query.reshape((GLOBAL,) + block_shape), axis=0)
    part_key = jnp.sum(glob_key.reshape((GLOBAL,) + block_shape), axis=1)
    part_value = jnp.sum(glob_value.reshape((GLOBAL,) + block_shape), axis=1)
    total_key, total_value = gather_to_root(jnp.stack([part_key, part_value]), "ctx")
    owner_flag = jnp.where(first_dev, 1.0, 0.0).astype(jnp.float32)
    padding = jnp.zeros((slot_count - GLOBAL,) + block_shape[1:], jnp.float32)
    glob_key_add = jnp.concatenate([total_key * owner_flag, padding])
    glob_value_add = jnp.concatenate([total_value * owner_flag, padding])
    ref_valid = rand_blocks >= 0
    in_front = rand_blocks < block_total // 2
    mirror = block_total - 1 - rand_blocks
    owner_dev = jnp.where(in_front, rand_blocks // PAIR, mirror // PAIR)
    owner_dev = jnp.where(ref_valid, owner_dev, ctx_size).reshape(-1)
    key_slot = jnp.where(in_front, rand_blocks % PAIR, PAIR + mirror % PAIR) + 1
    key_slot = jnp.where(ref_valid, key_slot, 0).reshape(-1)
    targets = jnp.arange(ctx_size, dtype=jnp.int32)
    matches = owner_dev[None, :] == targets[:, None]
    slot_send = jnp.sum(jnp.where(matches, key_slot[None, :], 0), axis=1)
    key_flat = key_blk.reshape(slot_count, -1)
    value_flat = value_blk.reshape(slot_count, -1)
    slot_ids = jnp.arange(1, slot_count + 1, dtype=jnp.int32)
    select = jnp.any(matches.reshape(ctx_size, slot_count, RANDOM), axis=2).astype(jnp.bfloat16)

    def route_rows(block):
        return jnp.dot(
            select, block.reshape(slot_count, -1), preferred_element_type=jnp.float32
        ).astype(jnp.bfloat16)

    arrived = (
        lax.all_to_all(route_rows(query_blk), "ctx", split_axis=0, concat_axis=0, tiled=True),
        lax.all_to_all(route_rows(grad_blk), "ctx", split_axis=0, concat_axis=0, tiled=True),
        lax.all_to_all(route_rows(norm_blk), "ctx", split_axis=0, concat_axis=0, tiled=True),
        lax.all_to_all(route_rows(delta_blk), "ctx", split_axis=0, concat_axis=0, tiled=True),
        lax.all_to_all(slot_send, "ctx", split_axis=0, concat_axis=0, tiled=True),
    )
    group_size = 8
    rounds = ctx_size // group_size
    item_shape = (group_size,) + block_shape[1:]
    stat_shape = (group_size, head_count, height)

    def owner_step(carry, item):
        query_item, grad_item, norm_item, delta_item, slot_item = item
        choose = slot_item[:, None] == slot_ids[None, :]
        choose_low = choose.astype(jnp.bfloat16)
        key_item = (
            jnp.dot(choose_low, key_flat, preferred_element_type=jnp.float32)
            .astype(jnp.bfloat16)
            .reshape(item_shape)
        )
        value_item = (
            jnp.dot(choose_low, value_flat, preferred_element_type=jnp.float32)
            .astype(jnp.bfloat16)
            .reshape(item_shape)
        )
        visible_rand = (slot_item > 0).astype(jnp.float32)[:, None, None]
        term_query, term_key, term_value = pair_grads(
            query_item.reshape(item_shape),
            grad_item.reshape(item_shape),
            norm_item.reshape(stat_shape),
            delta_item.reshape(stat_shape),
            key_item,
            value_item,
            visible_rand,
        )
        choose_float = choose.astype(jnp.float32)
        key_acc = carry[0] + jnp.einsum(
            "gs,gx->sx",
            choose_float,
            term_key.reshape(group_size, -1),
            precision=lax.Precision.HIGHEST,
        )
        value_acc = carry[1] + jnp.einsum(
            "gs,gx->sx",
            choose_float,
            term_value.reshape(group_size, -1),
            precision=lax.Precision.HIGHEST,
        )
        return ((key_acc, value_acc), term_query.astype(jnp.bfloat16).reshape(group_size, -1))

    def regroup(array):
        return array.reshape((rounds, group_size) + array.shape[1:])

    zero_acc = jnp.zeros((slot_count, height * features), jnp.float32)
    (rand_key, rand_value), answers = lax.scan(
        owner_step,
        (zero_acc, zero_acc),
        (
            regroup(arrived[0]),
            regroup(arrived[1]),
            regroup(arrived[2]),
            regroup(arrived[3]),
            regroup(arrived[4]),
        ),
    )
    answers = answers.reshape(ctx_size, height * features)
    returned = lax.all_to_all(answers, "ctx", split_axis=0, concat_axis=0, tiled=True)
    rand_query = jnp.dot(select.T, returned, preferred_element_type=jnp.float32)
    query_total = self_query + window_query + glob_query + rand_query.reshape(block_shape)
    key_total = self_key + window_key + glob_key_add + rand_key.reshape(block_shape)
    value_total = self_value + window_value + glob_value_add + rand_value.reshape(block_shape)

    def rows_major(array):
        return jnp.transpose(array.astype(jnp.bfloat16), (0, 2, 1, 3)).reshape(row_count, features)

    return (rows_major(query_total), rows_major(key_total), rows_major(value_total))


def solution(mesh):
    return jax.shard_map(
        shards,
        mesh=mesh,
        in_specs=(
            P("ctx", "head"),
            P("ctx", "head"),
            P("ctx", "head"),
            P("ctx", "head"),
            P("ctx", "head"),
            P("head", "ctx"),
            P("ctx", None),
        ),
        out_specs=(P("ctx", "head"), P("ctx", "head"), P("ctx", "head")),
        check_vma=False,
    )
```

```python
import jax
import jax.numpy as jnp
from jax import lax
from jax.experimental import pallas as pl
from jax.experimental.pallas import tpu as pltpu
from jax.sharding import PartitionSpec as P

PAIR = 2
WINDOW = 2
GLOBAL = 1
RANDOM = 3
KINDS = 3
STAT_ROWS = 16


def spread_2(array, axis, root):
    count = lax.axis_size(axis)
    mine = lax.axis_index(axis) == root
    array = jnp.where(mine, array, jnp.zeros_like(array))
    step = 1
    while step < count:
        pairs = [(i, i + step) for i in range(step) if i + step < count]
        array = array + lax.ppermute(array, axis, pairs)
        step *= 2
    return array


def gather_to_root(array, axis):
    count = lax.axis_size(axis)
    step = 1
    while step * 2 < count:
        step *= 2
    while step >= 1:
        pairs = [(i + step, i) for i in range(step) if i + step < count]
        array = array + lax.ppermute(array, axis, pairs)
        step //= 2
    return array


def shift(array, axis, offset):
    count = lax.axis_size(axis)
    pairs = [(i, i + offset) for i in range(count) if 0 <= i + offset < count]
    return lax.ppermute(array, axis, pairs)


def pair_math(q, do, k, v, nrm, dlt, mode):
    scale = q.shape[-1] ** (-0.5)
    nt = (((1,), (1,)), ((), ()))
    s_t = lax.dot_general(k, q, nt, preferred_element_type=jnp.float32) * scale
    rows = lax.broadcasted_iota(jnp.int32, s_t.shape, 0)
    cols = lax.broadcasted_iota(jnp.int32, s_t.shape, 1)
    full = (mode == 1).astype(jnp.float32)
    causal = (mode == 2).astype(jnp.float32)
    visible = full + causal * (rows <= cols).astype(jnp.float32)
    p_t = jnp.exp(s_t - nrm) * visible
    dv = jnp.dot(p_t.astype(jnp.bfloat16), do, preferred_element_type=jnp.float32)
    dp_t = lax.dot_general(v, do, nt, preferred_element_type=jnp.float32)
    ds_t = (p_t * (dp_t - dlt)).astype(jnp.bfloat16)
    dk = jnp.dot(ds_t, q, preferred_element_type=jnp.float32) * scale
    ds = jnp.transpose(ds_t.astype(jnp.float32)).astype(jnp.bfloat16)
    dq = jnp.dot(ds, k, preferred_element_type=jnp.float32) * scale
    return dq, dk, dv


def local_kernel(ktab, mtab, q_ref, do_ref, nrm_ref, dlt_ref, k_ref, v_ref, dq_ref, dk_ref, dv_ref):
    b = pl.program_id(0)
    kind = pl.program_id(2)
    mode = mtab[b * KINDS + kind]
    dq, dk, dv = pair_math(
        q_ref[...], do_ref[...], k_ref[...], v_ref[...], nrm_ref[0], dlt_ref[0], mode
    )

    @pl.when(kind == 0)
    def _():
        dq_ref[...] = dq

    @pl.when(kind > 0)
    def _():
        dq_ref[...] += dq

    dk_ref[...] = dk
    dv_ref[...] = dv


def rand_kernel(ktab, mtab, q_ref, do_ref, st_ref, k_ref, v_ref, dq_ref, dk_ref, dv_ref):
    p = pl.program_id(0)
    mode = mtab[p]
    stats = st_ref[0].astype(jnp.float32)
    dq, dk, dv = pair_math(
        q_ref[0], do_ref[0], k_ref[...], v_ref[...], stats[0:1, :], stats[1:2, :], mode
    )
    dq_ref[...] = dq.astype(jnp.bfloat16)
    dk_ref[...] = dk
    dv_ref[...] = dv


def local_pairs(ktab, mtab, queries, out_grad, norm3, delta3, key_cat, value_cat):
    slot_count = 2 * PAIR
    height = queries.shape[0] // slot_count
    heads = norm3.shape[0]
    width = queries.shape[1] // heads
    blk = (height, width)
    grid_spec = pltpu.PrefetchScalarGridSpec(
        num_scalar_prefetch=2,
        grid=(slot_count, heads, KINDS),
        in_specs=[
            pl.BlockSpec(blk, lambda b, h, c, kt, mt: (b, h)),
            pl.BlockSpec(blk, lambda b, h, c, kt, mt: (b, h)),
            pl.BlockSpec((1, 1, height), lambda b, h, c, kt, mt: (h, 0, b)),
            pl.BlockSpec((1, 1, height), lambda b, h, c, kt, mt: (h, 0, b)),
            pl.BlockSpec(blk, lambda b, h, c, kt, mt: (kt[b * KINDS + c], h)),
            pl.BlockSpec(blk, lambda b, h, c, kt, mt: (kt[b * KINDS + c], h)),
        ],
        out_specs=[
            pl.BlockSpec(blk, lambda b, h, c, kt, mt: (b, h)),
            pl.BlockSpec(blk, lambda b, h, c, kt, mt: (b * KINDS + c, h)),
            pl.BlockSpec(blk, lambda b, h, c, kt, mt: (b * KINDS + c, h)),
        ],
    )
    rows = queries.shape[0]
    return pl.pallas_call(
        local_kernel,
        grid_spec=grid_spec,
        out_shape=[
            jax.ShapeDtypeStruct((rows, queries.shape[1]), jnp.float32),
            jax.ShapeDtypeStruct((rows * KINDS, queries.shape[1]), jnp.float32),
            jax.ShapeDtypeStruct((rows * KINDS, queries.shape[1]), jnp.float32),
        ],
    )(ktab, mtab, queries, out_grad, norm3, delta3, key_cat, value_cat)


def rand_pairs(ktab, mtab, arrived, key_rows, value_rows, heads):
    items, packed_rows, features = arrived.shape
    width = features // heads
    height = (packed_rows - STAT_ROWS) // 2
    blk = (height, width)
    grid_spec = pltpu.PrefetchScalarGridSpec(
        num_scalar_prefetch=2,
        grid=(items, heads),
        in_specs=[
            pl.BlockSpec((1, height, width), lambda p, h, kt, mt: (p, 0, h)),
            pl.BlockSpec((1, height, width), lambda p, h, kt, mt: (p, 1, h)),
            pl.BlockSpec(
                (1, STAT_ROWS, width), lambda p, h, kt, mt: (p, 2 * height // STAT_ROWS, h)
            ),
            pl.BlockSpec(blk, lambda p, h, kt, mt: (kt[p], h)),
            pl.BlockSpec(blk, lambda p, h, kt, mt: (kt[p], h)),
        ],
        out_specs=[
            pl.BlockSpec(blk, lambda p, h, kt, mt: (p, h)),
            pl.BlockSpec(blk, lambda p, h, kt, mt: (p, h)),
            pl.BlockSpec(blk, lambda p, h, kt, mt: (p, h)),
        ],
    )
    return pl.pallas_call(
        rand_kernel,
        grid_spec=grid_spec,
        out_shape=[
            jax.ShapeDtypeStruct((items * height, features), jnp.bfloat16),
            jax.ShapeDtypeStruct((items * height, features), jnp.float32),
            jax.ShapeDtypeStruct((items * height, features), jnp.float32),
        ],
    )(ktab, mtab, arrived, arrived, arrived, key_rows, value_rows)


def shards(queries, key_rows, values, outputs, out_grad, log_norm, rand_blocks):
    ctx_size = lax.axis_size("ctx")
    my_index = lax.axis_index("ctx")
    row_count, features = queries.shape
    heads = log_norm.shape[0]
    slot_count = 2 * PAIR
    height = row_count // slot_count
    block_total = slot_count * ctx_size
    first_dev = my_index == 0
    last_dev = my_index == ctx_size - 1

    delta = jnp.sum(
        (out_grad.astype(jnp.float32) * outputs.astype(jnp.float32)).reshape(
            row_count, heads, features // heads
        ),
        axis=-1,
    )
    delta = jnp.transpose(delta).astype(jnp.bfloat16)
    norm3 = log_norm.astype(jnp.float32).reshape(heads, 1, row_count)
    delta3 = delta.astype(jnp.float32).reshape(heads, 1, row_count)

    def block(array, slot):
        return array[slot * height : (slot + 1) * height]

    from_left = shift(jnp.stack([block(key_rows, 1), block(values, 1)]), "ctx", 1)
    from_right = shift(jnp.stack([block(key_rows, 2), block(values, 2)]), "ctx", -1)
    global_kv = spread_2(jnp.stack([block(key_rows, 0), block(values, 0)]), "ctx", 0)
    key_cat = jnp.concatenate([key_rows, from_left[0], from_right[0], global_kv[0]])
    value_cat = jnp.concatenate([values, from_left[1], from_right[1], global_kv[1]])

    within = jnp.arange(slot_count, dtype=jnp.int32)
    seq_blk = jnp.where(
        within < PAIR, PAIR * my_index + within, block_total - 1 - PAIR * my_index - (within - PAIR)
    )
    last_prev = jnp.where(last_dev, 1, slot_count + 1).astype(jnp.int32)
    glob_slot = slot_count + 2
    ktab = jnp.stack(
        [
            jnp.int32(0), jnp.int32(slot_count), jnp.int32(glob_slot),
            jnp.int32(1), jnp.int32(0), jnp.int32(glob_slot),
            jnp.int32(2), jnp.int32(3), jnp.int32(glob_slot),
            jnp.int32(3), last_prev, jnp.int32(glob_slot),
        ]
    )
    glob_mode = (seq_blk >= WINDOW).astype(jnp.int32)
    first_prev = jnp.where(first_dev, 0, 1).astype(jnp.int32)
    mtab = jnp.stack(
        [
            jnp.int32(2), first_prev, glob_mode[0],
            jnp.int32(2), jnp.int32(1), glob_mode[1],
            jnp.int32(2), jnp.int32(1), glob_mode[2],
            jnp.int32(2), jnp.int32(1), glob_mode[3],
        ]
    )
    dq_local, dk_terms, dv_terms = local_pairs(
        ktab, mtab, queries, out_grad, norm3, delta3, key_cat, value_cat
    )
    dk_terms = dk_terms.reshape(slot_count, KINDS, height, features)
    dv_terms = dv_terms.reshape(slot_count, KINDS, height, features)

    ref_valid = rand_blocks >= 0
    in_front = rand_blocks < block_total // 2
    mirror = block_total - 1 - rand_blocks
    owner_dev = jnp.where(in_front, rand_blocks // PAIR, mirror // PAIR)
    owner_dev = jnp.where(ref_valid, owner_dev, ctx_size).reshape(-1)
    key_slot = jnp.where(in_front, rand_blocks % PAIR, PAIR + mirror % PAIR) + 1
    key_slot = jnp.where(ref_valid, key_slot, 0).reshape(-1)
    targets = jnp.arange(ctx_size, dtype=jnp.int32)
    matches = owner_dev[None, :] == targets[:, None]
    slot_send = jnp.sum(jnp.where(matches, key_slot[None, :], 0), axis=1)
    select = jnp.any(matches.reshape(ctx_size, slot_count, RANDOM), axis=2).astype(jnp.bfloat16)

    def per_slot_row(stat):
        return jnp.transpose(stat.reshape(heads, slot_count, height), (1, 0, 2)).reshape(
            slot_count, 1, features
        )

    packed = jnp.concatenate(
        [
            queries.reshape(slot_count, height, features),
            out_grad.reshape(slot_count, height, features),
            per_slot_row(log_norm),
            per_slot_row(delta),
        ],
        axis=1,
    )
    routed = jnp.dot(
        select, packed.reshape(slot_count, -1), preferred_element_type=jnp.float32
    ).astype(jnp.bfloat16)
    routed = routed.reshape(ctx_size, 2 * height + 2, features)
    slot_rows = jnp.broadcast_to(
        slot_send.astype(jnp.bfloat16)[:, None, None], (ctx_size, STAT_ROWS - 2, features)
    )
    routed = jnp.concatenate([routed, slot_rows], axis=1)
    arrived = lax.all_to_all(routed, "ctx", split_axis=0, concat_axis=0, tiled=True)
    slot_recv = arrived[:, 2 * height + 2, 0].astype(jnp.float32).astype(jnp.int32)
    ktab_r = jnp.maximum(slot_recv - 1, 0)
    mtab_r = (slot_recv > 0).astype(jnp.int32)
    dq_rand, dk_rand, dv_rand = rand_pairs(ktab_r, mtab_r, arrived, key_rows, values, heads)
    returned = lax.all_to_all(
        dq_rand.reshape(ctx_size, height * features), "ctx", split_axis=0, concat_axis=0, tiled=True
    )
    rand_query = jnp.dot(select.T, returned, preferred_element_type=jnp.float32)
    choose = (slot_recv[:, None] == jnp.arange(1, slot_count + 1)[None, :]).astype(jnp.float32)
    rand_key = jnp.einsum(
        "ps,px->sx", choose, dk_rand.reshape(ctx_size, -1), precision=lax.Precision.HIGHEST
    )
    rand_value = jnp.einsum(
        "ps,px->sx", choose, dv_rand.reshape(ctx_size, -1), precision=lax.Precision.HIGHEST
    )

    to_left = jnp.stack([dk_terms[0, 1], dv_terms[0, 1]]).astype(jnp.bfloat16)
    to_right = jnp.stack([dk_terms[slot_count - 1, 1], dv_terms[slot_count - 1, 1]]).astype(
        jnp.bfloat16
    )
    back_right = shift(to_left, "ctx", -1).astype(jnp.float32)
    back_left = shift(to_right, "ctx", 1).astype(jnp.float32)
    own_tail = jnp.where(last_dev, 1.0, 0.0).astype(jnp.float32)

    part = jnp.stack([jnp.sum(dk_terms[:, 2], axis=0), jnp.sum(dv_terms[:, 2], axis=0)])
    total = gather_to_root(part, "ctx")
    owner_flag = jnp.where(first_dev, 1.0, 0.0).astype(jnp.float32)

    def assemble(terms, which, rand_part):
        slots = [
            terms[0, 0] + terms[1, 1] + total[which] * owner_flag,
            terms[1, 0] + terms[slot_count - 1, 1] * own_tail + back_right[which],
            terms[2, 0] + back_left[which],
            terms[3, 0] + terms[2, 1],
        ]
        whole = jnp.stack(slots).reshape(row_count, features)
        return (whole + rand_part.reshape(row_count, features)).astype(jnp.bfloat16)

    query_total = (dq_local + rand_query.reshape(row_count, features)).astype(jnp.bfloat16)
    return (
        query_total,
        assemble(dk_terms, 0, rand_key),
        assemble(dv_terms, 1, rand_value),
    )


def solution(mesh):
    return jax.shard_map(
        shards,
        mesh=mesh,
        in_specs=(
            P("ctx", "head"),
            P("ctx", "head"),
            P("ctx", "head"),
            P("ctx", "head"),
            P("ctx", "head"),
            P("head", "ctx"),
            P("ctx", None),
        ),
        out_specs=(P("ctx", "head"), P("ctx", "head"), P("ctx", "head")),
        check_vma=False,
    )
```

```python
import functools

import jax
import jax.numpy as jnp
from jax import lax
from jax.experimental import pallas as pl
from jax.experimental.pallas import tpu as pltpu
from jax.sharding import PartitionSpec as P

PAIR = 2
WINDOW = 2
GLOBAL = 1
RANDOM = 3
KINDS = 3
STAT_ROWS = 16


def spread_2(array, axis, root):
    count = lax.axis_size(axis)
    mine = lax.axis_index(axis) == root
    array = jnp.where(mine, array, jnp.zeros_like(array))
    step = 1
    while step < count:
        pairs = [(i, i + step) for i in range(step) if i + step < count]
        array = array + lax.ppermute(array, axis, pairs)
        step *= 2
    return array


def gather_to_root(array, axis):
    count = lax.axis_size(axis)
    step = 1
    while step * 2 < count:
        step *= 2
    while step >= 1:
        pairs = [(i + step, i) for i in range(step) if i + step < count]
        array = array + lax.ppermute(array, axis, pairs)
        step //= 2
    return array


def shift(array, axis, offset):
    count = lax.axis_size(axis)
    pairs = [(i, i + offset) for i in range(count) if 0 <= i + offset < count]
    return lax.ppermute(array, axis, pairs)


def pair_math(q, do, k, v, nrm, dlt, mode):
    scale = q.shape[-1] ** (-0.5)
    nt = (((1,), (1,)), ((), ()))
    s_t = lax.dot_general(k, q, nt, preferred_element_type=jnp.float32) * scale
    rows = lax.broadcasted_iota(jnp.int32, s_t.shape, 0)
    cols = lax.broadcasted_iota(jnp.int32, s_t.shape, 1)
    full = (mode == 1).astype(jnp.float32)
    causal = (mode == 2).astype(jnp.float32)
    visible = full + causal * (rows <= cols).astype(jnp.float32)
    p_t = jnp.exp(s_t - nrm) * visible
    dv = jnp.dot(p_t.astype(jnp.bfloat16), do, preferred_element_type=jnp.float32)
    dp_t = lax.dot_general(v, do, nt, preferred_element_type=jnp.float32)
    ds_t = (p_t * (dp_t - dlt)).astype(jnp.bfloat16)
    dk = jnp.dot(ds_t, q, preferred_element_type=jnp.float32) * scale
    ds = jnp.transpose(ds_t.astype(jnp.float32)).astype(jnp.bfloat16)
    dq = jnp.dot(ds, k, preferred_element_type=jnp.float32) * scale
    return dq, dk, dv


def local_kernel(ktab, mtab, q_ref, do_ref, nrm_ref, dlt_ref, k_ref, v_ref, dq_ref, dk_ref, dv_ref):
    b = pl.program_id(0)
    kind = pl.program_id(1)
    mode = mtab[b * KINDS + kind]
    heads = nrm_ref.shape[0]
    width = q_ref.shape[1] // heads
    for h in range(heads):
        cols = slice(h * width, (h + 1) * width)
        dq, dk, dv = pair_math(
            q_ref[:, cols], do_ref[:, cols], k_ref[:, cols], v_ref[:, cols],
            nrm_ref[h], dlt_ref[h], mode,
        )

        @pl.when(kind == 0)
        def _():
            dq_ref[:, cols] = dq

        @pl.when(kind > 0)
        def _():
            dq_ref[:, cols] += dq

        dk_ref[:, cols] = dk
        dv_ref[:, cols] = dv


def rand_kernel(heads, ktab, mtab, q_ref, do_ref, st_ref, k_ref, v_ref, dq_ref, dk_ref, dv_ref):
    p = pl.program_id(0)
    mode = mtab[p]
    width = q_ref.shape[2] // heads
    for h in range(heads):
        cols = slice(h * width, (h + 1) * width)
        stats = st_ref[0, :, cols].astype(jnp.float32)
        dq, dk, dv = pair_math(
            q_ref[0, :, cols], do_ref[0, :, cols], k_ref[:, cols], v_ref[:, cols],
            stats[0:1, :], stats[1:2, :], mode,
        )
        dq_ref[0, :, cols] = dq.astype(jnp.bfloat16)
        dk_ref[0, :, cols] = dk
        dv_ref[0, :, cols] = dv


def local_pairs(ktab, mtab, queries, out_grad, norm3, delta3, key_cat, value_cat):
    slot_count = 2 * PAIR
    rows, features = queries.shape
    height = rows // slot_count
    heads = norm3.shape[0]
    blk = (height, features)
    stat = (heads, 1, height)
    grid_spec = pltpu.PrefetchScalarGridSpec(
        num_scalar_prefetch=2,
        grid=(slot_count, KINDS),
        in_specs=[
            pl.BlockSpec(blk, lambda b, c, kt, mt: (b, 0)),
            pl.BlockSpec(blk, lambda b, c, kt, mt: (b, 0)),
            pl.BlockSpec(stat, lambda b, c, kt, mt: (0, 0, b)),
            pl.BlockSpec(stat, lambda b, c, kt, mt: (0, 0, b)),
            pl.BlockSpec(blk, lambda b, c, kt, mt: (kt[b * KINDS + c], 0)),
            pl.BlockSpec(blk, lambda b, c, kt, mt: (kt[b * KINDS + c], 0)),
        ],
        out_specs=[
            pl.BlockSpec(blk, lambda b, c, kt, mt: (b, 0)),
            pl.BlockSpec(blk, lambda b, c, kt, mt: (b * KINDS + c, 0)),
            pl.BlockSpec(blk, lambda b, c, kt, mt: (b * KINDS + c, 0)),
        ],
    )
    return pl.pallas_call(
        local_kernel,
        grid_spec=grid_spec,
        out_shape=[
            jax.ShapeDtypeStruct((rows, features), jnp.float32),
            jax.ShapeDtypeStruct((rows * KINDS, features), jnp.float32),
            jax.ShapeDtypeStruct((rows * KINDS, features), jnp.float32),
        ],
    )(ktab, mtab, queries, out_grad, norm3, delta3, key_cat, value_cat)


def rand_pairs(ktab, mtab, arrived, key_rows, value_rows, heads):
    items, packed_rows, features = arrived.shape
    height = (packed_rows - STAT_ROWS) // 2
    grid_spec = pltpu.PrefetchScalarGridSpec(
        num_scalar_prefetch=2,
        grid=(items,),
        in_specs=[
            pl.BlockSpec((1, height, features), lambda p, kt, mt: (p, 0, 0)),
            pl.BlockSpec((1, height, features), lambda p, kt, mt: (p, 1, 0)),
            pl.BlockSpec(
                (1, STAT_ROWS, features), lambda p, kt, mt: (p, 2 * height // STAT_ROWS, 0)
            ),
            pl.BlockSpec((height, features), lambda p, kt, mt: (kt[p], 0)),
            pl.BlockSpec((height, features), lambda p, kt, mt: (kt[p], 0)),
        ],
        out_specs=[
            pl.BlockSpec((1, height, features), lambda p, kt, mt: (p, 0, 0)),
            pl.BlockSpec((1, height, features), lambda p, kt, mt: (p, 0, 0)),
            pl.BlockSpec((1, height, features), lambda p, kt, mt: (p, 0, 0)),
        ],
    )
    return pl.pallas_call(
        functools.partial(rand_kernel, heads),
        grid_spec=grid_spec,
        out_shape=[
            jax.ShapeDtypeStruct((items, height, features), jnp.bfloat16),
            jax.ShapeDtypeStruct((items, height, features), jnp.float32),
            jax.ShapeDtypeStruct((items, height, features), jnp.float32),
        ],
    )(ktab, mtab, arrived, arrived, arrived, key_rows, value_rows)


def shards(queries, key_rows, values, outputs, out_grad, log_norm, rand_blocks):
    ctx_size = lax.axis_size("ctx")
    my_index = lax.axis_index("ctx")
    row_count, features = queries.shape
    heads = log_norm.shape[0]
    slot_count = 2 * PAIR
    height = row_count // slot_count
    block_total = slot_count * ctx_size
    first_dev = my_index == 0
    last_dev = my_index == ctx_size - 1

    delta = jnp.sum(
        (out_grad.astype(jnp.float32) * outputs.astype(jnp.float32)).reshape(
            row_count, heads, features // heads
        ),
        axis=-1,
    )
    delta = jnp.transpose(delta).astype(jnp.bfloat16)
    norm3 = log_norm.astype(jnp.float32).reshape(heads, 1, row_count)
    delta3 = delta.astype(jnp.float32).reshape(heads, 1, row_count)

    def block(array, slot):
        return array[slot * height : (slot + 1) * height]

    from_left = shift(jnp.stack([block(key_rows, 1), block(values, 1)]), "ctx", 1)
    from_right = shift(jnp.stack([block(key_rows, 2), block(values, 2)]), "ctx", -1)
    global_kv = spread_2(jnp.stack([block(key_rows, 0), block(values, 0)]), "ctx", 0)
    key_cat = jnp.concatenate([key_rows, from_left[0], from_right[0], global_kv[0]])
    value_cat = jnp.concatenate([values, from_left[1], from_right[1], global_kv[1]])

    within = jnp.arange(slot_count, dtype=jnp.int32)
    seq_blk = jnp.where(
        within < PAIR, PAIR * my_index + within, block_total - 1 - PAIR * my_index - (within - PAIR)
    )
    last_prev = jnp.where(last_dev, 1, slot_count + 1).astype(jnp.int32)
    glob_slot = slot_count + 2
    ktab = jnp.stack(
        [
            jnp.int32(0), jnp.int32(slot_count), jnp.int32(glob_slot),
            jnp.int32(1), jnp.int32(0), jnp.int32(glob_slot),
            jnp.int32(2), jnp.int32(3), jnp.int32(glob_slot),
            jnp.int32(3), last_prev, jnp.int32(glob_slot),
        ]
    )
    glob_mode = (seq_blk >= WINDOW).astype(jnp.int32)
    first_prev = jnp.where(first_dev, 0, 1).astype(jnp.int32)
    mtab = jnp.stack(
        [
            jnp.int32(2), first_prev, glob_mode[0],
            jnp.int32(2), jnp.int32(1), glob_mode[1],
            jnp.int32(2), jnp.int32(1), glob_mode[2],
            jnp.int32(2), jnp.int32(1), glob_mode[3],
        ]
    )
    dq_local, dk_terms, dv_terms = local_pairs(
        ktab, mtab, queries, out_grad, norm3, delta3, key_cat, value_cat
    )
    dk_terms = dk_terms.reshape(slot_count, KINDS, height, features)
    dv_terms = dv_terms.reshape(slot_count, KINDS, height, features)

    ref_valid = rand_blocks >= 0
    in_front = rand_blocks < block_total // 2
    mirror = block_total - 1 - rand_blocks
    owner_dev = jnp.where(in_front, rand_blocks // PAIR, mirror // PAIR)
    owner_dev = jnp.where(ref_valid, owner_dev, ctx_size).reshape(-1)
    key_slot = jnp.where(in_front, rand_blocks % PAIR, PAIR + mirror % PAIR) + 1
    key_slot = jnp.where(ref_valid, key_slot, 0).reshape(-1)
    targets = jnp.arange(ctx_size, dtype=jnp.int32)
    matches = owner_dev[None, :] == targets[:, None]
    slot_send = jnp.sum(jnp.where(matches, key_slot[None, :], 0), axis=1)
    select = jnp.any(matches.reshape(ctx_size, slot_count, RANDOM), axis=2).astype(jnp.bfloat16)

    def per_slot_row(stat):
        return jnp.transpose(stat.reshape(heads, slot_count, height), (1, 0, 2)).reshape(
            slot_count, 1, features
        )

    packed = jnp.concatenate(
        [
            queries.reshape(slot_count, height, features),
            out_grad.reshape(slot_count, height, features),
            per_slot_row(log_norm),
            per_slot_row(delta),
        ],
        axis=1,
    )
    routed = jnp.dot(
        select, packed.reshape(slot_count, -1), preferred_element_type=jnp.float32
    ).astype(jnp.bfloat16)
    routed = routed.reshape(ctx_size, 2 * height + 2, features)
    slot_rows = jnp.broadcast_to(
        slot_send.astype(jnp.bfloat16)[:, None, None], (ctx_size, STAT_ROWS - 2, features)
    )
    routed = jnp.concatenate([routed, slot_rows], axis=1)
    arrived = lax.all_to_all(routed, "ctx", split_axis=0, concat_axis=0, tiled=True)
    slot_recv = arrived[:, 2 * height + 2, 0].astype(jnp.float32).astype(jnp.int32)
    ktab_r = jnp.maximum(slot_recv - 1, 0)
    mtab_r = (slot_recv > 0).astype(jnp.int32)
    dq_rand, dk_rand, dv_rand = rand_pairs(ktab_r, mtab_r, arrived, key_rows, values, heads)
    returned = lax.all_to_all(dq_rand, "ctx", split_axis=0, concat_axis=0, tiled=True)
    select_f = select.astype(jnp.float32)
    rand_query = jnp.sum(
        select_f[:, :, None, None] * returned.astype(jnp.float32)[:, None], axis=0
    )
    choose = (slot_recv[:, None] == jnp.arange(1, slot_count + 1)[None, :]).astype(jnp.float32)
    rand_key = jnp.sum(choose[:, :, None, None] * dk_rand[:, None], axis=0)
    rand_value = jnp.sum(choose[:, :, None, None] * dv_rand[:, None], axis=0)

    to_left = jnp.stack([dk_terms[0, 1], dv_terms[0, 1]]).astype(jnp.bfloat16)
    to_right = jnp.stack([dk_terms[slot_count - 1, 1], dv_terms[slot_count - 1, 1]]).astype(
        jnp.bfloat16
    )
    back_right = shift(to_left, "ctx", -1).astype(jnp.float32)
    back_left = shift(to_right, "ctx", 1).astype(jnp.float32)
    own_tail = jnp.where(last_dev, 1.0, 0.0).astype(jnp.float32)

    part = jnp.stack([jnp.sum(dk_terms[:, 2], axis=0), jnp.sum(dv_terms[:, 2], axis=0)])
    total = gather_to_root(part, "ctx")
    owner_flag = jnp.where(first_dev, 1.0, 0.0).astype(jnp.float32)

    def assemble(terms, which, rand_part):
        slots = [
            terms[0, 0] + terms[1, 1] + total[which] * owner_flag,
            terms[1, 0] + terms[slot_count - 1, 1] * own_tail + back_right[which],
            terms[2, 0] + back_left[which],
            terms[3, 0] + terms[2, 1],
        ]
        whole = jnp.stack(slots) + rand_part
        return whole.reshape(row_count, features).astype(jnp.bfloat16)

    query_total = (dq_local + rand_query.reshape(row_count, features)).astype(jnp.bfloat16)
    return (
        query_total,
        assemble(dk_terms, 0, rand_key),
        assemble(dv_terms, 1, rand_value),
    )


def solution(mesh):
    return jax.shard_map(
        shards,
        mesh=mesh,
        in_specs=(
            P("ctx", "head"),
            P("ctx", "head"),
            P("ctx", "head"),
            P("ctx", "head"),
            P("ctx", "head"),
            P("head", "ctx"),
            P("ctx", None),
        ),
        out_specs=(P("ctx", "head"), P("ctx", "head"), P("ctx", "head")),
        check_vma=False,
    )
```

```python
import functools

import jax
import jax.numpy as jnp
from jax import lax
from jax.experimental import pallas as pl
from jax.experimental.pallas import tpu as pltpu
from jax.sharding import PartitionSpec as P

PAIR = 2
WINDOW = 2
GLOBAL = 1
RANDOM = 3
STAT_ROWS = 16


def spread_2(array, axis, root):
    count = lax.axis_size(axis)
    mine = lax.axis_index(axis) == root
    array = jnp.where(mine, array, jnp.zeros_like(array))
    step = 1
    while step < count:
        pairs = [(i, i + step) for i in range(step) if i + step < count]
        array = array + lax.ppermute(array, axis, pairs)
        step *= 2
    return array


def gather_to_root(array, axis):
    count = lax.axis_size(axis)
    step = 1
    while step * 2 < count:
        step *= 2
    while step >= 1:
        pairs = [(i + step, i) for i in range(step) if i + step < count]
        array = array + lax.ppermute(array, axis, pairs)
        step //= 2
    return array


def shift(array, axis, offset):
    count = lax.axis_size(axis)
    pairs = [(i, i + offset) for i in range(count) if 0 <= i + offset < count]
    return lax.ppermute(array, axis, pairs)


def pair_math(q, do, k, v, nrm, dlt, mode):
    scale = q.shape[-1] ** (-0.5)
    nt = (((1,), (1,)), ((), ()))
    s_t = lax.dot_general(k, q, nt, preferred_element_type=jnp.float32) * scale
    rows = lax.broadcasted_iota(jnp.int32, s_t.shape, 0)
    cols = lax.broadcasted_iota(jnp.int32, s_t.shape, 1)
    full = (mode == 1).astype(jnp.float32)
    causal = (mode == 2).astype(jnp.float32)
    visible = full + causal * (rows <= cols).astype(jnp.float32)
    p_t = jnp.exp(s_t - nrm) * visible
    dv = jnp.dot(p_t.astype(jnp.bfloat16), do, preferred_element_type=jnp.float32)
    dp_t = lax.dot_general(v, do, nt, preferred_element_type=jnp.float32)
    ds_t = (p_t * (dp_t - dlt)).astype(jnp.bfloat16)
    dk = jnp.dot(ds_t, q, preferred_element_type=jnp.float32) * scale
    ds = jnp.transpose(ds_t.astype(jnp.float32)).astype(jnp.bfloat16)
    dq = jnp.dot(ds, k, preferred_element_type=jnp.float32) * scale
    return dq, dk, dv


def local_kernel(kinds, ktab, mtab, q_ref, do_ref, nrm_ref, dlt_ref, k_ref, v_ref, dq_ref, dk_ref, dv_ref):
    b = pl.program_id(0)
    kind = pl.program_id(1)
    mode = mtab[b * kinds + kind]
    heads = nrm_ref.shape[0]
    width = q_ref.shape[1] // heads
    for h in range(heads):
        cols = slice(h * width, (h + 1) * width)
        dq, dk, dv = pair_math(
            q_ref[:, cols], do_ref[:, cols], k_ref[:, cols], v_ref[:, cols],
            nrm_ref[h], dlt_ref[h], mode,
        )

        @pl.when(kind == 0)
        def _():
            dq_ref[:, cols] = dq

        @pl.when(kind > 0)
        def _():
            dq_ref[:, cols] += dq

        dk_ref[:, cols] = dk
        dv_ref[:, cols] = dv


def rand_kernel(heads, ktab, mtab, q_ref, do_ref, st_ref, k_ref, v_ref, dq_ref, dk_ref, dv_ref):
    p = pl.program_id(0)
    mode = mtab[p]
    slot = ktab[p]
    width = q_ref.shape[2] // heads

    @pl.when(p == 0)
    def _():
        dk_ref[...] = jnp.zeros_like(dk_ref)
        dv_ref[...] = jnp.zeros_like(dv_ref)

    for h in range(heads):
        cols = slice(h * width, (h + 1) * width)
        stats = st_ref[0, :, cols].astype(jnp.float32)
        dq, dk, dv = pair_math(
            q_ref[0, :, cols], do_ref[0, :, cols], k_ref[:, cols], v_ref[:, cols],
            stats[0:1, :], stats[1:2, :], mode,
        )
        dq_ref[0, :, cols] = dq.astype(jnp.bfloat16)

        @pl.when(mode > 0)
        def _():
            dk_ref[slot, :, cols] += dk
            dv_ref[slot, :, cols] += dv


def local_pairs(kinds, ktab, mtab, queries, out_grad, norm3, delta3, key_cat, value_cat):
    slot_count = 2 * PAIR
    rows, features = queries.shape
    height = rows // slot_count
    heads = norm3.shape[0]
    blk = (height, features)
    stat = (heads, 1, height)
    grid_spec = pltpu.PrefetchScalarGridSpec(
        num_scalar_prefetch=2,
        grid=(slot_count, kinds),
        in_specs=[
            pl.BlockSpec(blk, lambda b, c, kt, mt: (b, 0)),
            pl.BlockSpec(blk, lambda b, c, kt, mt: (b, 0)),
            pl.BlockSpec(stat, lambda b, c, kt, mt: (0, 0, b)),
            pl.BlockSpec(stat, lambda b, c, kt, mt: (0, 0, b)),
            pl.BlockSpec(blk, lambda b, c, kt, mt: (kt[b * kinds + c], 0)),
            pl.BlockSpec(blk, lambda b, c, kt, mt: (kt[b * kinds + c], 0)),
        ],
        out_specs=[
            pl.BlockSpec(blk, lambda b, c, kt, mt: (b, 0)),
            pl.BlockSpec(blk, lambda b, c, kt, mt: (b * kinds + c, 0)),
            pl.BlockSpec(blk, lambda b, c, kt, mt: (b * kinds + c, 0)),
        ],
    )
    return pl.pallas_call(
        functools.partial(local_kernel, kinds),
        grid_spec=grid_spec,
        out_shape=[
            jax.ShapeDtypeStruct((rows, features), jnp.float32),
            jax.ShapeDtypeStruct((rows * kinds, features), jnp.float32),
            jax.ShapeDtypeStruct((rows * kinds, features), jnp.float32),
        ],
    )(ktab, mtab, queries, out_grad, norm3, delta3, key_cat, value_cat)


def rand_pairs(ktab, mtab, arrived, key_rows, value_rows, heads):
    items, packed_rows, features = arrived.shape
    height = (packed_rows - STAT_ROWS) // 2
    slots = key_rows.shape[0] // height
    grid_spec = pltpu.PrefetchScalarGridSpec(
        num_scalar_prefetch=2,
        grid=(items,),
        in_specs=[
            pl.BlockSpec((1, height, features), lambda p, kt, mt: (p, 0, 0)),
            pl.BlockSpec((1, height, features), lambda p, kt, mt: (p, 1, 0)),
            pl.BlockSpec(
                (1, STAT_ROWS, features), lambda p, kt, mt: (p, 2 * height // STAT_ROWS, 0)
            ),
            pl.BlockSpec((height, features), lambda p, kt, mt: (kt[p], 0)),
            pl.BlockSpec((height, features), lambda p, kt, mt: (kt[p], 0)),
        ],
        out_specs=[
            pl.BlockSpec((1, height, features), lambda p, kt, mt: (p, 0, 0)),
            pl.BlockSpec((slots, height, features), lambda p, kt, mt: (0, 0, 0)),
            pl.BlockSpec((slots, height, features), lambda p, kt, mt: (0, 0, 0)),
        ],
    )
    return pl.pallas_call(
        functools.partial(rand_kernel, heads),
        grid_spec=grid_spec,
        out_shape=[
            jax.ShapeDtypeStruct((items, height, features), jnp.bfloat16),
            jax.ShapeDtypeStruct((slots, height, features), jnp.float32),
            jax.ShapeDtypeStruct((slots, height, features), jnp.float32),
        ],
    )(ktab, mtab, arrived, arrived, arrived, key_rows, value_rows)


def shards(queries, key_rows, values, outputs, out_grad, log_norm, rand_blocks):
    ctx_size = lax.axis_size("ctx")
    my_index = lax.axis_index("ctx")
    row_count, features = queries.shape
    heads = log_norm.shape[0]
    slot_count = 2 * PAIR
    height = row_count // slot_count
    block_total = slot_count * ctx_size
    first_dev = my_index == 0
    last_dev = my_index == ctx_size - 1

    delta = jnp.sum(
        (out_grad.astype(jnp.float32) * outputs.astype(jnp.float32)).reshape(
            row_count, heads, features // heads
        ),
        axis=-1,
    )
    delta = jnp.transpose(delta).astype(jnp.bfloat16)
    norm3 = log_norm.astype(jnp.float32).reshape(heads, 1, row_count)
    delta3 = delta.astype(jnp.float32).reshape(heads, 1, row_count)

    def block(array, slot):
        return array[slot * height : (slot + 1) * height]

    from_left = shift(jnp.stack([block(key_rows, 1), block(values, 1)]), "ctx", 1)
    from_right = shift(jnp.stack([block(key_rows, 2), block(values, 2)]), "ctx", -1)
    global_kv = spread_2(jnp.stack([block(key_rows, 0), block(values, 0)]), "ctx", 0)
    key_win = jnp.concatenate([key_rows, from_left[0], from_right[0]])
    value_win = jnp.concatenate([values, from_left[1], from_right[1]])

    within = jnp.arange(slot_count, dtype=jnp.int32)
    seq_blk = jnp.where(
        within < PAIR, PAIR * my_index + within, block_total - 1 - PAIR * my_index - (within - PAIR)
    )
    last_prev = jnp.where(last_dev, 1, slot_count + 1).astype(jnp.int32)
    first_prev = jnp.where(first_dev, 0, 1).astype(jnp.int32)
    ktab = jnp.stack(
        [
            jnp.int32(0), jnp.int32(slot_count),
            jnp.int32(1), jnp.int32(0),
            jnp.int32(2), jnp.int32(3),
            jnp.int32(3), last_prev,
        ]
    )
    mtab = jnp.stack(
        [
            jnp.int32(2), first_prev,
            jnp.int32(2), jnp.int32(1),
            jnp.int32(2), jnp.int32(1),
            jnp.int32(2), jnp.int32(1),
        ]
    )
    dq_win, dk_terms, dv_terms = local_pairs(
        2, ktab, mtab, queries, out_grad, norm3, delta3, key_win, value_win
    )
    dk_terms = dk_terms.reshape(slot_count, 2, height, features)
    dv_terms = dv_terms.reshape(slot_count, 2, height, features)
    glob_mode = (seq_blk >= WINDOW).astype(jnp.int32)
    dq_glob, dk_glob, dv_glob = local_pairs(
        1, jnp.zeros((slot_count,), jnp.int32), glob_mode, queries, out_grad, norm3, delta3,
        global_kv[0], global_kv[1],
    )
    dq_local = dq_win + dq_glob

    to_left = jnp.stack([dk_terms[0, 1], dv_terms[0, 1]]).astype(jnp.bfloat16)
    to_right = jnp.stack([dk_terms[slot_count - 1, 1], dv_terms[slot_count - 1, 1]]).astype(
        jnp.bfloat16
    )
    back_right = shift(to_left, "ctx", -1)
    back_left = shift(to_right, "ctx", 1)

    part = jnp.stack(
        [
            jnp.sum(dk_glob.reshape(slot_count, height, features), axis=0),
            jnp.sum(dv_glob.reshape(slot_count, height, features), axis=0),
        ]
    )
    total = gather_to_root(part, "ctx")

    ref_valid = rand_blocks >= 0
    in_front = rand_blocks < block_total // 2
    mirror = block_total - 1 - rand_blocks
    owner_dev = jnp.where(in_front, rand_blocks // PAIR, mirror // PAIR)
    owner_dev = jnp.where(ref_valid, owner_dev, ctx_size).reshape(-1)
    key_slot = jnp.where(in_front, rand_blocks % PAIR, PAIR + mirror % PAIR) + 1
    key_slot = jnp.where(ref_valid, key_slot, 0).reshape(-1)
    targets = jnp.arange(ctx_size, dtype=jnp.int32)
    matches = owner_dev[None, :] == targets[:, None]
    slot_send = jnp.sum(jnp.where(matches, key_slot[None, :], 0), axis=1)
    select = jnp.any(matches.reshape(ctx_size, slot_count, RANDOM), axis=2).astype(jnp.bfloat16)

    def per_slot_row(stat):
        return jnp.transpose(stat.reshape(heads, slot_count, height), (1, 0, 2)).reshape(
            slot_count, 1, features
        )

    packed = jnp.concatenate(
        [
            queries.reshape(slot_count, height, features),
            out_grad.reshape(slot_count, height, features),
            per_slot_row(log_norm),
            per_slot_row(delta),
        ],
        axis=1,
    )
    routed = jnp.dot(
        select, packed.reshape(slot_count, -1), preferred_element_type=jnp.float32
    ).astype(jnp.bfloat16)
    routed = routed.reshape(ctx_size, 2 * height + 2, features)
    slot_rows = jnp.broadcast_to(
        slot_send.astype(jnp.bfloat16)[:, None, None], (ctx_size, STAT_ROWS - 2, features)
    )
    routed = jnp.concatenate([routed, slot_rows], axis=1)
    arrived = lax.all_to_all(routed, "ctx", split_axis=0, concat_axis=0, tiled=True)
    slot_recv = arrived[:, 2 * height + 2, 0].astype(jnp.float32).astype(jnp.int32)
    ktab_r = jnp.maximum(slot_recv - 1, 0)
    mtab_r = (slot_recv > 0).astype(jnp.int32)
    dq_rand, dk_rand, dv_rand = rand_pairs(ktab_r, mtab_r, arrived, key_rows, values, heads)
    dq_rand, total, back_left, back_right = lax.optimization_barrier(
        (dq_rand, total, back_left, back_right)
    )
    back_left = back_left.astype(jnp.float32)
    back_right = back_right.astype(jnp.float32)
    returned = lax.all_to_all(dq_rand, "ctx", split_axis=0, concat_axis=0, tiled=True)
    select_f = select.astype(jnp.float32)
    rand_query = jnp.sum(
        select_f[:, :, None, None] * returned.astype(jnp.float32)[:, None], axis=0
    )
    rand_key = dk_rand
    rand_value = dv_rand

    own_tail = jnp.where(last_dev, 1.0, 0.0).astype(jnp.float32)

    owner_flag = jnp.where(first_dev, 1.0, 0.0).astype(jnp.float32)

    def assemble(terms, which, rand_part):
        slots = [
            terms[0, 0] + terms[1, 1] + total[which] * owner_flag,
            terms[1, 0] + terms[slot_count - 1, 1] * own_tail + back_right[which],
            terms[2, 0] + back_left[which],
            terms[3, 0] + terms[2, 1],
        ]
        whole = jnp.stack(slots) + rand_part
        return whole.reshape(row_count, features).astype(jnp.bfloat16)

    query_total = (dq_local + rand_query.reshape(row_count, features)).astype(jnp.bfloat16)
    return (
        query_total,
        assemble(dk_terms, 0, rand_key),
        assemble(dv_terms, 1, rand_value),
    )


def solution(mesh):
    return jax.shard_map(
        shards,
        mesh=mesh,
        in_specs=(
            P("ctx", "head"),
            P("ctx", "head"),
            P("ctx", "head"),
            P("ctx", "head"),
            P("ctx", "head"),
            P("head", "ctx"),
            P("ctx", None),
        ),
        out_specs=(P("ctx", "head"), P("ctx", "head"), P("ctx", "head")),
        check_vma=False,
    )
```

```python
import functools

import jax
import jax.numpy as jnp
from jax import lax
from jax.experimental import pallas as pl
from jax.experimental.pallas import tpu as pltpu
from jax.sharding import PartitionSpec as P

PAIR = 2
WINDOW = 2
GLOBAL = 1
RANDOM = 3
STAT_ROWS = 16


def spread_2(array, axis, root):
    count = lax.axis_size(axis)
    mine = lax.axis_index(axis) == root
    array = jnp.where(mine, array, jnp.zeros_like(array))
    step = 1
    while step < count:
        pairs = [(i, i + step) for i in range(step) if i + step < count]
        array = array + lax.ppermute(array, axis, pairs)
        step *= 2
    return array


def gather_to_root(array, axis):
    count = lax.axis_size(axis)
    step = 1
    while step * 2 < count:
        step *= 2
    while step >= 1:
        pairs = [(i + step, i) for i in range(step) if i + step < count]
        array = array + lax.ppermute(array, axis, pairs)
        step //= 2
    return array


def shift(array, axis, offset):
    count = lax.axis_size(axis)
    pairs = [(i, i + offset) for i in range(count) if 0 <= i + offset < count]
    return lax.ppermute(array, axis, pairs)


def pair_math(q, do, k, v, nrm, dlt, mode):
    scale = q.shape[-1] ** (-0.5)
    nt = (((1,), (1,)), ((), ()))
    s_t = lax.dot_general(k, q, nt, preferred_element_type=jnp.float32) * scale
    rows = lax.broadcasted_iota(jnp.int32, s_t.shape, 0)
    cols = lax.broadcasted_iota(jnp.int32, s_t.shape, 1)
    full = (mode == 1).astype(jnp.float32)
    causal = (mode == 2).astype(jnp.float32)
    visible = full + causal * (rows <= cols).astype(jnp.float32)
    p_t = jnp.exp(s_t - nrm) * visible
    dv = jnp.dot(p_t.astype(jnp.bfloat16), do, preferred_element_type=jnp.float32)
    dp_t = lax.dot_general(v, do, nt, preferred_element_type=jnp.float32)
    ds_t = (p_t * (dp_t - dlt)).astype(jnp.bfloat16)
    dk = jnp.dot(ds_t, q, preferred_element_type=jnp.float32) * scale
    ds = jnp.transpose(ds_t.astype(jnp.float32)).astype(jnp.bfloat16)
    dq = jnp.dot(ds, k, preferred_element_type=jnp.float32) * scale
    return dq, dk, dv


def local_kernel(kinds, ktab, mtab, q_ref, do_ref, nrm_ref, dlt_ref, k_ref, v_ref, dq_ref, dk_ref, dv_ref):
    b = pl.program_id(0)
    kind = pl.program_id(1)
    mode = mtab[b * kinds + kind]
    heads = nrm_ref.shape[0]
    width = q_ref.shape[1] // heads
    for h in range(heads):
        cols = slice(h * width, (h + 1) * width)
        dq, dk, dv = pair_math(
            q_ref[:, cols], do_ref[:, cols], k_ref[:, cols], v_ref[:, cols],
            nrm_ref[h], dlt_ref[h], mode,
        )

        @pl.when(kind == 0)
        def _():
            dq_ref[:, cols] = dq

        @pl.when(kind > 0)
        def _():
            dq_ref[:, cols] += dq

        dk_ref[:, cols] = dk
        dv_ref[:, cols] = dv


def rand_kernel(heads, ktab, mtab, q_ref, do_ref, st_ref, k_ref, v_ref, dq_ref, dk_ref, dv_ref):
    p = pl.program_id(0)
    mode = mtab[p]
    width = q_ref.shape[2] // heads

    @pl.when(mode == 0)
    def _():
        dq_ref[...] = jnp.zeros_like(dq_ref)
        dk_ref[...] = jnp.zeros_like(dk_ref)
        dv_ref[...] = jnp.zeros_like(dv_ref)

    @pl.when(mode > 0)
    def _():
        for h in range(heads):
            cols = slice(h * width, (h + 1) * width)
            stats = st_ref[0, :, cols].astype(jnp.float32)
            dq, dk, dv = pair_math(
                q_ref[0, :, cols], do_ref[0, :, cols], k_ref[:, cols], v_ref[:, cols],
                stats[0:1, :], stats[1:2, :], mode,
            )
            dq_ref[0, :, cols] = dq.astype(jnp.bfloat16)
            dk_ref[0, :, cols] = dk
            dv_ref[0, :, cols] = dv


def local_pairs(kinds, ktab, mtab, queries, out_grad, norm3, delta3, key_cat, value_cat):
    slot_count = 2 * PAIR
    rows, features = queries.shape
    height = rows // slot_count
    heads = norm3.shape[0]
    blk = (height, features)
    stat = (heads, 1, height)
    grid_spec = pltpu.PrefetchScalarGridSpec(
        num_scalar_prefetch=2,
        grid=(slot_count, kinds),
        in_specs=[
            pl.BlockSpec(blk, lambda b, c, kt, mt: (b, 0)),
            pl.BlockSpec(blk, lambda b, c, kt, mt: (b, 0)),
            pl.BlockSpec(stat, lambda b, c, kt, mt: (0, 0, b)),
            pl.BlockSpec(stat, lambda b, c, kt, mt: (0, 0, b)),
            pl.BlockSpec(blk, lambda b, c, kt, mt: (kt[b * kinds + c], 0)),
            pl.BlockSpec(blk, lambda b, c, kt, mt: (kt[b * kinds + c], 0)),
        ],
        out_specs=[
            pl.BlockSpec(blk, lambda b, c, kt, mt: (b, 0)),
            pl.BlockSpec(blk, lambda b, c, kt, mt: (b * kinds + c, 0)),
            pl.BlockSpec(blk, lambda b, c, kt, mt: (b * kinds + c, 0)),
        ],
    )
    return pl.pallas_call(
        functools.partial(local_kernel, kinds),
        grid_spec=grid_spec,
        out_shape=[
            jax.ShapeDtypeStruct((rows, features), jnp.float32),
            jax.ShapeDtypeStruct((rows * kinds, features), jnp.float32),
            jax.ShapeDtypeStruct((rows * kinds, features), jnp.float32),
        ],
    )(ktab, mtab, queries, out_grad, norm3, delta3, key_cat, value_cat)


def rand_pairs(ktab, mtab, arrived, key_rows, value_rows, heads):
    items, packed_rows, features = arrived.shape
    height = (packed_rows - STAT_ROWS) // 2
    grid_spec = pltpu.PrefetchScalarGridSpec(
        num_scalar_prefetch=2,
        grid=(items,),
        in_specs=[
            pl.BlockSpec((1, height, features), lambda p, kt, mt: (p, 0, 0)),
            pl.BlockSpec((1, height, features), lambda p, kt, mt: (p, 1, 0)),
            pl.BlockSpec(
                (1, STAT_ROWS, features), lambda p, kt, mt: (p, 2 * height // STAT_ROWS, 0)
            ),
            pl.BlockSpec((height, features), lambda p, kt, mt: (kt[p], 0)),
            pl.BlockSpec((height, features), lambda p, kt, mt: (kt[p], 0)),
        ],
        out_specs=[
            pl.BlockSpec((1, height, features), lambda p, kt, mt: (p, 0, 0)),
            pl.BlockSpec((1, height, features), lambda p, kt, mt: (p, 0, 0)),
            pl.BlockSpec((1, height, features), lambda p, kt, mt: (p, 0, 0)),
        ],
    )
    return pl.pallas_call(
        functools.partial(rand_kernel, heads),
        grid_spec=grid_spec,
        out_shape=[
            jax.ShapeDtypeStruct((items, height, features), jnp.bfloat16),
            jax.ShapeDtypeStruct((items, height, features), jnp.float32),
            jax.ShapeDtypeStruct((items, height, features), jnp.float32),
        ],
    )(ktab, mtab, arrived, arrived, arrived, key_rows, value_rows)


def shards(queries, key_rows, values, outputs, out_grad, log_norm, rand_blocks):
    ctx_size = lax.axis_size("ctx")
    my_index = lax.axis_index("ctx")
    row_count, features = queries.shape
    heads = log_norm.shape[0]
    slot_count = 2 * PAIR
    height = row_count // slot_count
    block_total = slot_count * ctx_size
    first_dev = my_index == 0
    last_dev = my_index == ctx_size - 1

    delta = jnp.sum(
        (out_grad.astype(jnp.float32) * outputs.astype(jnp.float32)).reshape(
            row_count, heads, features // heads
        ),
        axis=-1,
    )
    delta = jnp.transpose(delta).astype(jnp.bfloat16)
    norm3 = log_norm.astype(jnp.float32).reshape(heads, 1, row_count)
    delta3 = delta.astype(jnp.float32).reshape(heads, 1, row_count)

    def block(array, slot):
        return array[slot * height : (slot + 1) * height]

    from_left = shift(jnp.stack([block(key_rows, 1), block(values, 1)]), "ctx", 1)
    from_right = shift(jnp.stack([block(key_rows, 2), block(values, 2)]), "ctx", -1)
    global_kv = spread_2(jnp.stack([block(key_rows, 0), block(values, 0)]), "ctx", 0)
    key_win = jnp.concatenate([key_rows, from_left[0], from_right[0]])
    value_win = jnp.concatenate([values, from_left[1], from_right[1]])

    within = jnp.arange(slot_count, dtype=jnp.int32)
    seq_blk = jnp.where(
        within < PAIR, PAIR * my_index + within, block_total - 1 - PAIR * my_index - (within - PAIR)
    )
    last_prev = jnp.where(last_dev, 1, slot_count + 1).astype(jnp.int32)
    first_prev = jnp.where(first_dev, 0, 1).astype(jnp.int32)
    ktab = jnp.stack(
        [
            jnp.int32(0), jnp.int32(slot_count),
            jnp.int32(1), jnp.int32(0),
            jnp.int32(2), jnp.int32(3),
            jnp.int32(3), last_prev,
        ]
    )
    mtab = jnp.stack(
        [
            jnp.int32(2), first_prev,
            jnp.int32(2), jnp.int32(1),
            jnp.int32(2), jnp.int32(1),
            jnp.int32(2), jnp.int32(1),
        ]
    )
    dq_win, dk_terms, dv_terms = local_pairs(
        2, ktab, mtab, queries, out_grad, norm3, delta3, key_win, value_win
    )
    dk_terms = dk_terms.reshape(slot_count, 2, height, features)
    dv_terms = dv_terms.reshape(slot_count, 2, height, features)
    glob_mode = (seq_blk >= WINDOW).astype(jnp.int32)
    global_kv, dq_win, dk_terms, dv_terms = lax.optimization_barrier(
        (global_kv, dq_win, dk_terms, dv_terms)
    )
    dq_glob, dk_glob, dv_glob = local_pairs(
        1, jnp.zeros((slot_count,), jnp.int32), glob_mode, queries, out_grad, norm3, delta3,
        global_kv[0], global_kv[1],
    )
    dq_local = dq_win + dq_glob

    to_left = jnp.stack([dk_terms[0, 1], dv_terms[0, 1]]).astype(jnp.bfloat16)
    to_right = jnp.stack([dk_terms[slot_count - 1, 1], dv_terms[slot_count - 1, 1]]).astype(
        jnp.bfloat16
    )
    back_right = shift(to_left, "ctx", -1)
    back_left = shift(to_right, "ctx", 1)

    part = jnp.stack(
        [
            jnp.sum(dk_glob.reshape(slot_count, height, features), axis=0),
            jnp.sum(dv_glob.reshape(slot_count, height, features), axis=0),
        ]
    )
    total = gather_to_root(part, "ctx")

    ref_valid = rand_blocks >= 0
    in_front = rand_blocks < block_total // 2
    mirror = block_total - 1 - rand_blocks
    owner_dev = jnp.where(in_front, rand_blocks // PAIR, mirror // PAIR)
    owner_dev = jnp.where(ref_valid, owner_dev, ctx_size).reshape(-1)
    key_slot = jnp.where(in_front, rand_blocks % PAIR, PAIR + mirror % PAIR) + 1
    key_slot = jnp.where(ref_valid, key_slot, 0).reshape(-1)
    targets = jnp.arange(ctx_size, dtype=jnp.int32)
    matches = owner_dev[None, :] == targets[:, None]
    slot_send = jnp.sum(jnp.where(matches, key_slot[None, :], 0), axis=1)
    select = jnp.any(matches.reshape(ctx_size, slot_count, RANDOM), axis=2).astype(jnp.bfloat16)

    def per_slot_row(stat):
        return jnp.transpose(stat.reshape(heads, slot_count, height), (1, 0, 2)).reshape(
            slot_count, 1, features
        )

    packed = jnp.concatenate(
        [
            queries.reshape(slot_count, height, features),
            out_grad.reshape(slot_count, height, features),
            per_slot_row(log_norm),
            per_slot_row(delta),
        ],
        axis=1,
    )
    routed = jnp.dot(
        select, packed.reshape(slot_count, -1), preferred_element_type=jnp.float32
    ).astype(jnp.bfloat16)
    routed = routed.reshape(ctx_size, 2 * height + 2, features)
    slot_rows = jnp.broadcast_to(
        slot_send.astype(jnp.bfloat16)[:, None, None], (ctx_size, STAT_ROWS - 2, features)
    )
    routed = jnp.concatenate([routed, slot_rows], axis=1)
    arrived = lax.all_to_all(routed, "ctx", split_axis=0, concat_axis=0, tiled=True)
    slot_recv = arrived[:, 2 * height + 2, 0].astype(jnp.float32).astype(jnp.int32)
    ktab_r = jnp.maximum(slot_recv - 1, 0)
    mtab_r = (slot_recv > 0).astype(jnp.int32)
    dq_rand, dk_rand, dv_rand = rand_pairs(ktab_r, mtab_r, arrived, key_rows, values, heads)
    dq_rand, back_left, back_right = lax.optimization_barrier((dq_rand, back_left, back_right))
    back_left = back_left.astype(jnp.float32)
    back_right = back_right.astype(jnp.float32)
    returned = lax.all_to_all(dq_rand, "ctx", split_axis=0, concat_axis=0, tiled=True)
    select_f = select.astype(jnp.float32)
    rand_query = jnp.sum(
        select_f[:, :, None, None] * returned.astype(jnp.float32)[:, None], axis=0
    )
    choose = (slot_recv[:, None] == jnp.arange(1, slot_count + 1)[None, :]).astype(jnp.float32)
    rand_key = jnp.sum(choose[:, :, None, None] * dk_rand[:, None], axis=0)
    rand_value = jnp.sum(choose[:, :, None, None] * dv_rand[:, None], axis=0)

    own_tail = jnp.where(last_dev, 1.0, 0.0).astype(jnp.float32)

    owner_flag = jnp.where(first_dev, 1.0, 0.0).astype(jnp.float32)

    def assemble(terms, which, rand_part):
        slots = [
            terms[0, 0] + terms[1, 1] + total[which] * owner_flag,
            terms[1, 0] + terms[slot_count - 1, 1] * own_tail + back_right[which],
            terms[2, 0] + back_left[which],
            terms[3, 0] + terms[2, 1],
        ]
        whole = jnp.stack(slots) + rand_part
        return whole.reshape(row_count, features).astype(jnp.bfloat16)

    query_total = (dq_local + rand_query.reshape(row_count, features)).astype(jnp.bfloat16)
    return (
        query_total,
        assemble(dk_terms, 0, rand_key),
        assemble(dv_terms, 1, rand_value),
    )


def solution(mesh):
    return jax.shard_map(
        shards,
        mesh=mesh,
        in_specs=(
            P("ctx", "head"),
            P("ctx", "head"),
            P("ctx", "head"),
            P("ctx", "head"),
            P("ctx", "head"),
            P("head", "ctx"),
            P("ctx", None),
        ),
        out_specs=(P("ctx", "head"), P("ctx", "head"), P("ctx", "head")),
        check_vma=False,
    )
```

```python
import functools

import jax
import jax.numpy as jnp
from jax import lax
from jax.experimental import pallas as pl
from jax.experimental.pallas import tpu as pltpu
from jax.sharding import PartitionSpec as P

PAIR = 2
WINDOW = 2
GLOBAL = 1
RANDOM = 3
STAT_ROWS = 16


def spread_2(array, axis, root):
    count = lax.axis_size(axis)
    mine = lax.axis_index(axis) == root
    array = jnp.where(mine, array, jnp.zeros_like(array))
    step = 1
    while step < count:
        pairs = [(i, i + step) for i in range(step) if i + step < count]
        array = array + lax.ppermute(array, axis, pairs)
        step *= 2
    return array


def gather_to_root(array, axis):
    count = lax.axis_size(axis)
    step = 1
    while step * 2 < count:
        step *= 2
    while step >= 1:
        pairs = [(i + step, i) for i in range(step) if i + step < count]
        array = array + lax.ppermute(array, axis, pairs)
        step //= 2
    return array


def shift(array, axis, offset):
    count = lax.axis_size(axis)
    pairs = [(i, i + offset) for i in range(count) if 0 <= i + offset < count]
    return lax.ppermute(array, axis, pairs)


def pair_math(q, do, k, v, nrm, dlt, mode):
    scale = q.shape[-1] ** (-0.5)
    nt = (((1,), (1,)), ((), ()))
    s_t = lax.dot_general(k, q, nt, preferred_element_type=jnp.float32) * scale
    rows = lax.broadcasted_iota(jnp.int32, s_t.shape, 0)
    cols = lax.broadcasted_iota(jnp.int32, s_t.shape, 1)
    full = (mode == 1).astype(jnp.float32)
    causal = (mode == 2).astype(jnp.float32)
    visible = full + causal * (rows <= cols).astype(jnp.float32)
    p_t = jnp.exp(s_t - nrm) * visible
    dv = jnp.dot(p_t.astype(jnp.bfloat16), do, preferred_element_type=jnp.float32)
    dp_t = lax.dot_general(v, do, nt, preferred_element_type=jnp.float32)
    ds_t = (p_t * (dp_t - dlt)).astype(jnp.bfloat16)
    dk = jnp.dot(ds_t, q, preferred_element_type=jnp.float32) * scale
    ds = jnp.transpose(ds_t.astype(jnp.float32)).astype(jnp.bfloat16)
    dq = jnp.dot(ds, k, preferred_element_type=jnp.float32) * scale
    return dq, dk, dv


def list_kernel(qin, qout, first, ktab, mtab, q_ref, do_ref, nrm_ref, dlt_ref, k_ref, v_ref, dq_ref, dk_ref, dv_ref):
    p = pl.program_id(0)
    mode = mtab[p]
    lead = first[p]
    heads = nrm_ref.shape[0]
    width = q_ref.shape[1] // heads
    for h in range(heads):
        cols = slice(h * width, (h + 1) * width)
        dq, dk, dv = pair_math(
            q_ref[:, cols], do_ref[:, cols], k_ref[:, cols], v_ref[:, cols],
            nrm_ref[h], dlt_ref[h], mode,
        )

        @pl.when(lead == 1)
        def _():
            dq_ref[:, cols] = dq

        @pl.when(lead == 0)
        def _():
            dq_ref[:, cols] += dq

        dk_ref[:, cols] = dk
        dv_ref[:, cols] = dv


def rand_kernel(heads, ktab, mtab, q_ref, do_ref, st_ref, k_ref, v_ref, dq_ref, dk_ref, dv_ref):
    p = pl.program_id(0)
    mode = mtab[p]
    width = q_ref.shape[2] // heads

    @pl.when(mode == 0)
    def _():
        dq_ref[...] = jnp.zeros_like(dq_ref)
        dk_ref[...] = jnp.zeros_like(dk_ref)
        dv_ref[...] = jnp.zeros_like(dv_ref)

    @pl.when(mode > 0)
    def _():
        for h in range(heads):
            cols = slice(h * width, (h + 1) * width)
            stats = st_ref[0, :, cols].astype(jnp.float32)
            dq, dk, dv = pair_math(
                q_ref[0, :, cols], do_ref[0, :, cols], k_ref[:, cols], v_ref[:, cols],
                stats[0:1, :], stats[1:2, :], mode,
            )
            dq_ref[0, :, cols] = dq.astype(jnp.bfloat16)
            dk_ref[0, :, cols] = dk
            dv_ref[0, :, cols] = dv


def list_pairs(qin, qout, first, ktab, mtab, outs, queries, out_grad, norm3, delta3, key_src, value_src):
    rows, features = queries.shape
    heads = norm3.shape[0]
    height = rows // (2 * PAIR)
    count = ktab.shape[0]
    blk = (height, features)
    stat = (heads, 1, height)
    grid_spec = pltpu.PrefetchScalarGridSpec(
        num_scalar_prefetch=5,
        grid=(count,),
        in_specs=[
            pl.BlockSpec(blk, lambda p, qi, qo, f, kt, mt: (qi[p], 0)),
            pl.BlockSpec(blk, lambda p, qi, qo, f, kt, mt: (qi[p], 0)),
            pl.BlockSpec(stat, lambda p, qi, qo, f, kt, mt: (0, 0, qi[p])),
            pl.BlockSpec(stat, lambda p, qi, qo, f, kt, mt: (0, 0, qi[p])),
            pl.BlockSpec(blk, lambda p, qi, qo, f, kt, mt: (kt[p], 0)),
            pl.BlockSpec(blk, lambda p, qi, qo, f, kt, mt: (kt[p], 0)),
        ],
        out_specs=[
            pl.BlockSpec(blk, lambda p, qi, qo, f, kt, mt: (qo[p], 0)),
            pl.BlockSpec(blk, lambda p, qi, qo, f, kt, mt: (p, 0)),
            pl.BlockSpec(blk, lambda p, qi, qo, f, kt, mt: (p, 0)),
        ],
    )
    return pl.pallas_call(
        list_kernel,
        grid_spec=grid_spec,
        out_shape=[
            jax.ShapeDtypeStruct((outs * height, features), jnp.float32),
            jax.ShapeDtypeStruct((count * height, features), jnp.float32),
            jax.ShapeDtypeStruct((count * height, features), jnp.float32),
        ],
    )(qin, qout, first, ktab, mtab, queries, out_grad, norm3, delta3, key_src, value_src)


def rand_pairs(ktab, mtab, arrived, key_rows, value_rows, heads):
    items, packed_rows, features = arrived.shape
    height = (packed_rows - STAT_ROWS) // 2
    grid_spec = pltpu.PrefetchScalarGridSpec(
        num_scalar_prefetch=2,
        grid=(items,),
        in_specs=[
            pl.BlockSpec((1, height, features), lambda p, kt, mt: (p, 0, 0)),
            pl.BlockSpec((1, height, features), lambda p, kt, mt: (p, 1, 0)),
            pl.BlockSpec(
                (1, STAT_ROWS, features), lambda p, kt, mt: (p, 2 * height // STAT_ROWS, 0)
            ),
            pl.BlockSpec((height, features), lambda p, kt, mt: (kt[p], 0)),
            pl.BlockSpec((height, features), lambda p, kt, mt: (kt[p], 0)),
        ],
        out_specs=[
            pl.BlockSpec((1, height, features), lambda p, kt, mt: (p, 0, 0)),
            pl.BlockSpec((1, height, features), lambda p, kt, mt: (p, 0, 0)),
            pl.BlockSpec((1, height, features), lambda p, kt, mt: (p, 0, 0)),
        ],
    )
    return pl.pallas_call(
        functools.partial(rand_kernel, heads),
        grid_spec=grid_spec,
        out_shape=[
            jax.ShapeDtypeStruct((items, height, features), jnp.bfloat16),
            jax.ShapeDtypeStruct((items, height, features), jnp.float32),
            jax.ShapeDtypeStruct((items, height, features), jnp.float32),
        ],
    )(ktab, mtab, arrived, arrived, arrived, key_rows, value_rows)


def shards(queries, key_rows, values, outputs, out_grad, log_norm, rand_blocks):
    ctx_size = lax.axis_size("ctx")
    my_index = lax.axis_index("ctx")
    row_count, features = queries.shape
    heads = log_norm.shape[0]
    slot_count = 2 * PAIR
    height = row_count // slot_count
    block_total = slot_count * ctx_size
    first_dev = my_index == 0
    last_dev = my_index == ctx_size - 1

    delta = jnp.sum(
        (out_grad.astype(jnp.float32) * outputs.astype(jnp.float32)).reshape(
            row_count, heads, features // heads
        ),
        axis=-1,
    )
    delta = jnp.transpose(delta).astype(jnp.bfloat16)
    norm3 = log_norm.astype(jnp.float32).reshape(heads, 1, row_count)
    delta3 = delta.astype(jnp.float32).reshape(heads, 1, row_count)

    def block(array, slot):
        return array[slot * height : (slot + 1) * height]

    from_left = shift(jnp.stack([block(key_rows, 1), block(values, 1)]), "ctx", 1)
    from_right = shift(jnp.stack([block(key_rows, 2), block(values, 2)]), "ctx", -1)
    global_kv = spread_2(jnp.stack([block(key_rows, 0), block(values, 0)]), "ctx", 0)
    key_win = jnp.concatenate([key_rows, from_left[0], from_right[0]])
    value_win = jnp.concatenate([values, from_left[1], from_right[1]])

    within = jnp.arange(slot_count, dtype=jnp.int32)
    seq_blk = jnp.where(
        within < PAIR, PAIR * my_index + within, block_total - 1 - PAIR * my_index - (within - PAIR)
    )
    last_prev = jnp.where(last_dev, 1, slot_count + 1).astype(jnp.int32)
    first_prev = jnp.where(first_dev, 0, 1).astype(jnp.int32)
    def table(*items):
        return jnp.stack([jnp.asarray(x, jnp.int32) for x in items])

    dq_own, dk_own, dv_own = list_pairs(
        table(0, 1, 1, 2, 2, 3), table(0, 1, 1, 2, 2, 3), table(1, 1, 0, 1, 0, 1),
        table(0, 1, 0, 2, 3, 3), table(2, 2, 1, 2, 1, 2), slot_count,
        queries, out_grad, norm3, delta3, key_rows, values,
    )
    dk_own = dk_own.reshape(6, height, features)
    dv_own = dv_own.reshape(6, height, features)
    dq_rim, dk_rim, dv_rim = list_pairs(
        table(0, slot_count - 1), table(0, 1), table(1, 1),
        table(slot_count, last_prev), table(first_prev, 1), 2,
        queries, out_grad, norm3, delta3, key_win, value_win,
    )
    dq_rim = dq_rim.reshape(2, height, features)
    dk_rim = dk_rim.reshape(2, height, features)
    dv_rim = dv_rim.reshape(2, height, features)
    glob_mode = (seq_blk >= WINDOW).astype(jnp.int32)
    dq_glob, dk_glob, dv_glob = list_pairs(
        table(0, 1, 2, 3), table(0, 1, 2, 3), table(1, 1, 1, 1), table(0, 0, 0, 0), glob_mode,
        slot_count, queries, out_grad, norm3, delta3, global_kv[0], global_kv[1],
    )
    zero_blk = jnp.zeros((height, features), jnp.float32)
    dq_local = (
        dq_own + dq_glob
        + jnp.concatenate([dq_rim[0:1], zero_blk[None], zero_blk[None], dq_rim[1:2]]).reshape(
            row_count, features
        )
    )

    to_left = jnp.stack([dk_rim[0], dv_rim[0]]).astype(jnp.bfloat16)
    to_right = jnp.stack([dk_rim[1], dv_rim[1]]).astype(jnp.bfloat16)
    back_right = shift(to_left, "ctx", -1)
    back_left = shift(to_right, "ctx", 1)

    part = jnp.stack(
        [
            jnp.sum(dk_glob.reshape(slot_count, height, features), axis=0),
            jnp.sum(dv_glob.reshape(slot_count, height, features), axis=0),
        ]
    )
    total = gather_to_root(part, "ctx")

    ref_valid = rand_blocks >= 0
    in_front = rand_blocks < block_total // 2
    mirror = block_total - 1 - rand_blocks
    owner_dev = jnp.where(in_front, rand_blocks // PAIR, mirror // PAIR)
    owner_dev = jnp.where(ref_valid, owner_dev, ctx_size).reshape(-1)
    key_slot = jnp.where(in_front, rand_blocks % PAIR, PAIR + mirror % PAIR) + 1
    key_slot = jnp.where(ref_valid, key_slot, 0).reshape(-1)
    targets = jnp.arange(ctx_size, dtype=jnp.int32)
    matches = owner_dev[None, :] == targets[:, None]
    slot_send = jnp.sum(jnp.where(matches, key_slot[None, :], 0), axis=1)
    select = jnp.any(matches.reshape(ctx_size, slot_count, RANDOM), axis=2).astype(jnp.bfloat16)

    def per_slot_row(stat):
        return jnp.transpose(stat.reshape(heads, slot_count, height), (1, 0, 2)).reshape(
            slot_count, 1, features
        )

    packed = jnp.concatenate(
        [
            queries.reshape(slot_count, height, features),
            out_grad.reshape(slot_count, height, features),
            per_slot_row(log_norm),
            per_slot_row(delta),
        ],
        axis=1,
    )
    routed = jnp.dot(
        select, packed.reshape(slot_count, -1), preferred_element_type=jnp.float32
    ).astype(jnp.bfloat16)
    routed = routed.reshape(ctx_size, 2 * height + 2, features)
    slot_rows = jnp.broadcast_to(
        slot_send.astype(jnp.bfloat16)[:, None, None], (ctx_size, STAT_ROWS - 2, features)
    )
    routed = jnp.concatenate([routed, slot_rows], axis=1)
    arrived = lax.all_to_all(routed, "ctx", split_axis=0, concat_axis=0, tiled=True)
    slot_recv = arrived[:, 2 * height + 2, 0].astype(jnp.float32).astype(jnp.int32)
    ktab_r = jnp.maximum(slot_recv - 1, 0)
    mtab_r = (slot_recv > 0).astype(jnp.int32)
    dq_rand, dk_rand, dv_rand = rand_pairs(ktab_r, mtab_r, arrived, key_rows, values, heads)
    dq_rand, total, back_left, back_right = lax.optimization_barrier(
        (dq_rand, total, back_left, back_right)
    )
    back_left = back_left.astype(jnp.float32)
    back_right = back_right.astype(jnp.float32)
    returned = lax.all_to_all(dq_rand, "ctx", split_axis=0, concat_axis=0, tiled=True)
    select_f = select.astype(jnp.float32)
    rand_query = jnp.sum(
        select_f[:, :, None, None] * returned.astype(jnp.float32)[:, None], axis=0
    )
    choose = (slot_recv[:, None] == jnp.arange(1, slot_count + 1)[None, :]).astype(jnp.float32)
    rand_key = jnp.sum(choose[:, :, None, None] * dk_rand[:, None], axis=0)
    rand_value = jnp.sum(choose[:, :, None, None] * dv_rand[:, None], axis=0)

    own_tail = jnp.where(last_dev, 1.0, 0.0).astype(jnp.float32)

    owner_flag = jnp.where(first_dev, 1.0, 0.0).astype(jnp.float32)

    def assemble(own, rim, which, rand_part):
        slots = [
            own[0] + own[2] + total[which] * owner_flag,
            own[1] + rim[1] * own_tail + back_right[which],
            own[3] + back_left[which],
            own[5] + own[4],
        ]
        whole = jnp.stack(slots) + rand_part
        return whole.reshape(row_count, features).astype(jnp.bfloat16)

    query_total = (dq_local + rand_query.reshape(row_count, features)).astype(jnp.bfloat16)
    return (
        query_total,
        assemble(dk_own, dk_rim, 0, rand_key),
        assemble(dv_own, dv_rim, 1, rand_value),
    )


def solution(mesh):
    return jax.shard_map(
        shards,
        mesh=mesh,
        in_specs=(
            P("ctx", "head"),
            P("ctx", "head"),
            P("ctx", "head"),
            P("ctx", "head"),
            P("ctx", "head"),
            P("head", "ctx"),
            P("ctx", None),
        ),
        out_specs=(P("ctx", "head"), P("ctx", "head"), P("ctx", "head")),
        check_vma=False,
    )
```

```python
import functools

import jax
import jax.numpy as jnp
from jax import lax
from jax.experimental import pallas as pl
from jax.experimental.pallas import tpu as pltpu
from jax.sharding import PartitionSpec as P

PAIR = 2
WINDOW = 2
GLOBAL = 1
RANDOM = 3
STAT_ROWS = 16


def spread_2(array, axis, root):
    count = lax.axis_size(axis)
    mine = lax.axis_index(axis) == root
    array = jnp.where(mine, array, jnp.zeros_like(array))
    step = 1
    while step < count:
        pairs = [(i, i + step) for i in range(step) if i + step < count]
        array = array + lax.ppermute(array, axis, pairs)
        step *= 2
    return array


def gather_to_root(array, axis):
    count = lax.axis_size(axis)
    step = 1
    while step * 2 < count:
        step *= 2
    while step >= 1:
        pairs = [(i + step, i) for i in range(step) if i + step < count]
        array = array + lax.ppermute(array, axis, pairs)
        step //= 2
    return array


def shift(array, axis, offset):
    count = lax.axis_size(axis)
    pairs = [(i, i + offset) for i in range(count) if 0 <= i + offset < count]
    return lax.ppermute(array, axis, pairs)


def pair_math(q, do, k, v, nrm, dlt, mode):
    scale = q.shape[-1] ** (-0.5)
    nt = (((1,), (1,)), ((), ()))
    s_t = lax.dot_general(k, q, nt, preferred_element_type=jnp.float32) * scale
    rows = lax.broadcasted_iota(jnp.int32, s_t.shape, 0)
    cols = lax.broadcasted_iota(jnp.int32, s_t.shape, 1)
    full = (mode == 1).astype(jnp.float32)
    causal = (mode == 2).astype(jnp.float32)
    visible = full + causal * (rows <= cols).astype(jnp.float32)
    p_t = jnp.exp(s_t - nrm) * visible
    dv = jnp.dot(p_t.astype(jnp.bfloat16), do, preferred_element_type=jnp.float32)
    dp_t = lax.dot_general(v, do, nt, preferred_element_type=jnp.float32)
    ds_t = (p_t * (dp_t - dlt)).astype(jnp.bfloat16)
    dk = jnp.dot(ds_t, q, preferred_element_type=jnp.float32) * scale
    ds = jnp.transpose(ds_t.astype(jnp.float32)).astype(jnp.bfloat16)
    dq = jnp.dot(ds, k, preferred_element_type=jnp.float32) * scale
    return dq, dk, dv


def list_kernel(qin, qout, first, ktab, mtab, q_ref, do_ref, nrm_ref, dlt_ref, k_ref, v_ref, dq_ref, dk_ref, dv_ref):
    p = pl.program_id(0)
    mode = mtab[p]
    lead = first[p]
    heads = nrm_ref.shape[0]
    width = q_ref.shape[1] // heads
    for h in range(heads):
        cols = slice(h * width, (h + 1) * width)
        dq, dk, dv = pair_math(
            q_ref[:, cols], do_ref[:, cols], k_ref[:, cols], v_ref[:, cols],
            nrm_ref[h], dlt_ref[h], mode,
        )

        @pl.when(lead == 1)
        def _():
            dq_ref[:, cols] = dq

        @pl.when(lead == 0)
        def _():
            dq_ref[:, cols] += dq

        dk_ref[:, cols] = dk
        dv_ref[:, cols] = dv


def rand_kernel(heads, ktab, mtab, q_ref, do_ref, st_ref, k_ref, v_ref, dq_ref, dk_ref, dv_ref):
    p = pl.program_id(0)
    mode = mtab[p]
    width = q_ref.shape[2] // heads

    @pl.when(mode == 0)
    def _():
        dq_ref[...] = jnp.zeros_like(dq_ref)
        dk_ref[...] = jnp.zeros_like(dk_ref)
        dv_ref[...] = jnp.zeros_like(dv_ref)

    @pl.when(mode > 0)
    def _():
        for h in range(heads):
            cols = slice(h * width, (h + 1) * width)
            stats = st_ref[0, :, cols].astype(jnp.float32)
            dq, dk, dv = pair_math(
                q_ref[0, :, cols], do_ref[0, :, cols], k_ref[:, cols], v_ref[:, cols],
                stats[0:1, :], stats[1:2, :], mode,
            )
            dq_ref[0, :, cols] = dq.astype(jnp.bfloat16)
            dk_ref[0, :, cols] = dk
            dv_ref[0, :, cols] = dv


def list_pairs(qin, qout, first, ktab, mtab, outs, queries, out_grad, norm3, delta3, key_src, value_src):
    rows, features = queries.shape
    heads = norm3.shape[0]
    height = rows // (2 * PAIR)
    count = ktab.shape[0]
    blk = (height, features)
    stat = (heads, 1, height)
    grid_spec = pltpu.PrefetchScalarGridSpec(
        num_scalar_prefetch=5,
        grid=(count,),
        in_specs=[
            pl.BlockSpec(blk, lambda p, qi, qo, f, kt, mt: (qi[p], 0)),
            pl.BlockSpec(blk, lambda p, qi, qo, f, kt, mt: (qi[p], 0)),
            pl.BlockSpec(stat, lambda p, qi, qo, f, kt, mt: (0, 0, qi[p])),
            pl.BlockSpec(stat, lambda p, qi, qo, f, kt, mt: (0, 0, qi[p])),
            pl.BlockSpec(blk, lambda p, qi, qo, f, kt, mt: (kt[p], 0)),
            pl.BlockSpec(blk, lambda p, qi, qo, f, kt, mt: (kt[p], 0)),
        ],
        out_specs=[
            pl.BlockSpec(blk, lambda p, qi, qo, f, kt, mt: (qo[p], 0)),
            pl.BlockSpec(blk, lambda p, qi, qo, f, kt, mt: (p, 0)),
            pl.BlockSpec(blk, lambda p, qi, qo, f, kt, mt: (p, 0)),
        ],
    )
    return pl.pallas_call(
        list_kernel,
        grid_spec=grid_spec,
        out_shape=[
            jax.ShapeDtypeStruct((outs * height, features), jnp.float32),
            jax.ShapeDtypeStruct((count * height, features), jnp.float32),
            jax.ShapeDtypeStruct((count * height, features), jnp.float32),
        ],
    )(qin, qout, first, ktab, mtab, queries, out_grad, norm3, delta3, key_src, value_src)


def rand_pairs(ktab, mtab, arrived, key_rows, value_rows, heads):
    items, packed_rows, features = arrived.shape
    height = (packed_rows - STAT_ROWS) // 2
    grid_spec = pltpu.PrefetchScalarGridSpec(
        num_scalar_prefetch=2,
        grid=(items,),
        in_specs=[
            pl.BlockSpec((1, height, features), lambda p, kt, mt: (p, 0, 0)),
            pl.BlockSpec((1, height, features), lambda p, kt, mt: (p, 1, 0)),
            pl.BlockSpec(
                (1, STAT_ROWS, features), lambda p, kt, mt: (p, 2 * height // STAT_ROWS, 0)
            ),
            pl.BlockSpec((height, features), lambda p, kt, mt: (kt[p], 0)),
            pl.BlockSpec((height, features), lambda p, kt, mt: (kt[p], 0)),
        ],
        out_specs=[
            pl.BlockSpec((1, height, features), lambda p, kt, mt: (p, 0, 0)),
            pl.BlockSpec((1, height, features), lambda p, kt, mt: (p, 0, 0)),
            pl.BlockSpec((1, height, features), lambda p, kt, mt: (p, 0, 0)),
        ],
    )
    return pl.pallas_call(
        functools.partial(rand_kernel, heads),
        grid_spec=grid_spec,
        out_shape=[
            jax.ShapeDtypeStruct((items, height, features), jnp.bfloat16),
            jax.ShapeDtypeStruct((items, height, features), jnp.float32),
            jax.ShapeDtypeStruct((items, height, features), jnp.float32),
        ],
    )(ktab, mtab, arrived, arrived, arrived, key_rows, value_rows)


def shards(queries, key_rows, values, outputs, out_grad, log_norm, rand_blocks):
    ctx_size = lax.axis_size("ctx")
    my_index = lax.axis_index("ctx")
    row_count, features = queries.shape
    heads = log_norm.shape[0]
    slot_count = 2 * PAIR
    height = row_count // slot_count
    block_total = slot_count * ctx_size
    first_dev = my_index == 0
    last_dev = my_index == ctx_size - 1

    delta = jnp.sum(
        (out_grad.astype(jnp.float32) * outputs.astype(jnp.float32)).reshape(
            row_count, heads, features // heads
        ),
        axis=-1,
    )
    delta = jnp.transpose(delta).astype(jnp.bfloat16)
    norm3 = log_norm.astype(jnp.float32).reshape(heads, 1, row_count)
    delta3 = delta.astype(jnp.float32).reshape(heads, 1, row_count)

    def block(array, slot):
        return array[slot * height : (slot + 1) * height]

    from_left = shift(jnp.stack([block(key_rows, 1), block(values, 1)]), "ctx", 1)
    from_right = shift(jnp.stack([block(key_rows, 2), block(values, 2)]), "ctx", -1)
    global_kv = spread_2(jnp.stack([block(key_rows, 0), block(values, 0)]), "ctx", 0)
    key_win = jnp.concatenate([key_rows, from_left[0], from_right[0]])
    value_win = jnp.concatenate([values, from_left[1], from_right[1]])

    within = jnp.arange(slot_count, dtype=jnp.int32)
    seq_blk = jnp.where(
        within < PAIR, PAIR * my_index + within, block_total - 1 - PAIR * my_index - (within - PAIR)
    )
    last_prev = jnp.where(last_dev, 1, slot_count + 1).astype(jnp.int32)
    first_prev = jnp.where(first_dev, 0, 1).astype(jnp.int32)
    def table(*items):
        return jnp.stack([jnp.asarray(x, jnp.int32) for x in items])

    dq_own, dk_own, dv_own = list_pairs(
        table(0, 1, 1, 2, 2, 3), table(0, 1, 1, 2, 2, 3), table(1, 1, 0, 1, 0, 1),
        table(0, 1, 0, 2, 3, 3), table(2, 2, 1, 2, 1, 2), slot_count,
        queries, out_grad, norm3, delta3, key_rows, values,
    )
    dk_own = dk_own.reshape(6, height, features)
    dv_own = dv_own.reshape(6, height, features)
    dq_rim, dk_rim, dv_rim = list_pairs(
        table(0, slot_count - 1), table(0, 1), table(1, 1),
        table(slot_count, last_prev), table(first_prev, 1), 2,
        queries, out_grad, norm3, delta3, key_win, value_win,
    )
    dq_rim = dq_rim.reshape(2, height, features)
    dk_rim = dk_rim.reshape(2, height, features)
    dv_rim = dv_rim.reshape(2, height, features)
    glob_mode = (seq_blk >= WINDOW).astype(jnp.int32)
    dq_glob, dk_glob, dv_glob = list_pairs(
        table(0, 1, 2, 3), table(0, 1, 2, 3), table(1, 1, 1, 1), table(0, 0, 0, 0), glob_mode,
        slot_count, queries, out_grad, norm3, delta3, global_kv[0], global_kv[1],
    )
    zero_blk = jnp.zeros((height, features), jnp.float32)
    dq_local = (
        dq_own + dq_glob
        + jnp.concatenate([dq_rim[0:1], zero_blk[None], zero_blk[None], dq_rim[1:2]]).reshape(
            row_count, features
        )
    )

    to_left = jnp.stack([dk_rim[0], dv_rim[0]]).astype(jnp.bfloat16)
    to_right = jnp.stack([dk_rim[1], dv_rim[1]]).astype(jnp.bfloat16)
    back_right = shift(to_left, "ctx", -1)
    back_left = shift(to_right, "ctx", 1)

    part = jnp.stack(
        [
            jnp.sum(dk_glob.reshape(slot_count, height, features), axis=0),
            jnp.sum(dv_glob.reshape(slot_count, height, features), axis=0),
        ]
    )
    total = gather_to_root(part, "ctx")

    ref_valid = rand_blocks >= 0
    in_front = rand_blocks < block_total // 2
    mirror = block_total - 1 - rand_blocks
    owner_dev = jnp.where(in_front, rand_blocks // PAIR, mirror // PAIR)
    owner_dev = jnp.where(ref_valid, owner_dev, ctx_size).reshape(-1)
    key_slot = jnp.where(in_front, rand_blocks % PAIR, PAIR + mirror % PAIR) + 1
    key_slot = jnp.where(ref_valid, key_slot, 0).reshape(-1)
    targets = jnp.arange(ctx_size, dtype=jnp.int32)
    matches = owner_dev[None, :] == targets[:, None]
    slot_send = jnp.sum(jnp.where(matches, key_slot[None, :], 0), axis=1)
    select = jnp.any(matches.reshape(ctx_size, slot_count, RANDOM), axis=2).astype(jnp.bfloat16)

    def per_slot_row(stat):
        return jnp.transpose(stat.reshape(heads, slot_count, height), (1, 0, 2)).reshape(
            slot_count, 1, features
        )

    packed = jnp.concatenate(
        [
            queries.reshape(slot_count, height, features),
            out_grad.reshape(slot_count, height, features),
            per_slot_row(log_norm),
            per_slot_row(delta),
        ],
        axis=1,
    )
    routed = jnp.dot(
        select, packed.reshape(slot_count, -1), preferred_element_type=jnp.float32
    ).astype(jnp.bfloat16)
    routed = routed.reshape(ctx_size, 2 * height + 2, features)
    slot_rows = jnp.broadcast_to(
        slot_send.astype(jnp.bfloat16)[:, None, None], (ctx_size, STAT_ROWS - 2, features)
    )
    routed = jnp.concatenate([routed, slot_rows], axis=1)
    routed, global_kv, from_left, from_right = lax.optimization_barrier(
        (routed, global_kv, from_left, from_right)
    )
    arrived = lax.all_to_all(routed, "ctx", split_axis=0, concat_axis=0, tiled=True)
    slot_recv = arrived[:, 2 * height + 2, 0].astype(jnp.float32).astype(jnp.int32)
    ktab_r = jnp.maximum(slot_recv - 1, 0)
    mtab_r = (slot_recv > 0).astype(jnp.int32)
    dq_rand, dk_rand, dv_rand = rand_pairs(ktab_r, mtab_r, arrived, key_rows, values, heads)
    dq_rand, total, back_left, back_right = lax.optimization_barrier(
        (dq_rand, total, back_left, back_right)
    )
    back_left = back_left.astype(jnp.float32)
    back_right = back_right.astype(jnp.float32)
    returned = lax.all_to_all(dq_rand, "ctx", split_axis=0, concat_axis=0, tiled=True)
    select_f = select.astype(jnp.float32)
    rand_query = jnp.sum(
        select_f[:, :, None, None] * returned.astype(jnp.float32)[:, None], axis=0
    )
    choose = (slot_recv[:, None] == jnp.arange(1, slot_count + 1)[None, :]).astype(jnp.float32)
    rand_key = jnp.sum(choose[:, :, None, None] * dk_rand[:, None], axis=0)
    rand_value = jnp.sum(choose[:, :, None, None] * dv_rand[:, None], axis=0)

    own_tail = jnp.where(last_dev, 1.0, 0.0).astype(jnp.float32)

    owner_flag = jnp.where(first_dev, 1.0, 0.0).astype(jnp.float32)

    def assemble(own, rim, which, rand_part):
        slots = [
            own[0] + own[2] + total[which] * owner_flag,
            own[1] + rim[1] * own_tail + back_right[which],
            own[3] + back_left[which],
            own[5] + own[4],
        ]
        whole = jnp.stack(slots) + rand_part
        return whole.reshape(row_count, features).astype(jnp.bfloat16)

    query_total = (dq_local + rand_query.reshape(row_count, features)).astype(jnp.bfloat16)
    return (
        query_total,
        assemble(dk_own, dk_rim, 0, rand_key),
        assemble(dv_own, dv_rim, 1, rand_value),
    )


def solution(mesh):
    return jax.shard_map(
        shards,
        mesh=mesh,
        in_specs=(
            P("ctx", "head"),
            P("ctx", "head"),
            P("ctx", "head"),
            P("ctx", "head"),
            P("ctx", "head"),
            P("head", "ctx"),
            P("ctx", None),
        ),
        out_specs=(P("ctx", "head"), P("ctx", "head"), P("ctx", "head")),
        check_vma=False,
    )
```

```python
import functools

import jax
import jax.numpy as jnp
from jax import lax
from jax.experimental import pallas as pl
from jax.experimental.pallas import tpu as pltpu
from jax.sharding import PartitionSpec as P

PAIR = 2
WINDOW = 2
GLOBAL = 1
RANDOM = 3
STAT_ROWS = 16


def spread_2(array, axis, root):
    count = lax.axis_size(axis)
    mine = lax.axis_index(axis) == root
    array = jnp.where(mine, array, jnp.zeros_like(array))
    step = 1
    while step < count:
        pairs = [(i, i + step) for i in range(step) if i + step < count]
        array = array + lax.ppermute(array, axis, pairs)
        step *= 2
    return array


def gather_to_root(array, axis):
    count = lax.axis_size(axis)
    step = 1
    while step * 2 < count:
        step *= 2
    while step >= 1:
        pairs = [(i + step, i) for i in range(step) if i + step < count]
        array = array + lax.ppermute(array, axis, pairs)
        step //= 2
    return array


def shift(array, axis, offset):
    count = lax.axis_size(axis)
    pairs = [(i, i + offset) for i in range(count) if 0 <= i + offset < count]
    return lax.ppermute(array, axis, pairs)


def pair_math(q, do, k, v, nrm, dlt, mode):
    scale = q.shape[-1] ** (-0.5)
    nt = (((1,), (1,)), ((), ()))
    s_t = lax.dot_general(k, q, nt, preferred_element_type=jnp.float32) * scale
    rows = lax.broadcasted_iota(jnp.int32, s_t.shape, 0)
    cols = lax.broadcasted_iota(jnp.int32, s_t.shape, 1)
    full = (mode == 1).astype(jnp.float32)
    causal = (mode == 2).astype(jnp.float32)
    visible = full + causal * (rows <= cols).astype(jnp.float32)
    p_t = jnp.exp(s_t - nrm) * visible
    dv = jnp.dot(p_t.astype(jnp.bfloat16), do, preferred_element_type=jnp.float32)
    dp_t = lax.dot_general(v, do, nt, preferred_element_type=jnp.float32)
    ds_t = (p_t * (dp_t - dlt)).astype(jnp.bfloat16)
    dk = jnp.dot(ds_t, q, preferred_element_type=jnp.float32) * scale
    ds = jnp.transpose(ds_t.astype(jnp.float32)).astype(jnp.bfloat16)
    dq = jnp.dot(ds, k, preferred_element_type=jnp.float32) * scale
    return dq, dk, dv


def list_kernel(qin, qout, first, ktab, mtab, q_ref, do_ref, nrm_ref, dlt_ref, k_ref, v_ref, dq_ref, dk_ref, dv_ref):
    p = pl.program_id(0)
    mode = mtab[p]
    lead = first[p]
    heads = nrm_ref.shape[0]
    width = q_ref.shape[1] // heads
    for h in range(heads):
        cols = slice(h * width, (h + 1) * width)
        dq, dk, dv = pair_math(
            q_ref[:, cols], do_ref[:, cols], k_ref[:, cols], v_ref[:, cols],
            nrm_ref[h], dlt_ref[h], mode,
        )

        @pl.when(lead == 1)
        def _():
            dq_ref[:, cols] = dq

        @pl.when(lead == 0)
        def _():
            dq_ref[:, cols] += dq

        dk_ref[:, cols] = dk
        dv_ref[:, cols] = dv


def rand_kernel(heads, ktab, mtab, q_ref, do_ref, st_ref, k_ref, v_ref, dq_ref, dk_ref, dv_ref):
    p = pl.program_id(0)
    mode = mtab[p]
    width = q_ref.shape[2] // heads

    @pl.when(mode == 0)
    def _():
        dq_ref[...] = jnp.zeros_like(dq_ref)
        dk_ref[...] = jnp.zeros_like(dk_ref)
        dv_ref[...] = jnp.zeros_like(dv_ref)

    @pl.when(mode > 0)
    def _():
        for h in range(heads):
            cols = slice(h * width, (h + 1) * width)
            stats = st_ref[0, :, cols].astype(jnp.float32)
            dq, dk, dv = pair_math(
                q_ref[0, :, cols], do_ref[0, :, cols], k_ref[:, cols], v_ref[:, cols],
                stats[0:1, :], stats[1:2, :], mode,
            )
            dq_ref[0, :, cols] = dq.astype(jnp.bfloat16)
            dk_ref[0, :, cols] = dk
            dv_ref[0, :, cols] = dv


def list_pairs(qin, qout, first, ktab, mtab, outs, queries, out_grad, norm3, delta3, key_src, value_src):
    rows, features = queries.shape
    heads = norm3.shape[0]
    height = rows // (2 * PAIR)
    count = ktab.shape[0]
    blk = (height, features)
    stat = (heads, 1, height)
    grid_spec = pltpu.PrefetchScalarGridSpec(
        num_scalar_prefetch=5,
        grid=(count,),
        in_specs=[
            pl.BlockSpec(blk, lambda p, qi, qo, f, kt, mt: (qi[p], 0)),
            pl.BlockSpec(blk, lambda p, qi, qo, f, kt, mt: (qi[p], 0)),
            pl.BlockSpec(stat, lambda p, qi, qo, f, kt, mt: (0, 0, qi[p])),
            pl.BlockSpec(stat, lambda p, qi, qo, f, kt, mt: (0, 0, qi[p])),
            pl.BlockSpec(blk, lambda p, qi, qo, f, kt, mt: (kt[p], 0)),
            pl.BlockSpec(blk, lambda p, qi, qo, f, kt, mt: (kt[p], 0)),
        ],
        out_specs=[
            pl.BlockSpec(blk, lambda p, qi, qo, f, kt, mt: (qo[p], 0)),
            pl.BlockSpec(blk, lambda p, qi, qo, f, kt, mt: (p, 0)),
            pl.BlockSpec(blk, lambda p, qi, qo, f, kt, mt: (p, 0)),
        ],
    )
    return pl.pallas_call(
        list_kernel,
        grid_spec=grid_spec,
        out_shape=[
            jax.ShapeDtypeStruct((outs * height, features), jnp.float32),
            jax.ShapeDtypeStruct((count * height, features), jnp.float32),
            jax.ShapeDtypeStruct((count * height, features), jnp.float32),
        ],
    )(qin, qout, first, ktab, mtab, queries, out_grad, norm3, delta3, key_src, value_src)


def rand_pairs(ktab, mtab, arrived, key_rows, value_rows, heads):
    items, packed_rows, features = arrived.shape
    height = (packed_rows - STAT_ROWS) // 2
    grid_spec = pltpu.PrefetchScalarGridSpec(
        num_scalar_prefetch=2,
        grid=(items,),
        in_specs=[
            pl.BlockSpec((1, height, features), lambda p, kt, mt: (p, 0, 0)),
            pl.BlockSpec((1, height, features), lambda p, kt, mt: (p, 1, 0)),
            pl.BlockSpec(
                (1, STAT_ROWS, features), lambda p, kt, mt: (p, 2 * height // STAT_ROWS, 0)
            ),
            pl.BlockSpec((height, features), lambda p, kt, mt: (kt[p], 0)),
            pl.BlockSpec((height, features), lambda p, kt, mt: (kt[p], 0)),
        ],
        out_specs=[
            pl.BlockSpec((1, height, features), lambda p, kt, mt: (p, 0, 0)),
            pl.BlockSpec((1, height, features), lambda p, kt, mt: (p, 0, 0)),
            pl.BlockSpec((1, height, features), lambda p, kt, mt: (p, 0, 0)),
        ],
    )
    return pl.pallas_call(
        functools.partial(rand_kernel, heads),
        grid_spec=grid_spec,
        out_shape=[
            jax.ShapeDtypeStruct((items, height, features), jnp.bfloat16),
            jax.ShapeDtypeStruct((items, height, features), jnp.float32),
            jax.ShapeDtypeStruct((items, height, features), jnp.float32),
        ],
    )(ktab, mtab, arrived, arrived, arrived, key_rows, value_rows)


def shards(queries, key_rows, values, outputs, out_grad, log_norm, rand_blocks):
    ctx_size = lax.axis_size("ctx")
    my_index = lax.axis_index("ctx")
    row_count, features = queries.shape
    heads = log_norm.shape[0]
    slot_count = 2 * PAIR
    height = row_count // slot_count
    block_total = slot_count * ctx_size
    first_dev = my_index == 0
    last_dev = my_index == ctx_size - 1

    delta = jnp.sum(
        (out_grad.astype(jnp.float32) * outputs.astype(jnp.float32)).reshape(
            row_count, heads, features // heads
        ),
        axis=-1,
    )
    delta = jnp.transpose(delta).astype(jnp.bfloat16)
    norm3 = log_norm.astype(jnp.float32).reshape(heads, 1, row_count)
    delta3 = delta.astype(jnp.float32).reshape(heads, 1, row_count)

    def block(array, slot):
        return array[slot * height : (slot + 1) * height]

    from_left = shift(jnp.stack([block(key_rows, 1), block(values, 1)]), "ctx", 1)
    from_right = shift(jnp.stack([block(key_rows, 2), block(values, 2)]), "ctx", -1)
    global_kv = spread_2(jnp.stack([block(key_rows, 0), block(values, 0)]), "ctx", 0)
    key_win = jnp.concatenate([key_rows, from_left[0], from_right[0]])
    value_win = jnp.concatenate([values, from_left[1], from_right[1]])

    within = jnp.arange(slot_count, dtype=jnp.int32)
    seq_blk = jnp.where(
        within < PAIR, PAIR * my_index + within, block_total - 1 - PAIR * my_index - (within - PAIR)
    )
    last_prev = jnp.where(last_dev, 1, slot_count + 1).astype(jnp.int32)
    first_prev = jnp.where(first_dev, 0, 1).astype(jnp.int32)
    def table(*items):
        return jnp.stack([jnp.asarray(x, jnp.int32) for x in items])

    dq_own, dk_own, dv_own = list_pairs(
        table(0, 1, 1, 2, 2, 3), table(0, 1, 1, 2, 2, 3), table(1, 1, 0, 1, 0, 1),
        table(0, 1, 0, 2, 3, 3), table(2, 2, 1, 2, 1, 2), slot_count,
        queries, out_grad, norm3, delta3, key_rows, values,
    )
    dk_own = dk_own.reshape(6, height, features)
    dv_own = dv_own.reshape(6, height, features)
    dq_rim, dk_rim, dv_rim = list_pairs(
        table(0, slot_count - 1), table(0, 1), table(1, 1),
        table(slot_count, last_prev), table(first_prev, 1), 2,
        queries, out_grad, norm3, delta3, key_win, value_win,
    )
    dq_rim = dq_rim.reshape(2, height, features)
    dk_rim = dk_rim.reshape(2, height, features)
    dv_rim = dv_rim.reshape(2, height, features)
    glob_mode = (seq_blk >= WINDOW).astype(jnp.int32)
    global_kv, dq_own, dk_own, dv_own, dq_rim, dk_rim, dv_rim = lax.optimization_barrier(
        (global_kv, dq_own, dk_own, dv_own, dq_rim, dk_rim, dv_rim)
    )
    dq_glob, dk_glob, dv_glob = list_pairs(
        table(0, 1, 2, 3), table(0, 1, 2, 3), table(1, 1, 1, 1), table(0, 0, 0, 0), glob_mode,
        slot_count, queries, out_grad, norm3, delta3, global_kv[0], global_kv[1],
    )
    zero_blk = jnp.zeros((height, features), jnp.float32)
    dq_local = (
        dq_own + dq_glob
        + jnp.concatenate([dq_rim[0:1], zero_blk[None], zero_blk[None], dq_rim[1:2]]).reshape(
            row_count, features
        )
    )

    to_left = jnp.stack([dk_rim[0], dv_rim[0]]).astype(jnp.bfloat16)
    to_right = jnp.stack([dk_rim[1], dv_rim[1]]).astype(jnp.bfloat16)
    back_right = shift(to_left, "ctx", -1)
    back_left = shift(to_right, "ctx", 1)

    part = jnp.stack(
        [
            jnp.sum(dk_glob.reshape(slot_count, height, features), axis=0),
            jnp.sum(dv_glob.reshape(slot_count, height, features), axis=0),
        ]
    )
    total = gather_to_root(part, "ctx")

    ref_valid = rand_blocks >= 0
    in_front = rand_blocks < block_total // 2
    mirror = block_total - 1 - rand_blocks
    owner_dev = jnp.where(in_front, rand_blocks // PAIR, mirror // PAIR)
    owner_dev = jnp.where(ref_valid, owner_dev, ctx_size).reshape(-1)
    key_slot = jnp.where(in_front, rand_blocks % PAIR, PAIR + mirror % PAIR) + 1
    key_slot = jnp.where(ref_valid, key_slot, 0).reshape(-1)
    targets = jnp.arange(ctx_size, dtype=jnp.int32)
    matches = owner_dev[None, :] == targets[:, None]
    slot_send = jnp.sum(jnp.where(matches, key_slot[None, :], 0), axis=1)
    select = jnp.any(matches.reshape(ctx_size, slot_count, RANDOM), axis=2).astype(jnp.bfloat16)

    def per_slot_row(stat):
        return jnp.transpose(stat.reshape(heads, slot_count, height), (1, 0, 2)).reshape(
            slot_count, 1, features
        )

    packed = jnp.concatenate(
        [
            queries.reshape(slot_count, height, features),
            out_grad.reshape(slot_count, height, features),
            per_slot_row(log_norm),
            per_slot_row(delta),
        ],
        axis=1,
    )
    routed = jnp.dot(
        select, packed.reshape(slot_count, -1), preferred_element_type=jnp.float32
    ).astype(jnp.bfloat16)
    routed = routed.reshape(ctx_size, 2 * height + 2, features)
    slot_rows = jnp.broadcast_to(
        slot_send.astype(jnp.bfloat16)[:, None, None], (ctx_size, STAT_ROWS - 2, features)
    )
    routed = jnp.concatenate([routed, slot_rows], axis=1)
    routed, global_kv, from_left, from_right = lax.optimization_barrier(
        (routed, global_kv, from_left, from_right)
    )
    arrived = lax.all_to_all(routed, "ctx", split_axis=0, concat_axis=0, tiled=True)
    slot_recv = arrived[:, 2 * height + 2, 0].astype(jnp.float32).astype(jnp.int32)
    ktab_r = jnp.maximum(slot_recv - 1, 0)
    mtab_r = (slot_recv > 0).astype(jnp.int32)
    dq_rand, dk_rand, dv_rand = rand_pairs(ktab_r, mtab_r, arrived, key_rows, values, heads)
    dq_rand, total, back_left, back_right = lax.optimization_barrier(
        (dq_rand, total, back_left, back_right)
    )
    back_left = back_left.astype(jnp.float32)
    back_right = back_right.astype(jnp.float32)
    returned = lax.all_to_all(dq_rand, "ctx", split_axis=0, concat_axis=0, tiled=True)
    select_f = select.astype(jnp.float32)
    rand_query = jnp.sum(
        select_f[:, :, None, None] * returned.astype(jnp.float32)[:, None], axis=0
    )
    choose = (slot_recv[:, None] == jnp.arange(1, slot_count + 1)[None, :]).astype(jnp.float32)
    rand_key = jnp.sum(choose[:, :, None, None] * dk_rand[:, None], axis=0)
    rand_value = jnp.sum(choose[:, :, None, None] * dv_rand[:, None], axis=0)

    own_tail = jnp.where(last_dev, 1.0, 0.0).astype(jnp.float32)

    owner_flag = jnp.where(first_dev, 1.0, 0.0).astype(jnp.float32)

    def assemble(own, rim, which, rand_part):
        slots = [
            own[0] + own[2] + total[which] * owner_flag,
            own[1] + rim[1] * own_tail + back_right[which],
            own[3] + back_left[which],
            own[5] + own[4],
        ]
        whole = jnp.stack(slots) + rand_part
        return whole.reshape(row_count, features).astype(jnp.bfloat16)

    query_total = (dq_local + rand_query.reshape(row_count, features)).astype(jnp.bfloat16)
    return (
        query_total,
        assemble(dk_own, dk_rim, 0, rand_key),
        assemble(dv_own, dv_rim, 1, rand_value),
    )


def solution(mesh):
    return jax.shard_map(
        shards,
        mesh=mesh,
        in_specs=(
            P("ctx", "head"),
            P("ctx", "head"),
            P("ctx", "head"),
            P("ctx", "head"),
            P("ctx", "head"),
            P("head", "ctx"),
            P("ctx", None),
        ),
        out_specs=(P("ctx", "head"), P("ctx", "head"), P("ctx", "head")),
        check_vma=False,
    )
```

```python
import functools

import jax
import jax.numpy as jnp
from jax import lax
from jax.experimental import pallas as pl
from jax.experimental.pallas import tpu as pltpu
from jax.sharding import PartitionSpec as P

PAIR = 2
WINDOW = 2
GLOBAL = 1
RANDOM = 3
STAT_ROWS = 16


def spread_2(array, axis, root):
    count = lax.axis_size(axis)
    mine = lax.axis_index(axis) == root
    array = jnp.where(mine, array, jnp.zeros_like(array))
    step = 1
    while step < count:
        pairs = [(i, i + step) for i in range(step) if i + step < count]
        array = array + lax.ppermute(array, axis, pairs)
        step *= 2
    return array


def gather_to_root(array, axis):
    count = lax.axis_size(axis)
    step = 1
    while step * 2 < count:
        step *= 2
    while step >= 1:
        pairs = [(i + step, i) for i in range(step) if i + step < count]
        array = array + lax.ppermute(array, axis, pairs)
        step //= 2
    return array


def shift(array, axis, offset):
    count = lax.axis_size(axis)
    pairs = [(i, i + offset) for i in range(count) if 0 <= i + offset < count]
    return lax.ppermute(array, axis, pairs)


def pair_math(q, do, k, v, nrm, dlt, mode):
    scale = q.shape[-1] ** (-0.5)
    nt = (((1,), (1,)), ((), ()))
    s_t = lax.dot_general(k, q, nt, preferred_element_type=jnp.float32) * scale
    rows = lax.broadcasted_iota(jnp.int32, s_t.shape, 0)
    cols = lax.broadcasted_iota(jnp.int32, s_t.shape, 1)
    full = (mode == 1).astype(jnp.float32)
    causal = (mode == 2).astype(jnp.float32)
    visible = full + causal * (rows <= cols).astype(jnp.float32)
    p_t = jnp.exp(s_t - nrm) * visible
    dv = jnp.dot(p_t.astype(jnp.bfloat16), do, preferred_element_type=jnp.float32)
    dp_t = lax.dot_general(v, do, nt, preferred_element_type=jnp.float32)
    ds_t = (p_t * (dp_t - dlt)).astype(jnp.bfloat16)
    dk = jnp.dot(ds_t, q, preferred_element_type=jnp.float32) * scale
    ds = jnp.transpose(ds_t.astype(jnp.float32)).astype(jnp.bfloat16)
    dq = jnp.dot(ds, k, preferred_element_type=jnp.float32) * scale
    return dq, dk, dv


def list_kernel(qin, qout, first, ktab, mtab, q_ref, do_ref, nrm_ref, dlt_ref, k_ref, v_ref, dq_ref, dk_ref, dv_ref):
    p = pl.program_id(0)
    mode = mtab[p]
    lead = first[p]
    heads = nrm_ref.shape[0]
    width = q_ref.shape[1] // heads
    for h in range(heads):
        cols = slice(h * width, (h + 1) * width)
        dq, dk, dv = pair_math(
            q_ref[:, cols], do_ref[:, cols], k_ref[:, cols], v_ref[:, cols],
            nrm_ref[h], dlt_ref[h], mode,
        )

        @pl.when(lead == 1)
        def _():
            dq_ref[:, cols] = dq

        @pl.when(lead == 0)
        def _():
            dq_ref[:, cols] += dq

        dk_ref[:, cols] = dk
        dv_ref[:, cols] = dv


def rand_kernel(heads, ktab, mtab, q_ref, do_ref, st_ref, k_ref, v_ref, dq_ref, dk_ref, dv_ref):
    p = pl.program_id(0)
    mode = mtab[p]
    width = q_ref.shape[2] // heads

    @pl.when(mode == 0)
    def _():
        dq_ref[...] = jnp.zeros_like(dq_ref)
        dk_ref[...] = jnp.zeros_like(dk_ref)
        dv_ref[...] = jnp.zeros_like(dv_ref)

    @pl.when(mode > 0)
    def _():
        for h in range(heads):
            cols = slice(h * width, (h + 1) * width)
            stats = st_ref[0, :, cols].astype(jnp.float32)
            dq, dk, dv = pair_math(
                q_ref[0, :, cols], do_ref[0, :, cols], k_ref[:, cols], v_ref[:, cols],
                stats[0:1, :], stats[1:2, :], mode,
            )
            dq_ref[0, :, cols] = dq.astype(jnp.bfloat16)
            dk_ref[0, :, cols] = dk
            dv_ref[0, :, cols] = dv


def list_pairs(qin, qout, first, ktab, mtab, outs, queries, out_grad, norm3, delta3, key_src, value_src):
    rows, features = queries.shape
    heads = norm3.shape[0]
    height = rows // (2 * PAIR)
    count = ktab.shape[0]
    blk = (height, features)
    stat = (heads, 1, height)
    grid_spec = pltpu.PrefetchScalarGridSpec(
        num_scalar_prefetch=5,
        grid=(count,),
        in_specs=[
            pl.BlockSpec(blk, lambda p, qi, qo, f, kt, mt: (qi[p], 0)),
            pl.BlockSpec(blk, lambda p, qi, qo, f, kt, mt: (qi[p], 0)),
            pl.BlockSpec(stat, lambda p, qi, qo, f, kt, mt: (0, 0, qi[p])),
            pl.BlockSpec(stat, lambda p, qi, qo, f, kt, mt: (0, 0, qi[p])),
            pl.BlockSpec(blk, lambda p, qi, qo, f, kt, mt: (kt[p], 0)),
            pl.BlockSpec(blk, lambda p, qi, qo, f, kt, mt: (kt[p], 0)),
        ],
        out_specs=[
            pl.BlockSpec(blk, lambda p, qi, qo, f, kt, mt: (qo[p], 0)),
            pl.BlockSpec(blk, lambda p, qi, qo, f, kt, mt: (p, 0)),
            pl.BlockSpec(blk, lambda p, qi, qo, f, kt, mt: (p, 0)),
        ],
    )
    return pl.pallas_call(
        list_kernel,
        grid_spec=grid_spec,
        out_shape=[
            jax.ShapeDtypeStruct((outs * height, features), jnp.float32),
            jax.ShapeDtypeStruct((count * height, features), jnp.float32),
            jax.ShapeDtypeStruct((count * height, features), jnp.float32),
        ],
    )(qin, qout, first, ktab, mtab, queries, out_grad, norm3, delta3, key_src, value_src)


def rand_pairs(ktab, mtab, arrived, key_rows, value_rows, heads):
    items, packed_rows, features = arrived.shape
    height = (packed_rows - STAT_ROWS) // 2
    grid_spec = pltpu.PrefetchScalarGridSpec(
        num_scalar_prefetch=2,
        grid=(items,),
        in_specs=[
            pl.BlockSpec((1, height, features), lambda p, kt, mt: (p, 0, 0)),
            pl.BlockSpec((1, height, features), lambda p, kt, mt: (p, 1, 0)),
            pl.BlockSpec(
                (1, STAT_ROWS, features), lambda p, kt, mt: (p, 2 * height // STAT_ROWS, 0)
            ),
            pl.BlockSpec((height, features), lambda p, kt, mt: (kt[p], 0)),
            pl.BlockSpec((height, features), lambda p, kt, mt: (kt[p], 0)),
        ],
        out_specs=[
            pl.BlockSpec((1, height, features), lambda p, kt, mt: (p, 0, 0)),
            pl.BlockSpec((1, height, features), lambda p, kt, mt: (p, 0, 0)),
            pl.BlockSpec((1, height, features), lambda p, kt, mt: (p, 0, 0)),
        ],
    )
    return pl.pallas_call(
        functools.partial(rand_kernel, heads),
        grid_spec=grid_spec,
        out_shape=[
            jax.ShapeDtypeStruct((items, height, features), jnp.bfloat16),
            jax.ShapeDtypeStruct((items, height, features), jnp.float32),
            jax.ShapeDtypeStruct((items, height, features), jnp.float32),
        ],
    )(ktab, mtab, arrived, arrived, arrived, key_rows, value_rows)


def shards(queries, key_rows, values, outputs, out_grad, log_norm, rand_blocks):
    ctx_size = lax.axis_size("ctx")
    my_index = lax.axis_index("ctx")
    row_count, features = queries.shape
    heads = log_norm.shape[0]
    slot_count = 2 * PAIR
    height = row_count // slot_count
    block_total = slot_count * ctx_size
    first_dev = my_index == 0
    last_dev = my_index == ctx_size - 1

    delta = jnp.sum(
        (out_grad.astype(jnp.float32) * outputs.astype(jnp.float32)).reshape(
            row_count, heads, features // heads
        ),
        axis=-1,
    )
    delta = jnp.transpose(delta).astype(jnp.bfloat16)
    norm3 = log_norm.astype(jnp.float32).reshape(heads, 1, row_count)
    delta3 = delta.astype(jnp.float32).reshape(heads, 1, row_count)

    def block(array, slot):
        return array[slot * height : (slot + 1) * height]

    from_left = shift(jnp.stack([block(key_rows, 1), block(values, 1)]), "ctx", 1)
    from_right = shift(jnp.stack([block(key_rows, 2), block(values, 2)]), "ctx", -1)
    global_kv = spread_2(jnp.stack([block(key_rows, 0), block(values, 0)]), "ctx", 0)
    key_win = jnp.concatenate([key_rows, from_left[0], from_right[0]])
    value_win = jnp.concatenate([values, from_left[1], from_right[1]])

    within = jnp.arange(slot_count, dtype=jnp.int32)
    seq_blk = jnp.where(
        within < PAIR, PAIR * my_index + within, block_total - 1 - PAIR * my_index - (within - PAIR)
    )
    last_prev = jnp.where(last_dev, 1, slot_count + 1).astype(jnp.int32)
    first_prev = jnp.where(first_dev, 0, 1).astype(jnp.int32)
    def table(*items):
        return jnp.stack([jnp.asarray(x, jnp.int32) for x in items])

    dq_own, dk_own, dv_own = list_pairs(
        table(0, 1, 1, 2, 2, 3), table(0, 1, 1, 2, 2, 3), table(1, 1, 0, 1, 0, 1),
        table(0, 1, 0, 2, 3, 3), table(2, 2, 1, 2, 1, 2), slot_count,
        queries, out_grad, norm3, delta3, key_rows, values,
    )
    dk_own = dk_own.reshape(6, height, features)
    dv_own = dv_own.reshape(6, height, features)
    dq_rim, dk_rim, dv_rim = list_pairs(
        table(0, slot_count - 1), table(0, 1), table(1, 1),
        table(slot_count, last_prev), table(first_prev, 1), 2,
        queries, out_grad, norm3, delta3, key_win, value_win,
    )
    dq_rim = dq_rim.reshape(2, height, features)
    dk_rim = dk_rim.reshape(2, height, features)
    dv_rim = dv_rim.reshape(2, height, features)
    glob_mode = (seq_blk >= WINDOW).astype(jnp.int32)
    dq_glob, dk_glob, dv_glob = list_pairs(
        table(0, 1, 2, 3), table(0, 1, 2, 3), table(1, 1, 1, 1), table(0, 0, 0, 0), glob_mode,
        slot_count, queries, out_grad, norm3, delta3, global_kv[0], global_kv[1],
    )
    zero_blk = jnp.zeros((height, features), jnp.float32)
    dq_local = (
        dq_own + dq_glob
        + jnp.concatenate([dq_rim[0:1], zero_blk[None], zero_blk[None], dq_rim[1:2]]).reshape(
            row_count, features
        )
    )

    to_left = jnp.stack([dk_rim[0], dv_rim[0]]).astype(jnp.bfloat16)
    to_right = jnp.stack([dk_rim[1], dv_rim[1]]).astype(jnp.bfloat16)
    back_right = shift(to_left, "ctx", -1)
    back_left = shift(to_right, "ctx", 1)

    part = jnp.stack(
        [
            jnp.sum(dk_glob.reshape(slot_count, height, features), axis=0),
            jnp.sum(dv_glob.reshape(slot_count, height, features), axis=0),
        ]
    )
    total = gather_to_root(part, "ctx")

    ref_valid = rand_blocks >= 0
    in_front = rand_blocks < block_total // 2
    mirror = block_total - 1 - rand_blocks
    owner_dev = jnp.where(in_front, rand_blocks // PAIR, mirror // PAIR)
    owner_dev = jnp.where(ref_valid, owner_dev, ctx_size).reshape(-1)
    key_slot = jnp.where(in_front, rand_blocks % PAIR, PAIR + mirror % PAIR) + 1
    key_slot = jnp.where(ref_valid, key_slot, 0).reshape(-1)
    targets = jnp.arange(ctx_size, dtype=jnp.int32)
    matches = owner_dev[None, :] == targets[:, None]
    slot_send = jnp.sum(jnp.where(matches, key_slot[None, :], 0), axis=1)
    select = jnp.any(matches.reshape(ctx_size, slot_count, RANDOM), axis=2).astype(jnp.bfloat16)

    def per_slot_row(stat):
        return jnp.transpose(stat.reshape(heads, slot_count, height), (1, 0, 2)).reshape(
            slot_count, 1, features
        )

    packed = jnp.concatenate(
        [
            queries.reshape(slot_count, height, features),
            out_grad.reshape(slot_count, height, features),
            per_slot_row(log_norm),
            per_slot_row(delta),
            jnp.zeros((slot_count, STAT_ROWS - 2, features), jnp.bfloat16),
        ],
        axis=1,
    )
    pick = select > 0
    routed = jnp.sum(jnp.where(pick[:, :, None, None], packed[None], 0), axis=1).astype(
        jnp.bfloat16
    )
    row_id = lax.broadcasted_iota(jnp.int32, (1, packed.shape[1], 1), 1)
    routed = jnp.where(
        row_id == 2 * height + 2, slot_send.astype(jnp.bfloat16)[:, None, None], routed
    )
    arrived = lax.all_to_all(routed, "ctx", split_axis=0, concat_axis=0, tiled=True)
    slot_recv = arrived[:, 2 * height + 2, 0].astype(jnp.float32).astype(jnp.int32)
    ktab_r = jnp.maximum(slot_recv - 1, 0)
    mtab_r = (slot_recv > 0).astype(jnp.int32)
    dq_rand, dk_rand, dv_rand = rand_pairs(ktab_r, mtab_r, arrived, key_rows, values, heads)
    dq_rand, total, back_left, back_right = lax.optimization_barrier(
        (dq_rand, total, back_left, back_right)
    )
    back_left = back_left.astype(jnp.float32)
    back_right = back_right.astype(jnp.float32)
    returned = lax.all_to_all(dq_rand, "ctx", split_axis=0, concat_axis=0, tiled=True)
    select_f = select.astype(jnp.float32)
    rand_query = jnp.sum(
        select_f[:, :, None, None] * returned.astype(jnp.float32)[:, None], axis=0
    )
    choose = (slot_recv[:, None] == jnp.arange(1, slot_count + 1)[None, :]).astype(jnp.float32)
    rand_key = jnp.sum(choose[:, :, None, None] * dk_rand[:, None], axis=0)
    rand_value = jnp.sum(choose[:, :, None, None] * dv_rand[:, None], axis=0)

    own_tail = jnp.where(last_dev, 1.0, 0.0).astype(jnp.float32)

    owner_flag = jnp.where(first_dev, 1.0, 0.0).astype(jnp.float32)

    def assemble(own, rim, which, rand_part):
        slots = [
            own[0] + own[2] + total[which] * owner_flag,
            own[1] + rim[1] * own_tail + back_right[which],
            own[3] + back_left[which],
            own[5] + own[4],
        ]
        whole = jnp.stack(slots) + rand_part
        return whole.reshape(row_count, features).astype(jnp.bfloat16)

    query_total = (dq_local + rand_query.reshape(row_count, features)).astype(jnp.bfloat16)
    return (
        query_total,
        assemble(dk_own, dk_rim, 0, rand_key),
        assemble(dv_own, dv_rim, 1, rand_value),
    )


def solution(mesh):
    return jax.shard_map(
        shards,
        mesh=mesh,
        in_specs=(
            P("ctx", "head"),
            P("ctx", "head"),
            P("ctx", "head"),
            P("ctx", "head"),
            P("ctx", "head"),
            P("head", "ctx"),
            P("ctx", None),
        ),
        out_specs=(P("ctx", "head"), P("ctx", "head"), P("ctx", "head")),
        check_vma=False,
    )
```

```python
import functools

import jax
import jax.numpy as jnp
from jax import lax
from jax.experimental import pallas as pl
from jax.experimental.pallas import tpu as pltpu
from jax.sharding import PartitionSpec as P

PAIR = 2
WINDOW = 2
GLOBAL = 1
RANDOM = 3
STAT_ROWS = 16


RADIX = 4


def spread_2(array, axis, root):
    count = lax.axis_size(axis)
    mine = lax.axis_index(axis) == root
    array = jnp.where(mine, array, jnp.zeros_like(array))
    step = 1
    while step * RADIX < count:
        step *= RADIX
    while step >= 1:
        arrived = [
            lax.ppermute(array, axis, [(i, i + j * step) for i in range(0, count, RADIX * step) if i + j * step < count])
            for j in range(1, RADIX)
            if j * step < count
        ]
        for part in arrived:
            array = array + part
        step //= RADIX
    return array


def gather_to_root(array, axis):
    count = lax.axis_size(axis)
    step = 1
    while step < count:
        arrived = [
            lax.ppermute(array, axis, [(i + j * step, i) for i in range(0, count, RADIX * step) if i + j * step < count])
            for j in range(1, RADIX)
            if j * step < count
        ]
        for part in arrived:
            array = array + part
        step *= RADIX
    return array


def shift(array, axis, offset):
    count = lax.axis_size(axis)
    pairs = [(i, i + offset) for i in range(count) if 0 <= i + offset < count]
    return lax.ppermute(array, axis, pairs)


def pair_math(q, do, k, v, nrm, dlt, mode):
    scale = q.shape[-1] ** (-0.5)
    nt = (((1,), (1,)), ((), ()))
    s_t = lax.dot_general(k, q, nt, preferred_element_type=jnp.float32) * scale
    rows = lax.broadcasted_iota(jnp.int32, s_t.shape, 0)
    cols = lax.broadcasted_iota(jnp.int32, s_t.shape, 1)
    full = (mode == 1).astype(jnp.float32)
    causal = (mode == 2).astype(jnp.float32)
    visible = full + causal * (rows <= cols).astype(jnp.float32)
    p_t = jnp.exp(s_t - nrm) * visible
    dv = jnp.dot(p_t.astype(jnp.bfloat16), do, preferred_element_type=jnp.float32)
    dp_t = lax.dot_general(v, do, nt, preferred_element_type=jnp.float32)
    ds_t = (p_t * (dp_t - dlt)).astype(jnp.bfloat16)
    dk = jnp.dot(ds_t, q, preferred_element_type=jnp.float32) * scale
    ds = jnp.transpose(ds_t.astype(jnp.float32)).astype(jnp.bfloat16)
    dq = jnp.dot(ds, k, preferred_element_type=jnp.float32) * scale
    return dq, dk, dv


def list_kernel(qin, qout, first, ktab, mtab, q_ref, do_ref, nrm_ref, dlt_ref, k_ref, v_ref, dq_ref, dk_ref, dv_ref):
    p = pl.program_id(0)
    mode = mtab[p]
    lead = first[p]
    heads = nrm_ref.shape[0]
    width = q_ref.shape[1] // heads
    for h in range(heads):
        cols = slice(h * width, (h + 1) * width)
        dq, dk, dv = pair_math(
            q_ref[:, cols], do_ref[:, cols], k_ref[:, cols], v_ref[:, cols],
            nrm_ref[h], dlt_ref[h], mode,
        )

        @pl.when(lead == 1)
        def _():
            dq_ref[:, cols] = dq

        @pl.when(lead == 0)
        def _():
            dq_ref[:, cols] += dq

        dk_ref[:, cols] = dk
        dv_ref[:, cols] = dv


def rand_kernel(heads, ktab, mtab, q_ref, do_ref, st_ref, k_ref, v_ref, dq_ref, dk_ref, dv_ref):
    p = pl.program_id(0)
    mode = mtab[p]
    width = q_ref.shape[2] // heads

    @pl.when(mode == 0)
    def _():
        dq_ref[...] = jnp.zeros_like(dq_ref)
        dk_ref[...] = jnp.zeros_like(dk_ref)
        dv_ref[...] = jnp.zeros_like(dv_ref)

    @pl.when(mode > 0)
    def _():
        for h in range(heads):
            cols = slice(h * width, (h + 1) * width)
            stats = st_ref[0, :, cols].astype(jnp.float32)
            dq, dk, dv = pair_math(
                q_ref[0, :, cols], do_ref[0, :, cols], k_ref[:, cols], v_ref[:, cols],
                stats[0:1, :], stats[1:2, :], mode,
            )
            dq_ref[0, :, cols] = dq.astype(jnp.bfloat16)
            dk_ref[0, :, cols] = dk
            dv_ref[0, :, cols] = dv


def list_pairs(qin, qout, first, ktab, mtab, outs, queries, out_grad, norm3, delta3, key_src, value_src):
    rows, features = queries.shape
    heads = norm3.shape[0]
    height = rows // (2 * PAIR)
    count = ktab.shape[0]
    blk = (height, features)
    stat = (heads, 1, height)
    grid_spec = pltpu.PrefetchScalarGridSpec(
        num_scalar_prefetch=5,
        grid=(count,),
        in_specs=[
            pl.BlockSpec(blk, lambda p, qi, qo, f, kt, mt: (qi[p], 0)),
            pl.BlockSpec(blk, lambda p, qi, qo, f, kt, mt: (qi[p], 0)),
            pl.BlockSpec(stat, lambda p, qi, qo, f, kt, mt: (0, 0, qi[p])),
            pl.BlockSpec(stat, lambda p, qi, qo, f, kt, mt: (0, 0, qi[p])),
            pl.BlockSpec(blk, lambda p, qi, qo, f, kt, mt: (kt[p], 0)),
            pl.BlockSpec(blk, lambda p, qi, qo, f, kt, mt: (kt[p], 0)),
        ],
        out_specs=[
            pl.BlockSpec(blk, lambda p, qi, qo, f, kt, mt: (qo[p], 0)),
            pl.BlockSpec(blk, lambda p, qi, qo, f, kt, mt: (p, 0)),
            pl.BlockSpec(blk, lambda p, qi, qo, f, kt, mt: (p, 0)),
        ],
    )
    return pl.pallas_call(
        list_kernel,
        grid_spec=grid_spec,
        out_shape=[
            jax.ShapeDtypeStruct((outs * height, features), jnp.float32),
            jax.ShapeDtypeStruct((count * height, features), jnp.float32),
            jax.ShapeDtypeStruct((count * height, features), jnp.float32),
        ],
    )(qin, qout, first, ktab, mtab, queries, out_grad, norm3, delta3, key_src, value_src)


def rand_pairs(ktab, mtab, arrived, key_rows, value_rows, heads):
    items, packed_rows, features = arrived.shape
    height = (packed_rows - STAT_ROWS) // 2
    grid_spec = pltpu.PrefetchScalarGridSpec(
        num_scalar_prefetch=2,
        grid=(items,),
        in_specs=[
            pl.BlockSpec((1, height, features), lambda p, kt, mt: (p, 0, 0)),
            pl.BlockSpec((1, height, features), lambda p, kt, mt: (p, 1, 0)),
            pl.BlockSpec(
                (1, STAT_ROWS, features), lambda p, kt, mt: (p, 2 * height // STAT_ROWS, 0)
            ),
            pl.BlockSpec((height, features), lambda p, kt, mt: (kt[p], 0)),
            pl.BlockSpec((height, features), lambda p, kt, mt: (kt[p], 0)),
        ],
        out_specs=[
            pl.BlockSpec((1, height, features), lambda p, kt, mt: (p, 0, 0)),
            pl.BlockSpec((1, height, features), lambda p, kt, mt: (p, 0, 0)),
            pl.BlockSpec((1, height, features), lambda p, kt, mt: (p, 0, 0)),
        ],
    )
    return pl.pallas_call(
        functools.partial(rand_kernel, heads),
        grid_spec=grid_spec,
        out_shape=[
            jax.ShapeDtypeStruct((items, height, features), jnp.bfloat16),
            jax.ShapeDtypeStruct((items, height, features), jnp.float32),
            jax.ShapeDtypeStruct((items, height, features), jnp.float32),
        ],
    )(ktab, mtab, arrived, arrived, arrived, key_rows, value_rows)


def shards(queries, key_rows, values, outputs, out_grad, log_norm, rand_blocks):
    ctx_size = lax.axis_size("ctx")
    my_index = lax.axis_index("ctx")
    row_count, features = queries.shape
    heads = log_norm.shape[0]
    slot_count = 2 * PAIR
    height = row_count // slot_count
    block_total = slot_count * ctx_size
    first_dev = my_index == 0
    last_dev = my_index == ctx_size - 1

    delta = jnp.sum(
        (out_grad.astype(jnp.float32) * outputs.astype(jnp.float32)).reshape(
            row_count, heads, features // heads
        ),
        axis=-1,
    )
    delta = jnp.transpose(delta).astype(jnp.bfloat16)
    norm3 = log_norm.astype(jnp.float32).reshape(heads, 1, row_count)
    delta3 = delta.astype(jnp.float32).reshape(heads, 1, row_count)

    def block(array, slot):
        return array[slot * height : (slot + 1) * height]

    from_left = shift(jnp.stack([block(key_rows, 1), block(values, 1)]), "ctx", 1)
    from_right = shift(jnp.stack([block(key_rows, 2), block(values, 2)]), "ctx", -1)
    global_kv = spread_2(jnp.stack([block(key_rows, 0), block(values, 0)]), "ctx", 0)
    key_win = jnp.concatenate([key_rows, from_left[0], from_right[0]])
    value_win = jnp.concatenate([values, from_left[1], from_right[1]])

    within = jnp.arange(slot_count, dtype=jnp.int32)
    seq_blk = jnp.where(
        within < PAIR, PAIR * my_index + within, block_total - 1 - PAIR * my_index - (within - PAIR)
    )
    last_prev = jnp.where(last_dev, 1, slot_count + 1).astype(jnp.int32)
    first_prev = jnp.where(first_dev, 0, 1).astype(jnp.int32)
    def table(*items):
        return jnp.stack([jnp.asarray(x, jnp.int32) for x in items])

    dq_own, dk_own, dv_own = list_pairs(
        table(0, 1, 1, 2, 2, 3), table(0, 1, 1, 2, 2, 3), table(1, 1, 0, 1, 0, 1),
        table(0, 1, 0, 2, 3, 3), table(2, 2, 1, 2, 1, 2), slot_count,
        queries, out_grad, norm3, delta3, key_rows, values,
    )
    dk_own = dk_own.reshape(6, height, features)
    dv_own = dv_own.reshape(6, height, features)
    dq_rim, dk_rim, dv_rim = list_pairs(
        table(0, slot_count - 1), table(0, 1), table(1, 1),
        table(slot_count, last_prev), table(first_prev, 1), 2,
        queries, out_grad, norm3, delta3, key_win, value_win,
    )
    dq_rim = dq_rim.reshape(2, height, features)
    dk_rim = dk_rim.reshape(2, height, features)
    dv_rim = dv_rim.reshape(2, height, features)
    glob_mode = (seq_blk >= WINDOW).astype(jnp.int32)
    dq_glob, dk_glob, dv_glob = list_pairs(
        table(0, 1, 2, 3), table(0, 1, 2, 3), table(1, 1, 1, 1), table(0, 0, 0, 0), glob_mode,
        slot_count, queries, out_grad, norm3, delta3, global_kv[0], global_kv[1],
    )
    zero_blk = jnp.zeros((height, features), jnp.float32)
    dq_local = (
        dq_own + dq_glob
        + jnp.concatenate([dq_rim[0:1], zero_blk[None], zero_blk[None], dq_rim[1:2]]).reshape(
            row_count, features
        )
    )

    to_left = jnp.stack([dk_rim[0], dv_rim[0]]).astype(jnp.bfloat16)
    to_right = jnp.stack([dk_rim[1], dv_rim[1]]).astype(jnp.bfloat16)
    back_right = shift(to_left, "ctx", -1)
    back_left = shift(to_right, "ctx", 1)

    part = jnp.stack(
        [
            jnp.sum(dk_glob.reshape(slot_count, height, features), axis=0),
            jnp.sum(dv_glob.reshape(slot_count, height, features), axis=0),
        ]
    )
    total = gather_to_root(part, "ctx")

    ref_valid = rand_blocks >= 0
    in_front = rand_blocks < block_total // 2
    mirror = block_total - 1 - rand_blocks
    owner_dev = jnp.where(in_front, rand_blocks // PAIR, mirror // PAIR)
    owner_dev = jnp.where(ref_valid, owner_dev, ctx_size).reshape(-1)
    key_slot = jnp.where(in_front, rand_blocks % PAIR, PAIR + mirror % PAIR) + 1
    key_slot = jnp.where(ref_valid, key_slot, 0).reshape(-1)
    targets = jnp.arange(ctx_size, dtype=jnp.int32)
    matches = owner_dev[None, :] == targets[:, None]
    slot_send = jnp.sum(jnp.where(matches, key_slot[None, :], 0), axis=1)
    select = jnp.any(matches.reshape(ctx_size, slot_count, RANDOM), axis=2).astype(jnp.bfloat16)

    def per_slot_row(stat):
        return jnp.transpose(stat.reshape(heads, slot_count, height), (1, 0, 2)).reshape(
            slot_count, 1, features
        )

    packed = jnp.concatenate(
        [
            queries.reshape(slot_count, height, features),
            out_grad.reshape(slot_count, height, features),
            per_slot_row(log_norm),
            per_slot_row(delta),
            jnp.zeros((slot_count, STAT_ROWS - 2, features), jnp.bfloat16),
        ],
        axis=1,
    )
    pick = select > 0
    routed = jnp.sum(jnp.where(pick[:, :, None, None], packed[None], 0), axis=1).astype(
        jnp.bfloat16
    )
    row_id = lax.broadcasted_iota(jnp.int32, (1, packed.shape[1], 1), 1)
    routed = jnp.where(
        row_id == 2 * height + 2, slot_send.astype(jnp.bfloat16)[:, None, None], routed
    )
    arrived = lax.all_to_all(routed, "ctx", split_axis=0, concat_axis=0, tiled=True)
    slot_recv = arrived[:, 2 * height + 2, 0].astype(jnp.float32).astype(jnp.int32)
    ktab_r = jnp.maximum(slot_recv - 1, 0)
    mtab_r = (slot_recv > 0).astype(jnp.int32)
    dq_rand, dk_rand, dv_rand = rand_pairs(ktab_r, mtab_r, arrived, key_rows, values, heads)
    dq_rand, total, back_left, back_right = lax.optimization_barrier(
        (dq_rand, total, back_left, back_right)
    )
    back_left = back_left.astype(jnp.float32)
    back_right = back_right.astype(jnp.float32)
    returned = lax.all_to_all(dq_rand, "ctx", split_axis=0, concat_axis=0, tiled=True)
    select_f = select.astype(jnp.float32)
    rand_query = jnp.sum(
        select_f[:, :, None, None] * returned.astype(jnp.float32)[:, None], axis=0
    )
    choose = (slot_recv[:, None] == jnp.arange(1, slot_count + 1)[None, :]).astype(jnp.float32)
    rand_key = jnp.sum(choose[:, :, None, None] * dk_rand[:, None], axis=0)
    rand_value = jnp.sum(choose[:, :, None, None] * dv_rand[:, None], axis=0)

    own_tail = jnp.where(last_dev, 1.0, 0.0).astype(jnp.float32)

    owner_flag = jnp.where(first_dev, 1.0, 0.0).astype(jnp.float32)

    def assemble(own, rim, which, rand_part):
        slots = [
            own[0] + own[2] + total[which] * owner_flag,
            own[1] + rim[1] * own_tail + back_right[which],
            own[3] + back_left[which],
            own[5] + own[4],
        ]
        whole = jnp.stack(slots) + rand_part
        return whole.reshape(row_count, features).astype(jnp.bfloat16)

    query_total = (dq_local + rand_query.reshape(row_count, features)).astype(jnp.bfloat16)
    return (
        query_total,
        assemble(dk_own, dk_rim, 0, rand_key),
        assemble(dv_own, dv_rim, 1, rand_value),
    )


def solution(mesh):
    return jax.shard_map(
        shards,
        mesh=mesh,
        in_specs=(
            P("ctx", "head"),
            P("ctx", "head"),
            P("ctx", "head"),
            P("ctx", "head"),
            P("ctx", "head"),
            P("head", "ctx"),
            P("ctx", None),
        ),
        out_specs=(P("ctx", "head"), P("ctx", "head"), P("ctx", "head")),
        check_vma=False,
    )
```

```python
import functools

import jax
import jax.numpy as jnp
from jax import lax
from jax.experimental import pallas as pl
from jax.experimental.pallas import tpu as pltpu
from jax.sharding import PartitionSpec as P

PAIR = 2
WINDOW = 2
GLOBAL = 1
RANDOM = 3
STAT_ROWS = 16


RADIX = 4


def spread_2(array, axis, root):
    count = lax.axis_size(axis)
    mine = lax.axis_index(axis) == root
    array = jnp.where(mine, array, jnp.zeros_like(array))
    step = 1
    while step * RADIX < count:
        step *= RADIX
    while step >= 1:
        arrived = [
            lax.ppermute(array, axis, [(i, i + j * step) for i in range(0, count, RADIX * step) if i + j * step < count])
            for j in range(1, RADIX)
            if j * step < count
        ]
        for part in arrived:
            array = array + part
        step //= RADIX
    return array


def gather_to_root(array, axis):
    count = lax.axis_size(axis)
    step = 1
    while step < count:
        arrived = [
            lax.ppermute(array, axis, [(i + j * step, i) for i in range(0, count, RADIX * step) if i + j * step < count])
            for j in range(1, RADIX)
            if j * step < count
        ]
        for part in arrived:
            array = array + part
        step *= RADIX
    return array


def shift(array, axis, offset):
    count = lax.axis_size(axis)
    pairs = [(i, i + offset) for i in range(count) if 0 <= i + offset < count]
    return lax.ppermute(array, axis, pairs)


def pair_math(q, do, k, v, nrm, dlt, mode):
    scale = q.shape[-1] ** (-0.5)
    nt = (((1,), (1,)), ((), ()))
    s_t = lax.dot_general(k, q, nt, preferred_element_type=jnp.float32) * scale
    rows = lax.broadcasted_iota(jnp.int32, s_t.shape, 0)
    cols = lax.broadcasted_iota(jnp.int32, s_t.shape, 1)
    full = (mode == 1).astype(jnp.float32)
    causal = (mode == 2).astype(jnp.float32)
    visible = full + causal * (rows <= cols).astype(jnp.float32)
    p_t = jnp.exp(s_t - nrm) * visible
    dv = jnp.dot(p_t.astype(jnp.bfloat16), do, preferred_element_type=jnp.float32)
    dp_t = lax.dot_general(v, do, nt, preferred_element_type=jnp.float32)
    ds_t = (p_t * (dp_t - dlt)).astype(jnp.bfloat16)
    dk = jnp.dot(ds_t, q, preferred_element_type=jnp.float32) * scale
    ds = jnp.transpose(ds_t.astype(jnp.float32)).astype(jnp.bfloat16)
    dq = jnp.dot(ds, k, preferred_element_type=jnp.float32) * scale
    return dq, dk, dv


def list_kernel(qin, qout, first, ktab, mtab, q_ref, do_ref, nrm_ref, dlt_ref, k_ref, v_ref, dq_ref, dk_ref, dv_ref):
    p = pl.program_id(0)
    mode = mtab[p]
    lead = first[p]
    heads = nrm_ref.shape[0]
    width = q_ref.shape[1] // heads
    for h in range(heads):
        cols = slice(h * width, (h + 1) * width)
        dq, dk, dv = pair_math(
            q_ref[:, cols], do_ref[:, cols], k_ref[:, cols], v_ref[:, cols],
            nrm_ref[h], dlt_ref[h], mode,
        )

        @pl.when(lead == 1)
        def _():
            dq_ref[:, cols] = dq

        @pl.when(lead == 0)
        def _():
            dq_ref[:, cols] += dq

        dk_ref[:, cols] = dk
        dv_ref[:, cols] = dv


def rand_kernel(heads, ktab, mtab, q_ref, do_ref, st_ref, k_ref, v_ref, dq_ref, dk_ref, dv_ref):
    p = pl.program_id(0)
    mode = mtab[p]
    width = q_ref.shape[2] // heads

    @pl.when(mode == 0)
    def _():
        dq_ref[...] = jnp.zeros_like(dq_ref)
        dk_ref[...] = jnp.zeros_like(dk_ref)
        dv_ref[...] = jnp.zeros_like(dv_ref)

    @pl.when(mode > 0)
    def _():
        for h in range(heads):
            cols = slice(h * width, (h + 1) * width)
            stats = st_ref[0, :, cols].astype(jnp.float32)
            dq, dk, dv = pair_math(
                q_ref[0, :, cols], do_ref[0, :, cols], k_ref[:, cols], v_ref[:, cols],
                stats[0:1, :], stats[1:2, :], mode,
            )
            dq_ref[0, :, cols] = dq.astype(jnp.bfloat16)
            dk_ref[0, :, cols] = dk
            dv_ref[0, :, cols] = dv


def list_pairs(qin, qout, first, ktab, mtab, outs, queries, out_grad, norm3, delta3, key_src, value_src):
    rows, features = queries.shape
    heads = norm3.shape[0]
    height = rows // (2 * PAIR)
    count = ktab.shape[0]
    blk = (height, features)
    stat = (heads, 1, height)
    grid_spec = pltpu.PrefetchScalarGridSpec(
        num_scalar_prefetch=5,
        grid=(count,),
        in_specs=[
            pl.BlockSpec(blk, lambda p, qi, qo, f, kt, mt: (qi[p], 0)),
            pl.BlockSpec(blk, lambda p, qi, qo, f, kt, mt: (qi[p], 0)),
            pl.BlockSpec(stat, lambda p, qi, qo, f, kt, mt: (0, 0, qi[p])),
            pl.BlockSpec(stat, lambda p, qi, qo, f, kt, mt: (0, 0, qi[p])),
            pl.BlockSpec(blk, lambda p, qi, qo, f, kt, mt: (kt[p], 0)),
            pl.BlockSpec(blk, lambda p, qi, qo, f, kt, mt: (kt[p], 0)),
        ],
        out_specs=[
            pl.BlockSpec(blk, lambda p, qi, qo, f, kt, mt: (qo[p], 0)),
            pl.BlockSpec(blk, lambda p, qi, qo, f, kt, mt: (p, 0)),
            pl.BlockSpec(blk, lambda p, qi, qo, f, kt, mt: (p, 0)),
        ],
    )
    return pl.pallas_call(
        list_kernel,
        grid_spec=grid_spec,
        out_shape=[
            jax.ShapeDtypeStruct((outs * height, features), jnp.float32),
            jax.ShapeDtypeStruct((count * height, features), jnp.float32),
            jax.ShapeDtypeStruct((count * height, features), jnp.float32),
        ],
    )(qin, qout, first, ktab, mtab, queries, out_grad, norm3, delta3, key_src, value_src)


def rand_pairs(ktab, mtab, arrived, key_rows, value_rows, heads):
    items, packed_rows, features = arrived.shape
    height = (packed_rows - STAT_ROWS) // 2
    grid_spec = pltpu.PrefetchScalarGridSpec(
        num_scalar_prefetch=2,
        grid=(items,),
        in_specs=[
            pl.BlockSpec((1, height, features), lambda p, kt, mt: (p, 0, 0)),
            pl.BlockSpec((1, height, features), lambda p, kt, mt: (p, 1, 0)),
            pl.BlockSpec(
                (1, STAT_ROWS, features), lambda p, kt, mt: (p, 2 * height // STAT_ROWS, 0)
            ),
            pl.BlockSpec((height, features), lambda p, kt, mt: (kt[p], 0)),
            pl.BlockSpec((height, features), lambda p, kt, mt: (kt[p], 0)),
        ],
        out_specs=[
            pl.BlockSpec((1, height, features), lambda p, kt, mt: (p, 0, 0)),
            pl.BlockSpec((1, height, features), lambda p, kt, mt: (p, 0, 0)),
            pl.BlockSpec((1, height, features), lambda p, kt, mt: (p, 0, 0)),
        ],
    )
    return pl.pallas_call(
        functools.partial(rand_kernel, heads),
        grid_spec=grid_spec,
        out_shape=[
            jax.ShapeDtypeStruct((items, height, features), jnp.bfloat16),
            jax.ShapeDtypeStruct((items, height, features), jnp.float32),
            jax.ShapeDtypeStruct((items, height, features), jnp.float32),
        ],
    )(ktab, mtab, arrived, arrived, arrived, key_rows, value_rows)


def shards(queries, key_rows, values, outputs, out_grad, log_norm, rand_blocks):
    ctx_size = lax.axis_size("ctx")
    my_index = lax.axis_index("ctx")
    row_count, features = queries.shape
    heads = log_norm.shape[0]
    slot_count = 2 * PAIR
    height = row_count // slot_count
    block_total = slot_count * ctx_size
    first_dev = my_index == 0
    last_dev = my_index == ctx_size - 1

    delta = jnp.sum(
        (out_grad.astype(jnp.float32) * outputs.astype(jnp.float32)).reshape(
            row_count, heads, features // heads
        ),
        axis=-1,
    )
    delta = jnp.transpose(delta).astype(jnp.bfloat16)
    norm3 = log_norm.astype(jnp.float32).reshape(heads, 1, row_count)
    delta3 = delta.astype(jnp.float32).reshape(heads, 1, row_count)

    def block(array, slot):
        return array[slot * height : (slot + 1) * height]

    from_left = shift(jnp.stack([block(key_rows, 1), block(values, 1)]), "ctx", 1)
    from_right = shift(jnp.stack([block(key_rows, 2), block(values, 2)]), "ctx", -1)
    global_kv = spread_2(jnp.stack([block(key_rows, 0), block(values, 0)]), "ctx", 0)
    key_win = jnp.concatenate([key_rows, from_left[0], from_right[0]])
    value_win = jnp.concatenate([values, from_left[1], from_right[1]])

    within = jnp.arange(slot_count, dtype=jnp.int32)
    seq_blk = jnp.where(
        within < PAIR, PAIR * my_index + within, block_total - 1 - PAIR * my_index - (within - PAIR)
    )
    last_prev = jnp.where(last_dev, 1, slot_count + 1).astype(jnp.int32)
    first_prev = jnp.where(first_dev, 0, 1).astype(jnp.int32)
    def table(*items):
        return jnp.stack([jnp.asarray(x, jnp.int32) for x in items])

    dq_own, dk_own, dv_own = list_pairs(
        table(0, 1, 1, 2, 2, 3), table(0, 1, 1, 2, 2, 3), table(1, 1, 0, 1, 0, 1),
        table(0, 1, 0, 2, 3, 3), table(2, 2, 1, 2, 1, 2), slot_count,
        queries, out_grad, norm3, delta3, key_rows, values,
    )
    dk_own = dk_own.reshape(6, height, features)
    dv_own = dv_own.reshape(6, height, features)
    dq_rim, dk_rim, dv_rim = list_pairs(
        table(0, slot_count - 1), table(0, 1), table(1, 1),
        table(slot_count, last_prev), table(first_prev, 1), 2,
        queries, out_grad, norm3, delta3, key_win, value_win,
    )
    dq_rim = dq_rim.reshape(2, height, features)
    dk_rim = dk_rim.reshape(2, height, features)
    dv_rim = dv_rim.reshape(2, height, features)
    to_left = jnp.stack([dk_rim[0], dv_rim[0]]).astype(jnp.bfloat16)
    to_right = jnp.stack([dk_rim[1], dv_rim[1]]).astype(jnp.bfloat16)
    back_right = shift(to_left, "ctx", -1)
    back_left = shift(to_right, "ctx", 1)

    ref_valid = rand_blocks >= 0
    in_front = rand_blocks < block_total // 2
    mirror = block_total - 1 - rand_blocks
    owner_dev = jnp.where(in_front, rand_blocks // PAIR, mirror // PAIR)
    owner_dev = jnp.where(ref_valid, owner_dev, ctx_size).reshape(-1)
    key_slot = jnp.where(in_front, rand_blocks % PAIR, PAIR + mirror % PAIR) + 1
    key_slot = jnp.where(ref_valid, key_slot, 0).reshape(-1)
    targets = jnp.arange(ctx_size, dtype=jnp.int32)
    matches = owner_dev[None, :] == targets[:, None]
    slot_send = jnp.sum(jnp.where(matches, key_slot[None, :], 0), axis=1)
    select = jnp.any(matches.reshape(ctx_size, slot_count, RANDOM), axis=2).astype(jnp.bfloat16)

    def per_slot_row(stat):
        return jnp.transpose(stat.reshape(heads, slot_count, height), (1, 0, 2)).reshape(
            slot_count, 1, features
        )

    packed = jnp.concatenate(
        [
            queries.reshape(slot_count, height, features),
            out_grad.reshape(slot_count, height, features),
            per_slot_row(log_norm),
            per_slot_row(delta),
            jnp.zeros((slot_count, STAT_ROWS - 2, features), jnp.bfloat16),
        ],
        axis=1,
    )
    pick = select > 0
    routed = jnp.sum(jnp.where(pick[:, :, None, None], packed[None], 0), axis=1).astype(
        jnp.bfloat16
    )
    row_id = lax.broadcasted_iota(jnp.int32, (1, packed.shape[1], 1), 1)
    routed = jnp.where(
        row_id == 2 * height + 2, slot_send.astype(jnp.bfloat16)[:, None, None], routed
    )
    arrived = lax.all_to_all(routed, "ctx", split_axis=0, concat_axis=0, tiled=True)
    slot_recv = arrived[:, 2 * height + 2, 0].astype(jnp.float32).astype(jnp.int32)
    ktab_r = jnp.maximum(slot_recv - 1, 0)
    mtab_r = (slot_recv > 0).astype(jnp.int32)
    dq_rand, dk_rand, dv_rand = rand_pairs(ktab_r, mtab_r, arrived, key_rows, values, heads)
    global_kv, dq_rand, dk_rand, dv_rand = lax.optimization_barrier(
        (global_kv, dq_rand, dk_rand, dv_rand)
    )
    glob_mode = (seq_blk >= WINDOW).astype(jnp.int32)
    dq_glob, dk_glob, dv_glob = list_pairs(
        table(0, 1, 2, 3), table(0, 1, 2, 3), table(1, 1, 1, 1), table(0, 0, 0, 0), glob_mode,
        slot_count, queries, out_grad, norm3, delta3, global_kv[0], global_kv[1],
    )
    part = jnp.stack(
        [
            jnp.sum(dk_glob.reshape(slot_count, height, features), axis=0),
            jnp.sum(dv_glob.reshape(slot_count, height, features), axis=0),
        ]
    )
    total = gather_to_root(part, "ctx")

    zero_blk = jnp.zeros((height, features), jnp.float32)
    dq_local = (
        dq_own + dq_glob
        + jnp.concatenate([dq_rim[0:1], zero_blk[None], zero_blk[None], dq_rim[1:2]]).reshape(
            row_count, features
        )
    )

    dq_rand, total, back_left, back_right = lax.optimization_barrier(
        (dq_rand, total, back_left, back_right)
    )
    back_left = back_left.astype(jnp.float32)
    back_right = back_right.astype(jnp.float32)
    returned = lax.all_to_all(dq_rand, "ctx", split_axis=0, concat_axis=0, tiled=True)
    select_f = select.astype(jnp.float32)
    rand_query = jnp.sum(
        select_f[:, :, None, None] * returned.astype(jnp.float32)[:, None], axis=0
    )
    choose = (slot_recv[:, None] == jnp.arange(1, slot_count + 1)[None, :]).astype(jnp.float32)
    rand_key = jnp.sum(choose[:, :, None, None] * dk_rand[:, None], axis=0)
    rand_value = jnp.sum(choose[:, :, None, None] * dv_rand[:, None], axis=0)

    own_tail = jnp.where(last_dev, 1.0, 0.0).astype(jnp.float32)

    owner_flag = jnp.where(first_dev, 1.0, 0.0).astype(jnp.float32)

    def assemble(own, rim, which, rand_part):
        slots = [
            own[0] + own[2] + total[which] * owner_flag,
            own[1] + rim[1] * own_tail + back_right[which],
            own[3] + back_left[which],
            own[5] + own[4],
        ]
        whole = jnp.stack(slots) + rand_part
        return whole.reshape(row_count, features).astype(jnp.bfloat16)

    query_total = (dq_local + rand_query.reshape(row_count, features)).astype(jnp.bfloat16)
    return (
        query_total,
        assemble(dk_own, dk_rim, 0, rand_key),
        assemble(dv_own, dv_rim, 1, rand_value),
    )


def solution(mesh):
    return jax.shard_map(
        shards,
        mesh=mesh,
        in_specs=(
            P("ctx", "head"),
            P("ctx", "head"),
            P("ctx", "head"),
            P("ctx", "head"),
            P("ctx", "head"),
            P("head", "ctx"),
            P("ctx", None),
        ),
        out_specs=(P("ctx", "head"), P("ctx", "head"), P("ctx", "head")),
        check_vma=False,
    )
```

```python
import functools

import jax
import jax.numpy as jnp
from jax import lax
from jax.experimental import pallas as pl
from jax.experimental.pallas import tpu as pltpu
from jax.sharding import PartitionSpec as P

PAIR = 2
WINDOW = 2
GLOBAL = 1
RANDOM = 3
STAT_ROWS = 16


RADIX = 4


def spread_2(array, axis, root):
    count = lax.axis_size(axis)
    mine = lax.axis_index(axis) == root
    array = jnp.where(mine, array, jnp.zeros_like(array))
    step = 1
    while step * RADIX < count:
        step *= RADIX
    while step >= 1:
        arrived = [
            lax.ppermute(array, axis, [(i, i + j * step) for i in range(0, count, RADIX * step) if i + j * step < count])
            for j in range(1, RADIX)
            if j * step < count
        ]
        for part in arrived:
            array = array + part
        step //= RADIX
    return array


def gather_to_root(array, axis):
    count = lax.axis_size(axis)
    step = 1
    while step < count:
        sent = array.astype(jnp.bfloat16)
        arrived = [
            lax.ppermute(sent, axis, [(i + j * step, i) for i in range(0, count, RADIX * step) if i + j * step < count])
            for j in range(1, RADIX)
            if j * step < count
        ]
        for part in arrived:
            array = array + part.astype(jnp.float32)
        step *= RADIX
    return array


def shift(array, axis, offset):
    count = lax.axis_size(axis)
    pairs = [(i, i + offset) for i in range(count) if 0 <= i + offset < count]
    return lax.ppermute(array, axis, pairs)


def pair_math(q, do, k, v, nrm, dlt, mode):
    scale = q.shape[-1] ** (-0.5)
    nt = (((1,), (1,)), ((), ()))
    s_t = lax.dot_general(k, q, nt, preferred_element_type=jnp.float32) * scale
    rows = lax.broadcasted_iota(jnp.int32, s_t.shape, 0)
    cols = lax.broadcasted_iota(jnp.int32, s_t.shape, 1)
    full = (mode == 1).astype(jnp.float32)
    causal = (mode == 2).astype(jnp.float32)
    visible = full + causal * (rows <= cols).astype(jnp.float32)
    p_t = jnp.exp(s_t - nrm) * visible
    dv = jnp.dot(p_t.astype(jnp.bfloat16), do, preferred_element_type=jnp.float32)
    dp_t = lax.dot_general(v, do, nt, preferred_element_type=jnp.float32)
    ds_t = (p_t * (dp_t - dlt)).astype(jnp.bfloat16)
    dk = jnp.dot(ds_t, q, preferred_element_type=jnp.float32) * scale
    ds = jnp.transpose(ds_t.astype(jnp.float32)).astype(jnp.bfloat16)
    dq = jnp.dot(ds, k, preferred_element_type=jnp.float32) * scale
    return dq, dk, dv


def list_kernel(qin, qout, first, ktab, mtab, q_ref, do_ref, nrm_ref, dlt_ref, k_ref, v_ref, dq_ref, dk_ref, dv_ref):
    p = pl.program_id(0)
    mode = mtab[p]
    lead = first[p]
    heads = nrm_ref.shape[0]
    width = q_ref.shape[1] // heads
    for h in range(heads):
        cols = slice(h * width, (h + 1) * width)
        dq, dk, dv = pair_math(
            q_ref[:, cols], do_ref[:, cols], k_ref[:, cols], v_ref[:, cols],
            nrm_ref[h], dlt_ref[h], mode,
        )

        @pl.when(lead == 1)
        def _():
            dq_ref[:, cols] = dq

        @pl.when(lead == 0)
        def _():
            dq_ref[:, cols] += dq

        dk_ref[:, cols] = dk
        dv_ref[:, cols] = dv


def rand_kernel(heads, ktab, mtab, q_ref, do_ref, st_ref, k_ref, v_ref, dq_ref, dk_ref, dv_ref):
    p = pl.program_id(0)
    mode = mtab[p]
    width = q_ref.shape[2] // heads

    @pl.when(mode == 0)
    def _():
        dq_ref[...] = jnp.zeros_like(dq_ref)
        dk_ref[...] = jnp.zeros_like(dk_ref)
        dv_ref[...] = jnp.zeros_like(dv_ref)

    @pl.when(mode > 0)
    def _():
        for h in range(heads):
            cols = slice(h * width, (h + 1) * width)
            stats = st_ref[0, :, cols].astype(jnp.float32)
            dq, dk, dv = pair_math(
                q_ref[0, :, cols], do_ref[0, :, cols], k_ref[:, cols], v_ref[:, cols],
                stats[0:1, :], stats[1:2, :], mode,
            )
            dq_ref[0, :, cols] = dq.astype(jnp.bfloat16)
            dk_ref[0, :, cols] = dk
            dv_ref[0, :, cols] = dv


def list_pairs(qin, qout, first, ktab, mtab, outs, queries, out_grad, norm3, delta3, key_src, value_src):
    rows, features = queries.shape
    heads = norm3.shape[0]
    height = rows // (2 * PAIR)
    count = ktab.shape[0]
    blk = (height, features)
    stat = (heads, 1, height)
    grid_spec = pltpu.PrefetchScalarGridSpec(
        num_scalar_prefetch=5,
        grid=(count,),
        in_specs=[
            pl.BlockSpec(blk, lambda p, qi, qo, f, kt, mt: (qi[p], 0)),
            pl.BlockSpec(blk, lambda p, qi, qo, f, kt, mt: (qi[p], 0)),
            pl.BlockSpec(stat, lambda p, qi, qo, f, kt, mt: (0, 0, qi[p])),
            pl.BlockSpec(stat, lambda p, qi, qo, f, kt, mt: (0, 0, qi[p])),
            pl.BlockSpec(blk, lambda p, qi, qo, f, kt, mt: (kt[p], 0)),
            pl.BlockSpec(blk, lambda p, qi, qo, f, kt, mt: (kt[p], 0)),
        ],
        out_specs=[
            pl.BlockSpec(blk, lambda p, qi, qo, f, kt, mt: (qo[p], 0)),
            pl.BlockSpec(blk, lambda p, qi, qo, f, kt, mt: (p, 0)),
            pl.BlockSpec(blk, lambda p, qi, qo, f, kt, mt: (p, 0)),
        ],
    )
    return pl.pallas_call(
        list_kernel,
        grid_spec=grid_spec,
        out_shape=[
            jax.ShapeDtypeStruct((outs * height, features), jnp.float32),
            jax.ShapeDtypeStruct((count * height, features), jnp.float32),
            jax.ShapeDtypeStruct((count * height, features), jnp.float32),
        ],
    )(qin, qout, first, ktab, mtab, queries, out_grad, norm3, delta3, key_src, value_src)


def rand_pairs(ktab, mtab, arrived, key_rows, value_rows, heads):
    items, packed_rows, features = arrived.shape
    height = (packed_rows - STAT_ROWS) // 2
    grid_spec = pltpu.PrefetchScalarGridSpec(
        num_scalar_prefetch=2,
        grid=(items,),
        in_specs=[
            pl.BlockSpec((1, height, features), lambda p, kt, mt: (p, 0, 0)),
            pl.BlockSpec((1, height, features), lambda p, kt, mt: (p, 1, 0)),
            pl.BlockSpec(
                (1, STAT_ROWS, features), lambda p, kt, mt: (p, 2 * height // STAT_ROWS, 0)
            ),
            pl.BlockSpec((height, features), lambda p, kt, mt: (kt[p], 0)),
            pl.BlockSpec((height, features), lambda p, kt, mt: (kt[p], 0)),
        ],
        out_specs=[
            pl.BlockSpec((1, height, features), lambda p, kt, mt: (p, 0, 0)),
            pl.BlockSpec((1, height, features), lambda p, kt, mt: (p, 0, 0)),
            pl.BlockSpec((1, height, features), lambda p, kt, mt: (p, 0, 0)),
        ],
    )
    return pl.pallas_call(
        functools.partial(rand_kernel, heads),
        grid_spec=grid_spec,
        out_shape=[
            jax.ShapeDtypeStruct((items, height, features), jnp.bfloat16),
            jax.ShapeDtypeStruct((items, height, features), jnp.float32),
            jax.ShapeDtypeStruct((items, height, features), jnp.float32),
        ],
    )(ktab, mtab, arrived, arrived, arrived, key_rows, value_rows)


def shards(queries, key_rows, values, outputs, out_grad, log_norm, rand_blocks):
    ctx_size = lax.axis_size("ctx")
    my_index = lax.axis_index("ctx")
    row_count, features = queries.shape
    heads = log_norm.shape[0]
    slot_count = 2 * PAIR
    height = row_count // slot_count
    block_total = slot_count * ctx_size
    first_dev = my_index == 0
    last_dev = my_index == ctx_size - 1

    delta = jnp.sum(
        (out_grad.astype(jnp.float32) * outputs.astype(jnp.float32)).reshape(
            row_count, heads, features // heads
        ),
        axis=-1,
    )
    delta = jnp.transpose(delta).astype(jnp.bfloat16)
    norm3 = log_norm.astype(jnp.float32).reshape(heads, 1, row_count)
    delta3 = delta.astype(jnp.float32).reshape(heads, 1, row_count)

    def block(array, slot):
        return array[slot * height : (slot + 1) * height]

    from_left = shift(jnp.stack([block(key_rows, 1), block(values, 1)]), "ctx", 1)
    from_right = shift(jnp.stack([block(key_rows, 2), block(values, 2)]), "ctx", -1)
    global_kv = spread_2(jnp.stack([block(key_rows, 0), block(values, 0)]), "ctx", 0)
    key_win = jnp.concatenate([key_rows, from_left[0], from_right[0]])
    value_win = jnp.concatenate([values, from_left[1], from_right[1]])

    within = jnp.arange(slot_count, dtype=jnp.int32)
    seq_blk = jnp.where(
        within < PAIR, PAIR * my_index + within, block_total - 1 - PAIR * my_index - (within - PAIR)
    )
    last_prev = jnp.where(last_dev, 1, slot_count + 1).astype(jnp.int32)
    first_prev = jnp.where(first_dev, 0, 1).astype(jnp.int32)
    def table(*items):
        return jnp.stack([jnp.asarray(x, jnp.int32) for x in items])

    dq_own, dk_own, dv_own = list_pairs(
        table(0, 1, 1, 2, 2, 3), table(0, 1, 1, 2, 2, 3), table(1, 1, 0, 1, 0, 1),
        table(0, 1, 0, 2, 3, 3), table(2, 2, 1, 2, 1, 2), slot_count,
        queries, out_grad, norm3, delta3, key_rows, values,
    )
    dk_own = dk_own.reshape(6, height, features)
    dv_own = dv_own.reshape(6, height, features)
    dq_rim, dk_rim, dv_rim = list_pairs(
        table(0, slot_count - 1), table(0, 1), table(1, 1),
        table(slot_count, last_prev), table(first_prev, 1), 2,
        queries, out_grad, norm3, delta3, key_win, value_win,
    )
    dq_rim = dq_rim.reshape(2, height, features)
    dk_rim = dk_rim.reshape(2, height, features)
    dv_rim = dv_rim.reshape(2, height, features)
    glob_mode = (seq_blk >= WINDOW).astype(jnp.int32)
    dq_glob, dk_glob, dv_glob = list_pairs(
        table(0, 1, 2, 3), table(0, 1, 2, 3), table(1, 1, 1, 1), table(0, 0, 0, 0), glob_mode,
        slot_count, queries, out_grad, norm3, delta3, global_kv[0], global_kv[1],
    )
    zero_blk = jnp.zeros((height, features), jnp.float32)
    dq_local = (
        dq_own + dq_glob
        + jnp.concatenate([dq_rim[0:1], zero_blk[None], zero_blk[None], dq_rim[1:2]]).reshape(
            row_count, features
        )
    )

    to_left = jnp.stack([dk_rim[0], dv_rim[0]]).astype(jnp.bfloat16)
    to_right = jnp.stack([dk_rim[1], dv_rim[1]]).astype(jnp.bfloat16)
    back_right = shift(to_left, "ctx", -1)
    back_left = shift(to_right, "ctx", 1)

    part = jnp.stack(
        [
            jnp.sum(dk_glob.reshape(slot_count, height, features), axis=0),
            jnp.sum(dv_glob.reshape(slot_count, height, features), axis=0),
        ]
    )
    total = gather_to_root(part, "ctx")

    ref_valid = rand_blocks >= 0
    in_front = rand_blocks < block_total // 2
    mirror = block_total - 1 - rand_blocks
    owner_dev = jnp.where(in_front, rand_blocks // PAIR, mirror // PAIR)
    owner_dev = jnp.where(ref_valid, owner_dev, ctx_size).reshape(-1)
    key_slot = jnp.where(in_front, rand_blocks % PAIR, PAIR + mirror % PAIR) + 1
    key_slot = jnp.where(ref_valid, key_slot, 0).reshape(-1)
    targets = jnp.arange(ctx_size, dtype=jnp.int32)
    matches = owner_dev[None, :] == targets[:, None]
    slot_send = jnp.sum(jnp.where(matches, key_slot[None, :], 0), axis=1)
    select = jnp.any(matches.reshape(ctx_size, slot_count, RANDOM), axis=2).astype(jnp.bfloat16)

    def per_slot_row(stat):
        return jnp.transpose(stat.reshape(heads, slot_count, height), (1, 0, 2)).reshape(
            slot_count, 1, features
        )

    packed = jnp.concatenate(
        [
            queries.reshape(slot_count, height, features),
            out_grad.reshape(slot_count, height, features),
            per_slot_row(log_norm),
            per_slot_row(delta),
            jnp.zeros((slot_count, STAT_ROWS - 2, features), jnp.bfloat16),
        ],
        axis=1,
    )
    pick = select > 0
    routed = jnp.sum(jnp.where(pick[:, :, None, None], packed[None], 0), axis=1).astype(
        jnp.bfloat16
    )
    row_id = lax.broadcasted_iota(jnp.int32, (1, packed.shape[1], 1), 1)
    routed = jnp.where(
        row_id == 2 * height + 2, slot_send.astype(jnp.bfloat16)[:, None, None], routed
    )
    arrived = lax.all_to_all(routed, "ctx", split_axis=0, concat_axis=0, tiled=True)
    slot_recv = arrived[:, 2 * height + 2, 0].astype(jnp.float32).astype(jnp.int32)
    ktab_r = jnp.maximum(slot_recv - 1, 0)
    mtab_r = (slot_recv > 0).astype(jnp.int32)
    dq_rand, dk_rand, dv_rand = rand_pairs(ktab_r, mtab_r, arrived, key_rows, values, heads)
    dq_rand, total, back_left, back_right = lax.optimization_barrier(
        (dq_rand, total, back_left, back_right)
    )
    back_left = back_left.astype(jnp.float32)
    back_right = back_right.astype(jnp.float32)
    returned = lax.all_to_all(dq_rand, "ctx", split_axis=0, concat_axis=0, tiled=True)
    select_f = select.astype(jnp.float32)
    rand_query = jnp.sum(
        select_f[:, :, None, None] * returned.astype(jnp.float32)[:, None], axis=0
    )
    choose = (slot_recv[:, None] == jnp.arange(1, slot_count + 1)[None, :]).astype(jnp.float32)
    rand_key = jnp.sum(choose[:, :, None, None] * dk_rand[:, None], axis=0)
    rand_value = jnp.sum(choose[:, :, None, None] * dv_rand[:, None], axis=0)

    own_tail = jnp.where(last_dev, 1.0, 0.0).astype(jnp.float32)

    owner_flag = jnp.where(first_dev, 1.0, 0.0).astype(jnp.float32)

    def assemble(own, rim, which, rand_part):
        slots = [
            own[0] + own[2] + total[which] * owner_flag,
            own[1] + rim[1] * own_tail + back_right[which],
            own[3] + back_left[which],
            own[5] + own[4],
        ]
        whole = jnp.stack(slots) + rand_part
        return whole.reshape(row_count, features).astype(jnp.bfloat16)

    query_total = (dq_local + rand_query.reshape(row_count, features)).astype(jnp.bfloat16)
    return (
        query_total,
        assemble(dk_own, dk_rim, 0, rand_key),
        assemble(dv_own, dv_rim, 1, rand_value),
    )


def solution(mesh):
    return jax.shard_map(
        shards,
        mesh=mesh,
        in_specs=(
            P("ctx", "head"),
            P("ctx", "head"),
            P("ctx", "head"),
            P("ctx", "head"),
            P("ctx", "head"),
            P("head", "ctx"),
            P("ctx", None),
        ),
        out_specs=(P("ctx", "head"), P("ctx", "head"), P("ctx", "head")),
        check_vma=False,
    )
```

```python
import functools

import jax
import jax.numpy as jnp
from jax import lax
from jax.experimental import pallas as pl
from jax.experimental.pallas import tpu as pltpu
from jax.sharding import PartitionSpec as P

PAIR = 2
WINDOW = 2
GLOBAL = 1
RANDOM = 3
STAT_ROWS = 16


RADIX = 4


def spread_2(array, axis, root):
    count = lax.axis_size(axis)
    mine = lax.axis_index(axis) == root
    array = jnp.where(mine, array, jnp.zeros_like(array))
    total = array
    for target in range(count):
        if target != root:
            total = total + lax.ppermute(array, axis, [(root, target)])
    return total


def gather_to_root(array, axis):
    count = lax.axis_size(axis)
    step = 1
    while step < count:
        sent = array.astype(jnp.bfloat16)
        arrived = [
            lax.ppermute(sent, axis, [(i + j * step, i) for i in range(0, count, RADIX * step) if i + j * step < count])
            for j in range(1, RADIX)
            if j * step < count
        ]
        for part in arrived:
            array = array + part.astype(jnp.float32)
        step *= RADIX
    return array


def shift(array, axis, offset):
    count = lax.axis_size(axis)
    pairs = [(i, i + offset) for i in range(count) if 0 <= i + offset < count]
    return lax.ppermute(array, axis, pairs)


def pair_math(q, do, k, v, nrm, dlt, mode):
    scale = q.shape[-1] ** (-0.5)
    nt = (((1,), (1,)), ((), ()))
    s_t = lax.dot_general(k, q, nt, preferred_element_type=jnp.float32) * scale
    rows = lax.broadcasted_iota(jnp.int32, s_t.shape, 0)
    cols = lax.broadcasted_iota(jnp.int32, s_t.shape, 1)
    full = (mode == 1).astype(jnp.float32)
    causal = (mode == 2).astype(jnp.float32)
    visible = full + causal * (rows <= cols).astype(jnp.float32)
    p_t = jnp.exp(s_t - nrm) * visible
    dv = jnp.dot(p_t.astype(jnp.bfloat16), do, preferred_element_type=jnp.float32)
    dp_t = lax.dot_general(v, do, nt, preferred_element_type=jnp.float32)
    ds_t = (p_t * (dp_t - dlt)).astype(jnp.bfloat16)
    dk = jnp.dot(ds_t, q, preferred_element_type=jnp.float32) * scale
    ds = jnp.transpose(ds_t.astype(jnp.float32)).astype(jnp.bfloat16)
    dq = jnp.dot(ds, k, preferred_element_type=jnp.float32) * scale
    return dq, dk, dv


def list_kernel(qin, qout, first, ktab, mtab, q_ref, do_ref, nrm_ref, dlt_ref, k_ref, v_ref, dq_ref, dk_ref, dv_ref):
    p = pl.program_id(0)
    mode = mtab[p]
    lead = first[p]
    heads = nrm_ref.shape[0]
    width = q_ref.shape[1] // heads
    for h in range(heads):
        cols = slice(h * width, (h + 1) * width)
        dq, dk, dv = pair_math(
            q_ref[:, cols], do_ref[:, cols], k_ref[:, cols], v_ref[:, cols],
            nrm_ref[h], dlt_ref[h], mode,
        )

        @pl.when(lead == 1)
        def _():
            dq_ref[:, cols] = dq

        @pl.when(lead == 0)
        def _():
            dq_ref[:, cols] += dq

        dk_ref[:, cols] = dk
        dv_ref[:, cols] = dv


def rand_kernel(heads, ktab, mtab, q_ref, do_ref, st_ref, k_ref, v_ref, dq_ref, dk_ref, dv_ref):
    p = pl.program_id(0)
    mode = mtab[p]
    width = q_ref.shape[2] // heads

    @pl.when(mode == 0)
    def _():
        dq_ref[...] = jnp.zeros_like(dq_ref)
        dk_ref[...] = jnp.zeros_like(dk_ref)
        dv_ref[...] = jnp.zeros_like(dv_ref)

    @pl.when(mode > 0)
    def _():
        for h in range(heads):
            cols = slice(h * width, (h + 1) * width)
            stats = st_ref[0, :, cols].astype(jnp.float32)
            dq, dk, dv = pair_math(
                q_ref[0, :, cols], do_ref[0, :, cols], k_ref[:, cols], v_ref[:, cols],
                stats[0:1, :], stats[1:2, :], mode,
            )
            dq_ref[0, :, cols] = dq.astype(jnp.bfloat16)
            dk_ref[0, :, cols] = dk
            dv_ref[0, :, cols] = dv


def list_pairs(qin, qout, first, ktab, mtab, outs, queries, out_grad, norm3, delta3, key_src, value_src):
    rows, features = queries.shape
    heads = norm3.shape[0]
    height = rows // (2 * PAIR)
    count = ktab.shape[0]
    blk = (height, features)
    stat = (heads, 1, height)
    grid_spec = pltpu.PrefetchScalarGridSpec(
        num_scalar_prefetch=5,
        grid=(count,),
        in_specs=[
            pl.BlockSpec(blk, lambda p, qi, qo, f, kt, mt: (qi[p], 0)),
            pl.BlockSpec(blk, lambda p, qi, qo, f, kt, mt: (qi[p], 0)),
            pl.BlockSpec(stat, lambda p, qi, qo, f, kt, mt: (0, 0, qi[p])),
            pl.BlockSpec(stat, lambda p, qi, qo, f, kt, mt: (0, 0, qi[p])),
            pl.BlockSpec(blk, lambda p, qi, qo, f, kt, mt: (kt[p], 0)),
            pl.BlockSpec(blk, lambda p, qi, qo, f, kt, mt: (kt[p], 0)),
        ],
        out_specs=[
            pl.BlockSpec(blk, lambda p, qi, qo, f, kt, mt: (qo[p], 0)),
            pl.BlockSpec(blk, lambda p, qi, qo, f, kt, mt: (p, 0)),
            pl.BlockSpec(blk, lambda p, qi, qo, f, kt, mt: (p, 0)),
        ],
    )
    return pl.pallas_call(
        list_kernel,
        grid_spec=grid_spec,
        out_shape=[
            jax.ShapeDtypeStruct((outs * height, features), jnp.float32),
            jax.ShapeDtypeStruct((count * height, features), jnp.float32),
            jax.ShapeDtypeStruct((count * height, features), jnp.float32),
        ],
    )(qin, qout, first, ktab, mtab, queries, out_grad, norm3, delta3, key_src, value_src)


def rand_pairs(ktab, mtab, arrived, key_rows, value_rows, heads):
    items, packed_rows, features = arrived.shape
    height = (packed_rows - STAT_ROWS) // 2
    grid_spec = pltpu.PrefetchScalarGridSpec(
        num_scalar_prefetch=2,
        grid=(items,),
        in_specs=[
            pl.BlockSpec((1, height, features), lambda p, kt, mt: (p, 0, 0)),
            pl.BlockSpec((1, height, features), lambda p, kt, mt: (p, 1, 0)),
            pl.BlockSpec(
                (1, STAT_ROWS, features), lambda p, kt, mt: (p, 2 * height // STAT_ROWS, 0)
            ),
            pl.BlockSpec((height, features), lambda p, kt, mt: (kt[p], 0)),
            pl.BlockSpec((height, features), lambda p, kt, mt: (kt[p], 0)),
        ],
        out_specs=[
            pl.BlockSpec((1, height, features), lambda p, kt, mt: (p, 0, 0)),
            pl.BlockSpec((1, height, features), lambda p, kt, mt: (p, 0, 0)),
            pl.BlockSpec((1, height, features), lambda p, kt, mt: (p, 0, 0)),
        ],
    )
    return pl.pallas_call(
        functools.partial(rand_kernel, heads),
        grid_spec=grid_spec,
        out_shape=[
            jax.ShapeDtypeStruct((items, height, features), jnp.bfloat16),
            jax.ShapeDtypeStruct((items, height, features), jnp.float32),
            jax.ShapeDtypeStruct((items, height, features), jnp.float32),
        ],
    )(ktab, mtab, arrived, arrived, arrived, key_rows, value_rows)


def shards(queries, key_rows, values, outputs, out_grad, log_norm, rand_blocks):
    ctx_size = lax.axis_size("ctx")
    my_index = lax.axis_index("ctx")
    row_count, features = queries.shape
    heads = log_norm.shape[0]
    slot_count = 2 * PAIR
    height = row_count // slot_count
    block_total = slot_count * ctx_size
    first_dev = my_index == 0
    last_dev = my_index == ctx_size - 1

    delta = jnp.sum(
        (out_grad.astype(jnp.float32) * outputs.astype(jnp.float32)).reshape(
            row_count, heads, features // heads
        ),
        axis=-1,
    )
    delta = jnp.transpose(delta).astype(jnp.bfloat16)
    norm3 = log_norm.astype(jnp.float32).reshape(heads, 1, row_count)
    delta3 = delta.astype(jnp.float32).reshape(heads, 1, row_count)

    def block(array, slot):
        return array[slot * height : (slot + 1) * height]

    from_left = shift(jnp.stack([block(key_rows, 1), block(values, 1)]), "ctx", 1)
    from_right = shift(jnp.stack([block(key_rows, 2), block(values, 2)]), "ctx", -1)
    global_kv = spread_2(jnp.stack([block(key_rows, 0), block(values, 0)]), "ctx", 0)
    key_win = jnp.concatenate([key_rows, from_left[0], from_right[0]])
    value_win = jnp.concatenate([values, from_left[1], from_right[1]])

    within = jnp.arange(slot_count, dtype=jnp.int32)
    seq_blk = jnp.where(
        within < PAIR, PAIR * my_index + within, block_total - 1 - PAIR * my_index - (within - PAIR)
    )
    last_prev = jnp.where(last_dev, 1, slot_count + 1).astype(jnp.int32)
    first_prev = jnp.where(first_dev, 0, 1).astype(jnp.int32)
    def table(*items):
        return jnp.stack([jnp.asarray(x, jnp.int32) for x in items])

    dq_own, dk_own, dv_own = list_pairs(
        table(0, 1, 1, 2, 2, 3), table(0, 1, 1, 2, 2, 3), table(1, 1, 0, 1, 0, 1),
        table(0, 1, 0, 2, 3, 3), table(2, 2, 1, 2, 1, 2), slot_count,
        queries, out_grad, norm3, delta3, key_rows, values,
    )
    dk_own = dk_own.reshape(6, height, features)
    dv_own = dv_own.reshape(6, height, features)
    dq_rim, dk_rim, dv_rim = list_pairs(
        table(0, slot_count - 1), table(0, 1), table(1, 1),
        table(slot_count, last_prev), table(first_prev, 1), 2,
        queries, out_grad, norm3, delta3, key_win, value_win,
    )
    dq_rim = dq_rim.reshape(2, height, features)
    dk_rim = dk_rim.reshape(2, height, features)
    dv_rim = dv_rim.reshape(2, height, features)
    glob_mode = (seq_blk >= WINDOW).astype(jnp.int32)
    dq_glob, dk_glob, dv_glob = list_pairs(
        table(0, 1, 2, 3), table(0, 1, 2, 3), table(1, 1, 1, 1), table(0, 0, 0, 0), glob_mode,
        slot_count, queries, out_grad, norm3, delta3, global_kv[0], global_kv[1],
    )
    zero_blk = jnp.zeros((height, features), jnp.float32)
    dq_local = (
        dq_own + dq_glob
        + jnp.concatenate([dq_rim[0:1], zero_blk[None], zero_blk[None], dq_rim[1:2]]).reshape(
            row_count, features
        )
    )

    to_left = jnp.stack([dk_rim[0], dv_rim[0]]).astype(jnp.bfloat16)
    to_right = jnp.stack([dk_rim[1], dv_rim[1]]).astype(jnp.bfloat16)
    back_right = shift(to_left, "ctx", -1)
    back_left = shift(to_right, "ctx", 1)

    part = jnp.stack(
        [
            jnp.sum(dk_glob.reshape(slot_count, height, features), axis=0),
            jnp.sum(dv_glob.reshape(slot_count, height, features), axis=0),
        ]
    )
    total = gather_to_root(part, "ctx")

    ref_valid = rand_blocks >= 0
    in_front = rand_blocks < block_total // 2
    mirror = block_total - 1 - rand_blocks
    owner_dev = jnp.where(in_front, rand_blocks // PAIR, mirror // PAIR)
    owner_dev = jnp.where(ref_valid, owner_dev, ctx_size).reshape(-1)
    key_slot = jnp.where(in_front, rand_blocks % PAIR, PAIR + mirror % PAIR) + 1
    key_slot = jnp.where(ref_valid, key_slot, 0).reshape(-1)
    targets = jnp.arange(ctx_size, dtype=jnp.int32)
    matches = owner_dev[None, :] == targets[:, None]
    slot_send = jnp.sum(jnp.where(matches, key_slot[None, :], 0), axis=1)
    select = jnp.any(matches.reshape(ctx_size, slot_count, RANDOM), axis=2).astype(jnp.bfloat16)

    def per_slot_row(stat):
        return jnp.transpose(stat.reshape(heads, slot_count, height), (1, 0, 2)).reshape(
            slot_count, 1, features
        )

    packed = jnp.concatenate(
        [
            queries.reshape(slot_count, height, features),
            out_grad.reshape(slot_count, height, features),
            per_slot_row(log_norm),
            per_slot_row(delta),
            jnp.zeros((slot_count, STAT_ROWS - 2, features), jnp.bfloat16),
        ],
        axis=1,
    )
    pick = select > 0
    routed = jnp.sum(jnp.where(pick[:, :, None, None], packed[None], 0), axis=1).astype(
        jnp.bfloat16
    )
    row_id = lax.broadcasted_iota(jnp.int32, (1, packed.shape[1], 1), 1)
    routed = jnp.where(
        row_id == 2 * height + 2, slot_send.astype(jnp.bfloat16)[:, None, None], routed
    )
    arrived = lax.all_to_all(routed, "ctx", split_axis=0, concat_axis=0, tiled=True)
    slot_recv = arrived[:, 2 * height + 2, 0].astype(jnp.float32).astype(jnp.int32)
    ktab_r = jnp.maximum(slot_recv - 1, 0)
    mtab_r = (slot_recv > 0).astype(jnp.int32)
    dq_rand, dk_rand, dv_rand = rand_pairs(ktab_r, mtab_r, arrived, key_rows, values, heads)
    dq_rand, total, back_left, back_right = lax.optimization_barrier(
        (dq_rand, total, back_left, back_right)
    )
    back_left = back_left.astype(jnp.float32)
    back_right = back_right.astype(jnp.float32)
    returned = lax.all_to_all(dq_rand, "ctx", split_axis=0, concat_axis=0, tiled=True)
    select_f = select.astype(jnp.float32)
    rand_query = jnp.sum(
        select_f[:, :, None, None] * returned.astype(jnp.float32)[:, None], axis=0
    )
    choose = (slot_recv[:, None] == jnp.arange(1, slot_count + 1)[None, :]).astype(jnp.float32)
    rand_key = jnp.sum(choose[:, :, None, None] * dk_rand[:, None], axis=0)
    rand_value = jnp.sum(choose[:, :, None, None] * dv_rand[:, None], axis=0)

    own_tail = jnp.where(last_dev, 1.0, 0.0).astype(jnp.float32)

    owner_flag = jnp.where(first_dev, 1.0, 0.0).astype(jnp.float32)

    def assemble(own, rim, which, rand_part):
        slots = [
            own[0] + own[2] + total[which] * owner_flag,
            own[1] + rim[1] * own_tail + back_right[which],
            own[3] + back_left[which],
            own[5] + own[4],
        ]
        whole = jnp.stack(slots) + rand_part
        return whole.reshape(row_count, features).astype(jnp.bfloat16)

    query_total = (dq_local + rand_query.reshape(row_count, features)).astype(jnp.bfloat16)
    return (
        query_total,
        assemble(dk_own, dk_rim, 0, rand_key),
        assemble(dv_own, dv_rim, 1, rand_value),
    )


def solution(mesh):
    return jax.shard_map(
        shards,
        mesh=mesh,
        in_specs=(
            P("ctx", "head"),
            P("ctx", "head"),
            P("ctx", "head"),
            P("ctx", "head"),
            P("ctx", "head"),
            P("head", "ctx"),
            P("ctx", None),
        ),
        out_specs=(P("ctx", "head"), P("ctx", "head"), P("ctx", "head")),
        check_vma=False,
    )
```

```python
import functools

import jax
import jax.numpy as jnp
from jax import lax
from jax.experimental import pallas as pl
from jax.experimental.pallas import tpu as pltpu
from jax.sharding import PartitionSpec as P

PAIR = 2
WINDOW = 2
GLOBAL = 1
RANDOM = 3
STAT_ROWS = 16


RADIX = 4


def spread_2(array, axis, root):
    count = lax.axis_size(axis)
    mine = lax.axis_index(axis) == root
    array = jnp.where(mine, array, jnp.zeros_like(array))
    step = 1
    while step * RADIX < count:
        step *= RADIX
    while step >= 1:
        arrived = [
            lax.ppermute(array, axis, [(i, i + j * step) for i in range(0, count, RADIX * step) if i + j * step < count])
            for j in range(1, RADIX)
            if j * step < count
        ]
        for part in arrived:
            array = array + part
        step //= RADIX
    return array


def gather_to_root(array, axis):
    count = lax.axis_size(axis)
    step = 1
    while step < count:
        sent = array.astype(jnp.bfloat16)
        arrived = [
            lax.ppermute(sent, axis, [(i + j * step, i) for i in range(0, count, RADIX * step) if i + j * step < count])
            for j in range(1, RADIX)
            if j * step < count
        ]
        for part in arrived:
            array = array + part.astype(jnp.float32)
        step *= RADIX
    return array


def shift(array, axis, offset):
    count = lax.axis_size(axis)
    pairs = [(i, i + offset) for i in range(count) if 0 <= i + offset < count]
    return lax.ppermute(array, axis, pairs)


def pair_math(q, do, k, v, nrm, dlt, mode):
    scale = q.shape[-1] ** (-0.5)
    nt = (((1,), (1,)), ((), ()))
    s_t = lax.dot_general(k, q, nt, preferred_element_type=jnp.float32) * scale
    rows = lax.broadcasted_iota(jnp.int32, s_t.shape, 0)
    cols = lax.broadcasted_iota(jnp.int32, s_t.shape, 1)
    full = (mode == 1).astype(jnp.float32)
    causal = (mode == 2).astype(jnp.float32)
    visible = full + causal * (rows <= cols).astype(jnp.float32)
    p_t = jnp.exp(s_t - nrm) * visible
    dv = jnp.dot(p_t.astype(jnp.bfloat16), do, preferred_element_type=jnp.float32)
    dp_t = lax.dot_general(v, do, nt, preferred_element_type=jnp.float32)
    ds_t = (p_t * (dp_t - dlt)).astype(jnp.bfloat16)
    dk = jnp.dot(ds_t, q, preferred_element_type=jnp.float32) * scale
    ds = jnp.transpose(ds_t.astype(jnp.float32)).astype(jnp.bfloat16)
    dq = jnp.dot(ds, k, preferred_element_type=jnp.float32) * scale
    return dq, dk, dv


def list_kernel(qin, qout, first, ktab, mtab, q_ref, do_ref, nrm_ref, dlt_ref, k_ref, v_ref, dq_ref, dk_ref, dv_ref):
    p = pl.program_id(0)
    mode = mtab[p]
    lead = first[p]
    heads = nrm_ref.shape[0]
    width = q_ref.shape[1] // heads
    for h in range(heads):
        cols = slice(h * width, (h + 1) * width)
        dq, dk, dv = pair_math(
            q_ref[:, cols], do_ref[:, cols], k_ref[:, cols], v_ref[:, cols],
            nrm_ref[h], dlt_ref[h], mode,
        )

        @pl.when(lead == 1)
        def _():
            dq_ref[:, cols] = dq

        @pl.when(lead == 0)
        def _():
            dq_ref[:, cols] += dq

        dk_ref[:, cols] = dk
        dv_ref[:, cols] = dv


def rand_kernel(heads, ktab, mtab, q_ref, do_ref, st_ref, k_ref, v_ref, dq_ref, dk_ref, dv_ref):
    p = pl.program_id(0)
    mode = mtab[p]
    width = q_ref.shape[2] // heads

    @pl.when(mode == 0)
    def _():
        dq_ref[...] = jnp.zeros_like(dq_ref)
        dk_ref[...] = jnp.zeros_like(dk_ref)
        dv_ref[...] = jnp.zeros_like(dv_ref)

    @pl.when(mode > 0)
    def _():
        for h in range(heads):
            cols = slice(h * width, (h + 1) * width)
            stats = st_ref[0, :, cols].astype(jnp.float32)
            dq, dk, dv = pair_math(
                q_ref[0, :, cols], do_ref[0, :, cols], k_ref[:, cols], v_ref[:, cols],
                stats[0:1, :], stats[1:2, :], mode,
            )
            dq_ref[0, :, cols] = dq.astype(jnp.bfloat16)
            dk_ref[0, :, cols] = dk
            dv_ref[0, :, cols] = dv


def list_pairs(qin, qout, first, ktab, mtab, outs, queries, out_grad, norm3, delta3, key_src, value_src):
    rows, features = queries.shape
    heads = norm3.shape[0]
    height = rows // (2 * PAIR)
    count = ktab.shape[0]
    blk = (height, features)
    stat = (heads, 1, height)
    grid_spec = pltpu.PrefetchScalarGridSpec(
        num_scalar_prefetch=5,
        grid=(count,),
        in_specs=[
            pl.BlockSpec(blk, lambda p, qi, qo, f, kt, mt: (qi[p], 0)),
            pl.BlockSpec(blk, lambda p, qi, qo, f, kt, mt: (qi[p], 0)),
            pl.BlockSpec(stat, lambda p, qi, qo, f, kt, mt: (0, 0, qi[p])),
            pl.BlockSpec(stat, lambda p, qi, qo, f, kt, mt: (0, 0, qi[p])),
            pl.BlockSpec(blk, lambda p, qi, qo, f, kt, mt: (kt[p], 0)),
            pl.BlockSpec(blk, lambda p, qi, qo, f, kt, mt: (kt[p], 0)),
        ],
        out_specs=[
            pl.BlockSpec(blk, lambda p, qi, qo, f, kt, mt: (qo[p], 0)),
            pl.BlockSpec(blk, lambda p, qi, qo, f, kt, mt: (p, 0)),
            pl.BlockSpec(blk, lambda p, qi, qo, f, kt, mt: (p, 0)),
        ],
    )
    return pl.pallas_call(
        list_kernel,
        grid_spec=grid_spec,
        out_shape=[
            jax.ShapeDtypeStruct((outs * height, features), jnp.float32),
            jax.ShapeDtypeStruct((count * height, features), jnp.float32),
            jax.ShapeDtypeStruct((count * height, features), jnp.float32),
        ],
    )(qin, qout, first, ktab, mtab, queries, out_grad, norm3, delta3, key_src, value_src)


def rand_pairs(ktab, mtab, arrived, key_rows, value_rows, heads):
    items, packed_rows, features = arrived.shape
    height = (packed_rows - STAT_ROWS) // 2
    grid_spec = pltpu.PrefetchScalarGridSpec(
        num_scalar_prefetch=2,
        grid=(items,),
        in_specs=[
            pl.BlockSpec((1, height, features), lambda p, kt, mt: (p, 0, 0)),
            pl.BlockSpec((1, height, features), lambda p, kt, mt: (p, 1, 0)),
            pl.BlockSpec(
                (1, STAT_ROWS, features), lambda p, kt, mt: (p, 2 * height // STAT_ROWS, 0)
            ),
            pl.BlockSpec((height, features), lambda p, kt, mt: (kt[p], 0)),
            pl.BlockSpec((height, features), lambda p, kt, mt: (kt[p], 0)),
        ],
        out_specs=[
            pl.BlockSpec((1, height, features), lambda p, kt, mt: (p, 0, 0)),
            pl.BlockSpec((1, height, features), lambda p, kt, mt: (p, 0, 0)),
            pl.BlockSpec((1, height, features), lambda p, kt, mt: (p, 0, 0)),
        ],
    )
    return pl.pallas_call(
        functools.partial(rand_kernel, heads),
        grid_spec=grid_spec,
        out_shape=[
            jax.ShapeDtypeStruct((items, height, features), jnp.bfloat16),
            jax.ShapeDtypeStruct((items, height, features), jnp.float32),
            jax.ShapeDtypeStruct((items, height, features), jnp.float32),
        ],
    )(ktab, mtab, arrived, arrived, arrived, key_rows, value_rows)


def shards(queries, key_rows, values, outputs, out_grad, log_norm, rand_blocks):
    ctx_size = lax.axis_size("ctx")
    my_index = lax.axis_index("ctx")
    row_count, features = queries.shape
    heads = log_norm.shape[0]
    slot_count = 2 * PAIR
    height = row_count // slot_count
    block_total = slot_count * ctx_size
    first_dev = my_index == 0
    last_dev = my_index == ctx_size - 1

    delta = jnp.sum(
        (out_grad.astype(jnp.float32) * outputs.astype(jnp.float32)).reshape(
            row_count, heads, features // heads
        ),
        axis=-1,
    )
    delta = jnp.transpose(delta).astype(jnp.bfloat16)
    norm3 = log_norm.astype(jnp.float32).reshape(heads, 1, row_count)
    delta3 = delta.astype(jnp.float32).reshape(heads, 1, row_count)

    def block(array, slot):
        return array[slot * height : (slot + 1) * height]

    from_left = shift(jnp.stack([block(key_rows, 1), block(values, 1)]), "ctx", 1)
    from_right = shift(jnp.stack([block(key_rows, 2), block(values, 2)]), "ctx", -1)
    global_kv = spread_2(jnp.stack([block(key_rows, 0), block(values, 0)]), "ctx", 0)
    key_win = jnp.concatenate([key_rows, from_left[0], from_right[0]])
    value_win = jnp.concatenate([values, from_left[1], from_right[1]])

    within = jnp.arange(slot_count, dtype=jnp.int32)
    seq_blk = jnp.where(
        within < PAIR, PAIR * my_index + within, block_total - 1 - PAIR * my_index - (within - PAIR)
    )
    last_prev = jnp.where(last_dev, 1, slot_count + 1).astype(jnp.int32)
    first_prev = jnp.where(first_dev, 0, 1).astype(jnp.int32)
    def table(*items):
        return jnp.stack([jnp.asarray(x, jnp.int32) for x in items])

    dq_own, dk_own, dv_own = list_pairs(
        table(0, 1, 1, 2, 2, 3), table(0, 1, 1, 2, 2, 3), table(1, 1, 0, 1, 0, 1),
        table(0, 1, 0, 2, 3, 3), table(2, 2, 1, 2, 1, 2), slot_count,
        queries, out_grad, norm3, delta3, key_rows, values,
    )
    dk_own = dk_own.reshape(6, height, features)
    dv_own = dv_own.reshape(6, height, features)
    dq_rim, dk_rim, dv_rim = list_pairs(
        table(0, slot_count - 1), table(0, 1), table(1, 1),
        table(slot_count, last_prev), table(first_prev, 1), 2,
        queries, out_grad, norm3, delta3, key_win, value_win,
    )
    dq_rim = dq_rim.reshape(2, height, features)
    dk_rim = dk_rim.reshape(2, height, features)
    dv_rim = dv_rim.reshape(2, height, features)
    glob_mode = (seq_blk >= WINDOW).astype(jnp.int32)
    dq_glob, dk_glob, dv_glob = list_pairs(
        table(0, 1, 2, 3), table(0, 1, 2, 3), table(1, 1, 1, 1), table(0, 0, 0, 0), glob_mode,
        slot_count, queries, out_grad, norm3, delta3, global_kv[0], global_kv[1],
    )
    zero_blk = jnp.zeros((height, features), jnp.float32)
    dq_local = (
        dq_own + dq_glob
        + jnp.concatenate([dq_rim[0:1], zero_blk[None], zero_blk[None], dq_rim[1:2]]).reshape(
            row_count, features
        )
    )

    to_left = jnp.stack([dk_rim[0], dv_rim[0]]).astype(jnp.bfloat16)
    to_right = jnp.stack([dk_rim[1], dv_rim[1]]).astype(jnp.bfloat16)
    back_right = shift(to_left, "ctx", -1)
    back_left = shift(to_right, "ctx", 1)

    part = jnp.stack(
        [
            jnp.sum(dk_glob.reshape(slot_count, height, features), axis=0),
            jnp.sum(dv_glob.reshape(slot_count, height, features), axis=0),
        ]
    )
    total = gather_to_root(part, "ctx")

    ref_valid = rand_blocks >= 0
    in_front = rand_blocks < block_total // 2
    mirror = block_total - 1 - rand_blocks
    owner_dev = jnp.where(in_front, rand_blocks // PAIR, mirror // PAIR)
    owner_dev = jnp.where(ref_valid, owner_dev, ctx_size).reshape(-1)
    key_slot = jnp.where(in_front, rand_blocks % PAIR, PAIR + mirror % PAIR) + 1
    key_slot = jnp.where(ref_valid, key_slot, 0).reshape(-1)
    targets = jnp.arange(ctx_size, dtype=jnp.int32)
    matches = owner_dev[None, :] == targets[:, None]
    slot_send = jnp.sum(jnp.where(matches, key_slot[None, :], 0), axis=1)
    select = jnp.any(matches.reshape(ctx_size, slot_count, RANDOM), axis=2).astype(jnp.bfloat16)

    def per_slot_row(stat):
        return jnp.transpose(stat.reshape(heads, slot_count, height), (1, 0, 2)).reshape(
            slot_count, 1, features
        )

    packed = jnp.concatenate(
        [
            queries.reshape(slot_count, height, features),
            out_grad.reshape(slot_count, height, features),
            per_slot_row(log_norm),
            per_slot_row(delta),
            jnp.zeros((slot_count, STAT_ROWS - 2, features), jnp.bfloat16),
        ],
        axis=1,
    )
    pick = select > 0
    row_id = lax.broadcasted_iota(jnp.int32, (1, packed.shape[1], 1), 1)
    routed = jnp.where(
        row_id == 2 * height + 2, slot_send.astype(jnp.bfloat16)[:, None, None], jnp.bfloat16(0)
    )
    for slot in range(slot_count):
        routed = routed + jnp.where(pick[:, slot, None, None], packed[slot][None], jnp.bfloat16(0))
    arrived = lax.all_to_all(routed, "ctx", split_axis=0, concat_axis=0, tiled=True)
    slot_recv = arrived[:, 2 * height + 2, 0].astype(jnp.float32).astype(jnp.int32)
    ktab_r = jnp.maximum(slot_recv - 1, 0)
    mtab_r = (slot_recv > 0).astype(jnp.int32)
    dq_rand, dk_rand, dv_rand = rand_pairs(ktab_r, mtab_r, arrived, key_rows, values, heads)
    dq_rand, total, back_left, back_right = lax.optimization_barrier(
        (dq_rand, total, back_left, back_right)
    )
    back_left = back_left.astype(jnp.float32)
    back_right = back_right.astype(jnp.float32)
    returned = lax.all_to_all(dq_rand, "ctx", split_axis=0, concat_axis=0, tiled=True)
    select_f = select.astype(jnp.float32)
    rand_query = jnp.sum(
        select_f[:, :, None, None] * returned.astype(jnp.float32)[:, None], axis=0
    )
    choose = (slot_recv[:, None] == jnp.arange(1, slot_count + 1)[None, :]).astype(jnp.float32)
    rand_key = jnp.sum(choose[:, :, None, None] * dk_rand[:, None], axis=0)
    rand_value = jnp.sum(choose[:, :, None, None] * dv_rand[:, None], axis=0)

    own_tail = jnp.where(last_dev, 1.0, 0.0).astype(jnp.float32)

    owner_flag = jnp.where(first_dev, 1.0, 0.0).astype(jnp.float32)

    def assemble(own, rim, which, rand_part):
        slots = [
            own[0] + own[2] + total[which] * owner_flag,
            own[1] + rim[1] * own_tail + back_right[which],
            own[3] + back_left[which],
            own[5] + own[4],
        ]
        whole = jnp.stack(slots) + rand_part
        return whole.reshape(row_count, features).astype(jnp.bfloat16)

    query_total = (dq_local + rand_query.reshape(row_count, features)).astype(jnp.bfloat16)
    return (
        query_total,
        assemble(dk_own, dk_rim, 0, rand_key),
        assemble(dv_own, dv_rim, 1, rand_value),
    )


def solution(mesh):
    return jax.shard_map(
        shards,
        mesh=mesh,
        in_specs=(
            P("ctx", "head"),
            P("ctx", "head"),
            P("ctx", "head"),
            P("ctx", "head"),
            P("ctx", "head"),
            P("head", "ctx"),
            P("ctx", None),
        ),
        out_specs=(P("ctx", "head"), P("ctx", "head"), P("ctx", "head")),
        check_vma=False,
    )
```

```python
import functools

import jax
import jax.numpy as jnp
from jax import lax
from jax.experimental import pallas as pl
from jax.experimental.pallas import tpu as pltpu
from jax.sharding import PartitionSpec as P

PAIR = 2
WINDOW = 2
GLOBAL = 1
RANDOM = 3
STAT_ROWS = 16


RADIX = 4


def spread_2(array, axis, root):
    count = lax.axis_size(axis)
    mine = lax.axis_index(axis) == root
    array = jnp.where(mine, array, jnp.zeros_like(array))
    step = 1
    while step * RADIX < count:
        step *= RADIX
    while step >= 1:
        arrived = [
            lax.ppermute(array, axis, [(i, i + j * step) for i in range(0, count, RADIX * step) if i + j * step < count])
            for j in range(1, RADIX)
            if j * step < count
        ]
        for part in arrived:
            array = array + part
        step //= RADIX
    return array


def gather_to_root(array, axis):
    count = lax.axis_size(axis)
    step = 1
    while step < count:
        sent = array.astype(jnp.bfloat16)
        arrived = [
            lax.ppermute(sent, axis, [(i + j * step, i) for i in range(0, count, RADIX * step) if i + j * step < count])
            for j in range(1, RADIX)
            if j * step < count
        ]
        for part in arrived:
            array = array + part.astype(jnp.float32)
        step *= RADIX
    return array


def shift(array, axis, offset):
    count = lax.axis_size(axis)
    pairs = [(i, i + offset) for i in range(count) if 0 <= i + offset < count]
    return lax.ppermute(array, axis, pairs)


def pair_math(q, do, k, v, nrm, dlt, mode):
    scale = q.shape[-1] ** (-0.5)
    nt = (((1,), (1,)), ((), ()))
    s_t = lax.dot_general(k, q, nt, preferred_element_type=jnp.float32) * scale
    rows = lax.broadcasted_iota(jnp.int32, s_t.shape, 0)
    cols = lax.broadcasted_iota(jnp.int32, s_t.shape, 1)
    full = (mode == 1).astype(jnp.float32)
    causal = (mode == 2).astype(jnp.float32)
    visible = full + causal * (rows <= cols).astype(jnp.float32)
    p_t = jnp.exp(s_t - nrm) * visible
    dv = jnp.dot(p_t.astype(jnp.bfloat16), do, preferred_element_type=jnp.float32)
    dp_t = lax.dot_general(v, do, nt, preferred_element_type=jnp.float32)
    ds_t = (p_t * (dp_t - dlt)).astype(jnp.bfloat16)
    dk = jnp.dot(ds_t, q, preferred_element_type=jnp.float32) * scale
    ds = jnp.transpose(ds_t.astype(jnp.float32)).astype(jnp.bfloat16)
    dq = jnp.dot(ds, k, preferred_element_type=jnp.float32) * scale
    return dq, dk, dv


def list_kernel(fold, qin, qout, first, ktab, mtab, q_ref, do_ref, nrm_ref, dlt_ref, k_ref, v_ref, dq_ref, dk_ref, dv_ref):
    p = pl.program_id(0)
    mode = mtab[p]
    lead = first[p]
    heads = nrm_ref.shape[0]
    width = q_ref.shape[1] // heads
    for h in range(heads):
        cols = slice(h * width, (h + 1) * width)
        dq, dk, dv = pair_math(
            q_ref[:, cols], do_ref[:, cols], k_ref[:, cols], v_ref[:, cols],
            nrm_ref[h], dlt_ref[h], mode,
        )

        @pl.when(lead == 1)
        def _():
            dq_ref[:, cols] = dq

        @pl.when(lead == 0)
        def _():
            dq_ref[:, cols] += dq

        if fold:
            @pl.when(p == 0)
            def _():
                dk_ref[:, cols] = dk
                dv_ref[:, cols] = dv

            @pl.when(p > 0)
            def _():
                dk_ref[:, cols] += dk
                dv_ref[:, cols] += dv
        else:
            dk_ref[:, cols] = dk
            dv_ref[:, cols] = dv


def rand_kernel(heads, ktab, mtab, q_ref, do_ref, st_ref, k_ref, v_ref, dq_ref, dk_ref, dv_ref):
    p = pl.program_id(0)
    mode = mtab[p]
    width = q_ref.shape[2] // heads

    @pl.when(mode == 0)
    def _():
        dq_ref[...] = jnp.zeros_like(dq_ref)
        dk_ref[...] = jnp.zeros_like(dk_ref)
        dv_ref[...] = jnp.zeros_like(dv_ref)

    @pl.when(mode > 0)
    def _():
        for h in range(heads):
            cols = slice(h * width, (h + 1) * width)
            stats = st_ref[0, :, cols].astype(jnp.float32)
            dq, dk, dv = pair_math(
                q_ref[0, :, cols], do_ref[0, :, cols], k_ref[:, cols], v_ref[:, cols],
                stats[0:1, :], stats[1:2, :], mode,
            )
            dq_ref[0, :, cols] = dq.astype(jnp.bfloat16)
            dk_ref[0, :, cols] = dk
            dv_ref[0, :, cols] = dv


def list_pairs(qin, qout, first, ktab, mtab, outs, queries, out_grad, norm3, delta3, key_src, value_src, fold=False):
    rows, features = queries.shape
    heads = norm3.shape[0]
    height = rows // (2 * PAIR)
    count = ktab.shape[0]
    blk = (height, features)
    stat = (heads, 1, height)
    grid_spec = pltpu.PrefetchScalarGridSpec(
        num_scalar_prefetch=5,
        grid=(count,),
        in_specs=[
            pl.BlockSpec(blk, lambda p, qi, qo, f, kt, mt: (qi[p], 0)),
            pl.BlockSpec(blk, lambda p, qi, qo, f, kt, mt: (qi[p], 0)),
            pl.BlockSpec(stat, lambda p, qi, qo, f, kt, mt: (0, 0, qi[p])),
            pl.BlockSpec(stat, lambda p, qi, qo, f, kt, mt: (0, 0, qi[p])),
            pl.BlockSpec(blk, lambda p, qi, qo, f, kt, mt: (kt[p], 0)),
            pl.BlockSpec(blk, lambda p, qi, qo, f, kt, mt: (kt[p], 0)),
        ],
        out_specs=[
            pl.BlockSpec(blk, lambda p, qi, qo, f, kt, mt: (qo[p], 0)),
            pl.BlockSpec(blk, lambda p, qi, qo, f, kt, mt: (0 if fold else p, 0)),
            pl.BlockSpec(blk, lambda p, qi, qo, f, kt, mt: (0 if fold else p, 0)),
        ],
    )
    return pl.pallas_call(
        functools.partial(list_kernel, fold),
        grid_spec=grid_spec,
        out_shape=[
            jax.ShapeDtypeStruct((outs * height, features), jnp.float32),
            jax.ShapeDtypeStruct(((1 if fold else count) * height, features), jnp.float32),
            jax.ShapeDtypeStruct(((1 if fold else count) * height, features), jnp.float32),
        ],
    )(qin, qout, first, ktab, mtab, queries, out_grad, norm3, delta3, key_src, value_src)


def rand_pairs(ktab, mtab, arrived, key_rows, value_rows, heads):
    items, packed_rows, features = arrived.shape
    height = (packed_rows - STAT_ROWS) // 2
    grid_spec = pltpu.PrefetchScalarGridSpec(
        num_scalar_prefetch=2,
        grid=(items,),
        in_specs=[
            pl.BlockSpec((1, height, features), lambda p, kt, mt: (p, 0, 0)),
            pl.BlockSpec((1, height, features), lambda p, kt, mt: (p, 1, 0)),
            pl.BlockSpec(
                (1, STAT_ROWS, features), lambda p, kt, mt: (p, 2 * height // STAT_ROWS, 0)
            ),
            pl.BlockSpec((height, features), lambda p, kt, mt: (kt[p], 0)),
            pl.BlockSpec((height, features), lambda p, kt, mt: (kt[p], 0)),
        ],
        out_specs=[
            pl.BlockSpec((1, height, features), lambda p, kt, mt: (p, 0, 0)),
            pl.BlockSpec((1, height, features), lambda p, kt, mt: (p, 0, 0)),
            pl.BlockSpec((1, height, features), lambda p, kt, mt: (p, 0, 0)),
        ],
    )
    return pl.pallas_call(
        functools.partial(rand_kernel, heads),
        grid_spec=grid_spec,
        out_shape=[
            jax.ShapeDtypeStruct((items, height, features), jnp.bfloat16),
            jax.ShapeDtypeStruct((items, height, features), jnp.float32),
            jax.ShapeDtypeStruct((items, height, features), jnp.float32),
        ],
    )(ktab, mtab, arrived, arrived, arrived, key_rows, value_rows)


def shards(queries, key_rows, values, outputs, out_grad, log_norm, rand_blocks):
    ctx_size = lax.axis_size("ctx")
    my_index = lax.axis_index("ctx")
    row_count, features = queries.shape
    heads = log_norm.shape[0]
    slot_count = 2 * PAIR
    height = row_count // slot_count
    block_total = slot_count * ctx_size
    first_dev = my_index == 0
    last_dev = my_index == ctx_size - 1

    delta = jnp.sum(
        (out_grad.astype(jnp.float32) * outputs.astype(jnp.float32)).reshape(
            row_count, heads, features // heads
        ),
        axis=-1,
    )
    delta = jnp.transpose(delta).astype(jnp.bfloat16)
    norm3 = log_norm.astype(jnp.float32).reshape(heads, 1, row_count)
    delta3 = delta.astype(jnp.float32).reshape(heads, 1, row_count)

    def block(array, slot):
        return array[slot * height : (slot + 1) * height]

    from_left = shift(jnp.stack([block(key_rows, 1), block(values, 1)]), "ctx", 1)
    from_right = shift(jnp.stack([block(key_rows, 2), block(values, 2)]), "ctx", -1)
    global_kv = spread_2(jnp.stack([block(key_rows, 0), block(values, 0)]), "ctx", 0)
    key_win = jnp.concatenate([key_rows, from_left[0], from_right[0]])
    value_win = jnp.concatenate([values, from_left[1], from_right[1]])

    within = jnp.arange(slot_count, dtype=jnp.int32)
    seq_blk = jnp.where(
        within < PAIR, PAIR * my_index + within, block_total - 1 - PAIR * my_index - (within - PAIR)
    )
    last_prev = jnp.where(last_dev, 1, slot_count + 1).astype(jnp.int32)
    first_prev = jnp.where(first_dev, 0, 1).astype(jnp.int32)
    def table(*items):
        return jnp.stack([jnp.asarray(x, jnp.int32) for x in items])

    dq_own, dk_own, dv_own = list_pairs(
        table(0, 1, 1, 2, 2, 3), table(0, 1, 1, 2, 2, 3), table(1, 1, 0, 1, 0, 1),
        table(0, 1, 0, 2, 3, 3), table(2, 2, 1, 2, 1, 2), slot_count,
        queries, out_grad, norm3, delta3, key_rows, values,
    )
    dk_own = dk_own.reshape(6, height, features)
    dv_own = dv_own.reshape(6, height, features)
    dq_rim, dk_rim, dv_rim = list_pairs(
        table(0, slot_count - 1), table(0, 1), table(1, 1),
        table(slot_count, last_prev), table(first_prev, 1), 2,
        queries, out_grad, norm3, delta3, key_win, value_win,
    )
    dq_rim = dq_rim.reshape(2, height, features)
    dk_rim = dk_rim.reshape(2, height, features)
    dv_rim = dv_rim.reshape(2, height, features)
    glob_mode = (seq_blk >= WINDOW).astype(jnp.int32)
    dq_glob, dk_glob, dv_glob = list_pairs(
        table(0, 1, 2, 3), table(0, 1, 2, 3), table(1, 1, 1, 1), table(0, 0, 0, 0), glob_mode,
        slot_count, queries, out_grad, norm3, delta3, global_kv[0], global_kv[1], fold=True,
    )
    zero_blk = jnp.zeros((height, features), jnp.float32)
    dq_local = (
        dq_own + dq_glob
        + jnp.concatenate([dq_rim[0:1], zero_blk[None], zero_blk[None], dq_rim[1:2]]).reshape(
            row_count, features
        )
    )

    to_left = jnp.stack([dk_rim[0], dv_rim[0]]).astype(jnp.bfloat16)
    to_right = jnp.stack([dk_rim[1], dv_rim[1]]).astype(jnp.bfloat16)
    back_right = shift(to_left, "ctx", -1)
    back_left = shift(to_right, "ctx", 1)

    part = jnp.stack([dk_glob, dv_glob])
    total = gather_to_root(part, "ctx")

    ref_valid = rand_blocks >= 0
    in_front = rand_blocks < block_total // 2
    mirror = block_total - 1 - rand_blocks
    owner_dev = jnp.where(in_front, rand_blocks // PAIR, mirror // PAIR)
    owner_dev = jnp.where(ref_valid, owner_dev, ctx_size).reshape(-1)
    key_slot = jnp.where(in_front, rand_blocks % PAIR, PAIR + mirror % PAIR) + 1
    key_slot = jnp.where(ref_valid, key_slot, 0).reshape(-1)
    targets = jnp.arange(ctx_size, dtype=jnp.int32)
    matches = owner_dev[None, :] == targets[:, None]
    slot_send = jnp.sum(jnp.where(matches, key_slot[None, :], 0), axis=1)
    select = jnp.any(matches.reshape(ctx_size, slot_count, RANDOM), axis=2).astype(jnp.bfloat16)

    def per_slot_row(stat):
        return jnp.transpose(stat.reshape(heads, slot_count, height), (1, 0, 2)).reshape(
            slot_count, 1, features
        )

    packed = jnp.concatenate(
        [
            queries.reshape(slot_count, height, features),
            out_grad.reshape(slot_count, height, features),
            per_slot_row(log_norm),
            per_slot_row(delta),
            jnp.zeros((slot_count, STAT_ROWS - 2, features), jnp.bfloat16),
        ],
        axis=1,
    )
    pick = select > 0
    row_id = lax.broadcasted_iota(jnp.int32, (1, packed.shape[1], 1), 1)
    routed = jnp.where(
        row_id == 2 * height + 2, slot_send.astype(jnp.bfloat16)[:, None, None], jnp.bfloat16(0)
    )
    for slot in range(slot_count):
        routed = routed + jnp.where(pick[:, slot, None, None], packed[slot][None], jnp.bfloat16(0))
    arrived = lax.all_to_all(routed, "ctx", split_axis=0, concat_axis=0, tiled=True)
    slot_recv = arrived[:, 2 * height + 2, 0].astype(jnp.float32).astype(jnp.int32)
    ktab_r = jnp.maximum(slot_recv - 1, 0)
    mtab_r = (slot_recv > 0).astype(jnp.int32)
    dq_rand, dk_rand, dv_rand = rand_pairs(ktab_r, mtab_r, arrived, key_rows, values, heads)
    dq_rand, total, back_left, back_right = lax.optimization_barrier(
        (dq_rand, total, back_left, back_right)
    )
    back_left = back_left.astype(jnp.float32)
    back_right = back_right.astype(jnp.float32)
    returned = lax.all_to_all(dq_rand, "ctx", split_axis=0, concat_axis=0, tiled=True)
    select_f = select.astype(jnp.float32)
    rand_query = jnp.sum(
        select_f[:, :, None, None] * returned.astype(jnp.float32)[:, None], axis=0
    )
    choose = (slot_recv[:, None] == jnp.arange(1, slot_count + 1)[None, :]).astype(jnp.float32)
    rand_key = jnp.sum(choose[:, :, None, None] * dk_rand[:, None], axis=0)
    rand_value = jnp.sum(choose[:, :, None, None] * dv_rand[:, None], axis=0)

    own_tail = jnp.where(last_dev, 1.0, 0.0).astype(jnp.float32)

    owner_flag = jnp.where(first_dev, 1.0, 0.0).astype(jnp.float32)

    def assemble(own, rim, which, rand_part):
        slots = [
            own[0] + own[2] + total[which] * owner_flag,
            own[1] + rim[1] * own_tail + back_right[which],
            own[3] + back_left[which],
            own[5] + own[4],
        ]
        whole = jnp.stack(slots) + rand_part
        return whole.reshape(row_count, features).astype(jnp.bfloat16)

    query_total = (dq_local + rand_query.reshape(row_count, features)).astype(jnp.bfloat16)
    return (
        query_total,
        assemble(dk_own, dk_rim, 0, rand_key),
        assemble(dv_own, dv_rim, 1, rand_value),
    )


def solution(mesh):
    return jax.shard_map(
        shards,
        mesh=mesh,
        in_specs=(
            P("ctx", "head"),
            P("ctx", "head"),
            P("ctx", "head"),
            P("ctx", "head"),
            P("ctx", "head"),
            P("head", "ctx"),
            P("ctx", None),
        ),
        out_specs=(P("ctx", "head"), P("ctx", "head"), P("ctx", "head")),
        check_vma=False,
    )
```

```python
import functools

import jax
import jax.numpy as jnp
from jax import lax
from jax.experimental import pallas as pl
from jax.experimental.pallas import tpu as pltpu
from jax.sharding import PartitionSpec as P

PAIR = 2
WINDOW = 2
GLOBAL = 1
RANDOM = 3
STAT_ROWS = 16


RADIX = 4


def spread_2(array, axis, root):
    count = lax.axis_size(axis)
    mine = lax.axis_index(axis) == root
    array = jnp.where(mine, array, jnp.zeros_like(array))
    step = 1
    while step * RADIX < count:
        step *= RADIX
    while step >= 1:
        arrived = [
            lax.ppermute(array, axis, [(i, i + j * step) for i in range(0, count, RADIX * step) if i + j * step < count])
            for j in range(1, RADIX)
            if j * step < count
        ]
        for part in arrived:
            array = array + part
        step //= RADIX
    return array


def gather_to_root(array, axis):
    count = lax.axis_size(axis)
    step = 1
    while step < count:
        sent = array.astype(jnp.bfloat16)
        arrived = [
            lax.ppermute(sent, axis, [(i + j * step, i) for i in range(0, count, RADIX * step) if i + j * step < count])
            for j in range(1, RADIX)
            if j * step < count
        ]
        for part in arrived:
            array = array + part.astype(jnp.float32)
        step *= RADIX
    return array


def shift(array, axis, offset):
    count = lax.axis_size(axis)
    pairs = [(i, i + offset) for i in range(count) if 0 <= i + offset < count]
    return lax.ppermute(array, axis, pairs)


def pair_math(q, do, k, v, nrm, dlt, mode):
    scale = q.shape[-1] ** (-0.5)
    nt = (((1,), (1,)), ((), ()))
    s_t = lax.dot_general(k, q, nt, preferred_element_type=jnp.float32) * scale
    rows = lax.broadcasted_iota(jnp.int32, s_t.shape, 0)
    cols = lax.broadcasted_iota(jnp.int32, s_t.shape, 1)
    full = (mode == 1).astype(jnp.float32)
    causal = (mode == 2).astype(jnp.float32)
    visible = full + causal * (rows <= cols).astype(jnp.float32)
    p_t = jnp.exp(s_t - nrm) * visible
    dv = jnp.dot(p_t.astype(jnp.bfloat16), do, preferred_element_type=jnp.float32)
    dp_t = lax.dot_general(v, do, nt, preferred_element_type=jnp.float32)
    ds_t = (p_t * (dp_t - dlt)).astype(jnp.bfloat16)
    dk = jnp.dot(ds_t, q, preferred_element_type=jnp.float32) * scale
    tn = (((0,), (0,)), ((), ()))
    dq = lax.dot_general(ds_t, k, tn, preferred_element_type=jnp.float32) * scale
    return dq, dk, dv


def list_kernel(qin, qout, first, ktab, mtab, q_ref, do_ref, nrm_ref, dlt_ref, k_ref, v_ref, dq_ref, dk_ref, dv_ref):
    p = pl.program_id(0)
    mode = mtab[p]
    lead = first[p]
    heads = nrm_ref.shape[0]
    width = q_ref.shape[1] // heads
    for h in range(heads):
        cols = slice(h * width, (h + 1) * width)
        dq, dk, dv = pair_math(
            q_ref[:, cols], do_ref[:, cols], k_ref[:, cols], v_ref[:, cols],
            nrm_ref[h], dlt_ref[h], mode,
        )

        @pl.when(lead == 1)
        def _():
            dq_ref[:, cols] = dq

        @pl.when(lead == 0)
        def _():
            dq_ref[:, cols] += dq

        dk_ref[:, cols] = dk
        dv_ref[:, cols] = dv


def rand_kernel(heads, ktab, mtab, q_ref, do_ref, st_ref, k_ref, v_ref, dq_ref, dk_ref, dv_ref):
    p = pl.program_id(0)
    mode = mtab[p]
    width = q_ref.shape[2] // heads

    @pl.when(mode == 0)
    def _():
        dq_ref[...] = jnp.zeros_like(dq_ref)
        dk_ref[...] = jnp.zeros_like(dk_ref)
        dv_ref[...] = jnp.zeros_like(dv_ref)

    @pl.when(mode > 0)
    def _():
        for h in range(heads):
            cols = slice(h * width, (h + 1) * width)
            stats = st_ref[0, :, cols].astype(jnp.float32)
            dq, dk, dv = pair_math(
                q_ref[0, :, cols], do_ref[0, :, cols], k_ref[:, cols], v_ref[:, cols],
                stats[0:1, :], stats[1:2, :], mode,
            )
            dq_ref[0, :, cols] = dq.astype(jnp.bfloat16)
            dk_ref[0, :, cols] = dk
            dv_ref[0, :, cols] = dv


def list_pairs(qin, qout, first, ktab, mtab, outs, queries, out_grad, norm3, delta3, key_src, value_src):
    rows, features = queries.shape
    heads = norm3.shape[0]
    height = rows // (2 * PAIR)
    count = ktab.shape[0]
    blk = (height, features)
    stat = (heads, 1, height)
    grid_spec = pltpu.PrefetchScalarGridSpec(
        num_scalar_prefetch=5,
        grid=(count,),
        in_specs=[
            pl.BlockSpec(blk, lambda p, qi, qo, f, kt, mt: (qi[p], 0)),
            pl.BlockSpec(blk, lambda p, qi, qo, f, kt, mt: (qi[p], 0)),
            pl.BlockSpec(stat, lambda p, qi, qo, f, kt, mt: (0, 0, qi[p])),
            pl.BlockSpec(stat, lambda p, qi, qo, f, kt, mt: (0, 0, qi[p])),
            pl.BlockSpec(blk, lambda p, qi, qo, f, kt, mt: (kt[p], 0)),
            pl.BlockSpec(blk, lambda p, qi, qo, f, kt, mt: (kt[p], 0)),
        ],
        out_specs=[
            pl.BlockSpec(blk, lambda p, qi, qo, f, kt, mt: (qo[p], 0)),
            pl.BlockSpec(blk, lambda p, qi, qo, f, kt, mt: (p, 0)),
            pl.BlockSpec(blk, lambda p, qi, qo, f, kt, mt: (p, 0)),
        ],
    )
    return pl.pallas_call(
        list_kernel,
        grid_spec=grid_spec,
        out_shape=[
            jax.ShapeDtypeStruct((outs * height, features), jnp.float32),
            jax.ShapeDtypeStruct((count * height, features), jnp.float32),
            jax.ShapeDtypeStruct((count * height, features), jnp.float32),
        ],
    )(qin, qout, first, ktab, mtab, queries, out_grad, norm3, delta3, key_src, value_src)


def rand_pairs(ktab, mtab, arrived, key_rows, value_rows, heads):
    items, packed_rows, features = arrived.shape
    height = (packed_rows - STAT_ROWS) // 2
    grid_spec = pltpu.PrefetchScalarGridSpec(
        num_scalar_prefetch=2,
        grid=(items,),
        in_specs=[
            pl.BlockSpec((1, height, features), lambda p, kt, mt: (p, 0, 0)),
            pl.BlockSpec((1, height, features), lambda p, kt, mt: (p, 1, 0)),
            pl.BlockSpec(
                (1, STAT_ROWS, features), lambda p, kt, mt: (p, 2 * height // STAT_ROWS, 0)
            ),
            pl.BlockSpec((height, features), lambda p, kt, mt: (kt[p], 0)),
            pl.BlockSpec((height, features), lambda p, kt, mt: (kt[p], 0)),
        ],
        out_specs=[
            pl.BlockSpec((1, height, features), lambda p, kt, mt: (p, 0, 0)),
            pl.BlockSpec((1, height, features), lambda p, kt, mt: (p, 0, 0)),
            pl.BlockSpec((1, height, features), lambda p, kt, mt: (p, 0, 0)),
        ],
    )
    return pl.pallas_call(
        functools.partial(rand_kernel, heads),
        grid_spec=grid_spec,
        out_shape=[
            jax.ShapeDtypeStruct((items, height, features), jnp.bfloat16),
            jax.ShapeDtypeStruct((items, height, features), jnp.float32),
            jax.ShapeDtypeStruct((items, height, features), jnp.float32),
        ],
    )(ktab, mtab, arrived, arrived, arrived, key_rows, value_rows)


def shards(queries, key_rows, values, outputs, out_grad, log_norm, rand_blocks):
    ctx_size = lax.axis_size("ctx")
    my_index = lax.axis_index("ctx")
    row_count, features = queries.shape
    heads = log_norm.shape[0]
    slot_count = 2 * PAIR
    height = row_count // slot_count
    block_total = slot_count * ctx_size
    first_dev = my_index == 0
    last_dev = my_index == ctx_size - 1

    delta = jnp.sum(
        (out_grad.astype(jnp.float32) * outputs.astype(jnp.float32)).reshape(
            row_count, heads, features // heads
        ),
        axis=-1,
    )
    delta = jnp.transpose(delta).astype(jnp.bfloat16)
    norm3 = log_norm.astype(jnp.float32).reshape(heads, 1, row_count)
    delta3 = delta.astype(jnp.float32).reshape(heads, 1, row_count)

    def block(array, slot):
        return array[slot * height : (slot + 1) * height]

    from_left = shift(jnp.stack([block(key_rows, 1), block(values, 1)]), "ctx", 1)
    from_right = shift(jnp.stack([block(key_rows, 2), block(values, 2)]), "ctx", -1)
    global_kv = spread_2(jnp.stack([block(key_rows, 0), block(values, 0)]), "ctx", 0)
    key_win = jnp.concatenate([key_rows, from_left[0], from_right[0]])
    value_win = jnp.concatenate([values, from_left[1], from_right[1]])

    within = jnp.arange(slot_count, dtype=jnp.int32)
    seq_blk = jnp.where(
        within < PAIR, PAIR * my_index + within, block_total - 1 - PAIR * my_index - (within - PAIR)
    )
    last_prev = jnp.where(last_dev, 1, slot_count + 1).astype(jnp.int32)
    first_prev = jnp.where(first_dev, 0, 1).astype(jnp.int32)
    def table(*items):
        return jnp.stack([jnp.asarray(x, jnp.int32) for x in items])

    dq_own, dk_own, dv_own = list_pairs(
        table(0, 1, 1, 2, 2, 3), table(0, 1, 1, 2, 2, 3), table(1, 1, 0, 1, 0, 1),
        table(0, 1, 0, 2, 3, 3), table(2, 2, 1, 2, 1, 2), slot_count,
        queries, out_grad, norm3, delta3, key_rows, values,
    )
    dk_own = dk_own.reshape(6, height, features)
    dv_own = dv_own.reshape(6, height, features)
    dq_rim, dk_rim, dv_rim = list_pairs(
        table(0, slot_count - 1), table(0, 1), table(1, 1),
        table(slot_count, last_prev), table(first_prev, 1), 2,
        queries, out_grad, norm3, delta3, key_win, value_win,
    )
    dq_rim = dq_rim.reshape(2, height, features)
    dk_rim = dk_rim.reshape(2, height, features)
    dv_rim = dv_rim.reshape(2, height, features)
    glob_mode = (seq_blk >= WINDOW).astype(jnp.int32)
    dq_glob, dk_glob, dv_glob = list_pairs(
        table(0, 1, 2, 3), table(0, 1, 2, 3), table(1, 1, 1, 1), table(0, 0, 0, 0), glob_mode,
        slot_count, queries, out_grad, norm3, delta3, global_kv[0], global_kv[1],
    )
    zero_blk = jnp.zeros((height, features), jnp.float32)
    dq_local = (
        dq_own + dq_glob
        + jnp.concatenate([dq_rim[0:1], zero_blk[None], zero_blk[None], dq_rim[1:2]]).reshape(
            row_count, features
        )
    )

    to_left = jnp.stack([dk_rim[0], dv_rim[0]]).astype(jnp.bfloat16)
    to_right = jnp.stack([dk_rim[1], dv_rim[1]]).astype(jnp.bfloat16)
    back_right = shift(to_left, "ctx", -1)
    back_left = shift(to_right, "ctx", 1)

    part = jnp.stack(
        [
            jnp.sum(dk_glob.reshape(slot_count, height, features), axis=0),
            jnp.sum(dv_glob.reshape(slot_count, height, features), axis=0),
        ]
    )
    total = gather_to_root(part, "ctx")

    ref_valid = rand_blocks >= 0
    in_front = rand_blocks < block_total // 2
    mirror = block_total - 1 - rand_blocks
    owner_dev = jnp.where(in_front, rand_blocks // PAIR, mirror // PAIR)
    owner_dev = jnp.where(ref_valid, owner_dev, ctx_size).reshape(-1)
    key_slot = jnp.where(in_front, rand_blocks % PAIR, PAIR + mirror % PAIR) + 1
    key_slot = jnp.where(ref_valid, key_slot, 0).reshape(-1)
    targets = jnp.arange(ctx_size, dtype=jnp.int32)
    matches = owner_dev[None, :] == targets[:, None]
    slot_send = jnp.sum(jnp.where(matches, key_slot[None, :], 0), axis=1)
    select = jnp.any(matches.reshape(ctx_size, slot_count, RANDOM), axis=2).astype(jnp.bfloat16)

    def per_slot_row(stat):
        return jnp.transpose(stat.reshape(heads, slot_count, height), (1, 0, 2)).reshape(
            slot_count, 1, features
        )

    packed = jnp.concatenate(
        [
            queries.reshape(slot_count, height, features),
            out_grad.reshape(slot_count, height, features),
            per_slot_row(log_norm),
            per_slot_row(delta),
            jnp.zeros((slot_count, STAT_ROWS - 2, features), jnp.bfloat16),
        ],
        axis=1,
    )
    pick = select > 0
    row_id = lax.broadcasted_iota(jnp.int32, (1, packed.shape[1], 1), 1)
    routed = jnp.where(
        row_id == 2 * height + 2, slot_send.astype(jnp.bfloat16)[:, None, None], jnp.bfloat16(0)
    )
    for slot in range(slot_count):
        routed = routed + jnp.where(pick[:, slot, None, None], packed[slot][None], jnp.bfloat16(0))
    arrived = lax.all_to_all(routed, "ctx", split_axis=0, concat_axis=0, tiled=True)
    slot_recv = arrived[:, 2 * height + 2, 0].astype(jnp.float32).astype(jnp.int32)
    ktab_r = jnp.maximum(slot_recv - 1, 0)
    mtab_r = (slot_recv > 0).astype(jnp.int32)
    dq_rand, dk_rand, dv_rand = rand_pairs(ktab_r, mtab_r, arrived, key_rows, values, heads)
    dq_rand, total, back_left, back_right = lax.optimization_barrier(
        (dq_rand, total, back_left, back_right)
    )
    back_left = back_left.astype(jnp.float32)
    back_right = back_right.astype(jnp.float32)
    returned = lax.all_to_all(dq_rand, "ctx", split_axis=0, concat_axis=0, tiled=True)
    select_f = select.astype(jnp.float32)
    rand_query = jnp.sum(
        select_f[:, :, None, None] * returned.astype(jnp.float32)[:, None], axis=0
    )
    choose = (slot_recv[:, None] == jnp.arange(1, slot_count + 1)[None, :]).astype(jnp.float32)
    rand_key = jnp.sum(choose[:, :, None, None] * dk_rand[:, None], axis=0)
    rand_value = jnp.sum(choose[:, :, None, None] * dv_rand[:, None], axis=0)

    own_tail = jnp.where(last_dev, 1.0, 0.0).astype(jnp.float32)

    owner_flag = jnp.where(first_dev, 1.0, 0.0).astype(jnp.float32)

    def assemble(own, rim, which, rand_part):
        slots = [
            own[0] + own[2] + total[which] * owner_flag,
            own[1] + rim[1] * own_tail + back_right[which],
            own[3] + back_left[which],
            own[5] + own[4],
        ]
        whole = jnp.stack(slots) + rand_part
        return whole.reshape(row_count, features).astype(jnp.bfloat16)

    query_total = (dq_local + rand_query.reshape(row_count, features)).astype(jnp.bfloat16)
    return (
        query_total,
        assemble(dk_own, dk_rim, 0, rand_key),
        assemble(dv_own, dv_rim, 1, rand_value),
    )


def solution(mesh):
    return jax.shard_map(
        shards,
        mesh=mesh,
        in_specs=(
            P("ctx", "head"),
            P("ctx", "head"),
            P("ctx", "head"),
            P("ctx", "head"),
            P("ctx", "head"),
            P("head", "ctx"),
            P("ctx", None),
        ),
        out_specs=(P("ctx", "head"), P("ctx", "head"), P("ctx", "head")),
        check_vma=False,
    )
```

```python
import functools

import jax
import jax.numpy as jnp
from jax import lax
from jax.experimental import pallas as pl
from jax.experimental.pallas import tpu as pltpu
from jax.sharding import PartitionSpec as P

PAIR = 2
WINDOW = 2
GLOBAL = 1
RANDOM = 3
STAT_ROWS = 16


RADIX = 4


def spread_2(array, axis, root):
    count = lax.axis_size(axis)
    mine = lax.axis_index(axis) == root
    array = jnp.where(mine, array, jnp.zeros_like(array))
    step = 1
    while step * RADIX < count:
        step *= RADIX
    while step >= 1:
        arrived = [
            lax.ppermute(array, axis, [(i, i + j * step) for i in range(0, count, RADIX * step) if i + j * step < count])
            for j in range(1, RADIX)
            if j * step < count
        ]
        for part in arrived:
            array = array + part
        step //= RADIX
    return array


def gather_to_root(array, axis):
    count = lax.axis_size(axis)
    step = 1
    while step < count:
        sent = array.astype(jnp.bfloat16)
        arrived = [
            lax.ppermute(sent, axis, [(i + j * step, i) for i in range(0, count, RADIX * step) if i + j * step < count])
            for j in range(1, RADIX)
            if j * step < count
        ]
        for part in arrived:
            array = array + part.astype(jnp.float32)
        step *= RADIX
    return array


def shift(array, axis, offset):
    count = lax.axis_size(axis)
    pairs = [(i, i + offset) for i in range(count) if 0 <= i + offset < count]
    return lax.ppermute(array, axis, pairs)


def pair_math(q, do, k, v, nrm, dlt, mode):
    scale = q.shape[-1] ** (-0.5)
    nt = (((1,), (1,)), ((), ()))
    s_t = lax.dot_general(k, q, nt, preferred_element_type=jnp.float32) * scale
    rows = lax.broadcasted_iota(jnp.int32, s_t.shape, 0)
    cols = lax.broadcasted_iota(jnp.int32, s_t.shape, 1)
    full = (mode == 1).astype(jnp.float32)
    causal = (mode == 2).astype(jnp.float32)
    visible = full + causal * (rows <= cols).astype(jnp.float32)
    p_t = jnp.exp(s_t - nrm) * visible
    dv = jnp.dot(p_t.astype(jnp.bfloat16), do, preferred_element_type=jnp.float32)
    dp_t = lax.dot_general(v, do, nt, preferred_element_type=jnp.float32)
    ds_t = (p_t * (dp_t - dlt)).astype(jnp.bfloat16)
    dk = jnp.dot(ds_t, q, preferred_element_type=jnp.float32) * scale
    tn = (((0,), (0,)), ((), ()))
    dq = lax.dot_general(ds_t, k, tn, preferred_element_type=jnp.float32) * scale
    return dq, dk, dv


def list_kernel(qin, qout, first, ktab, mtab, q_ref, do_ref, nrm_ref, dlt_ref, k_ref, v_ref, dq_ref, dk_ref, dv_ref):
    p = pl.program_id(0)
    mode = mtab[p]
    lead = first[p]
    heads = nrm_ref.shape[0]
    width = q_ref.shape[1] // heads
    for h in range(heads):
        cols = slice(h * width, (h + 1) * width)
        dq, dk, dv = pair_math(
            q_ref[:, cols], do_ref[:, cols], k_ref[:, cols], v_ref[:, cols],
            nrm_ref[h], dlt_ref[h], mode,
        )

        @pl.when(lead == 1)
        def _():
            dq_ref[:, cols] = dq

        @pl.when(lead == 0)
        def _():
            dq_ref[:, cols] += dq

        dk_ref[:, cols] = dk
        dv_ref[:, cols] = dv


def rand_kernel(heads, ktab, mtab, q_ref, do_ref, st_ref, k_ref, v_ref, dq_ref, dk_ref, dv_ref):
    p = pl.program_id(0)
    mode = mtab[p]
    width = q_ref.shape[2] // heads

    @pl.when(mode == 0)
    def _():
        dq_ref[...] = jnp.zeros_like(dq_ref)
        dk_ref[...] = jnp.zeros_like(dk_ref)
        dv_ref[...] = jnp.zeros_like(dv_ref)

    @pl.when(mode > 0)
    def _():
        for h in range(heads):
            cols = slice(h * width, (h + 1) * width)
            stats = st_ref[0, :, cols].astype(jnp.float32)
            dq, dk, dv = pair_math(
                q_ref[0, :, cols], do_ref[0, :, cols], k_ref[:, cols], v_ref[:, cols],
                stats[0:1, :], stats[1:2, :], mode,
            )
            dq_ref[0, :, cols] = dq.astype(jnp.bfloat16)
            dk_ref[0, :, cols] = dk.astype(jnp.bfloat16)
            dv_ref[0, :, cols] = dv.astype(jnp.bfloat16)


def list_pairs(qin, qout, first, ktab, mtab, outs, queries, out_grad, norm3, delta3, key_src, value_src):
    rows, features = queries.shape
    heads = norm3.shape[0]
    height = rows // (2 * PAIR)
    count = ktab.shape[0]
    blk = (height, features)
    stat = (heads, 1, height)
    grid_spec = pltpu.PrefetchScalarGridSpec(
        num_scalar_prefetch=5,
        grid=(count,),
        in_specs=[
            pl.BlockSpec(blk, lambda p, qi, qo, f, kt, mt: (qi[p], 0)),
            pl.BlockSpec(blk, lambda p, qi, qo, f, kt, mt: (qi[p], 0)),
            pl.BlockSpec(stat, lambda p, qi, qo, f, kt, mt: (0, 0, qi[p])),
            pl.BlockSpec(stat, lambda p, qi, qo, f, kt, mt: (0, 0, qi[p])),
            pl.BlockSpec(blk, lambda p, qi, qo, f, kt, mt: (kt[p], 0)),
            pl.BlockSpec(blk, lambda p, qi, qo, f, kt, mt: (kt[p], 0)),
        ],
        out_specs=[
            pl.BlockSpec(blk, lambda p, qi, qo, f, kt, mt: (qo[p], 0)),
            pl.BlockSpec(blk, lambda p, qi, qo, f, kt, mt: (p, 0)),
            pl.BlockSpec(blk, lambda p, qi, qo, f, kt, mt: (p, 0)),
        ],
    )
    return pl.pallas_call(
        list_kernel,
        grid_spec=grid_spec,
        out_shape=[
            jax.ShapeDtypeStruct((outs * height, features), jnp.float32),
            jax.ShapeDtypeStruct((count * height, features), jnp.float32),
            jax.ShapeDtypeStruct((count * height, features), jnp.float32),
        ],
    )(qin, qout, first, ktab, mtab, queries, out_grad, norm3, delta3, key_src, value_src)


def rand_pairs(ktab, mtab, arrived, key_rows, value_rows, heads):
    items, packed_rows, features = arrived.shape
    height = (packed_rows - STAT_ROWS) // 2
    grid_spec = pltpu.PrefetchScalarGridSpec(
        num_scalar_prefetch=2,
        grid=(items,),
        in_specs=[
            pl.BlockSpec((1, height, features), lambda p, kt, mt: (p, 0, 0)),
            pl.BlockSpec((1, height, features), lambda p, kt, mt: (p, 1, 0)),
            pl.BlockSpec(
                (1, STAT_ROWS, features), lambda p, kt, mt: (p, 2 * height // STAT_ROWS, 0)
            ),
            pl.BlockSpec((height, features), lambda p, kt, mt: (kt[p], 0)),
            pl.BlockSpec((height, features), lambda p, kt, mt: (kt[p], 0)),
        ],
        out_specs=[
            pl.BlockSpec((1, height, features), lambda p, kt, mt: (p, 0, 0)),
            pl.BlockSpec((1, height, features), lambda p, kt, mt: (p, 0, 0)),
            pl.BlockSpec((1, height, features), lambda p, kt, mt: (p, 0, 0)),
        ],
    )
    return pl.pallas_call(
        functools.partial(rand_kernel, heads),
        grid_spec=grid_spec,
        out_shape=[
            jax.ShapeDtypeStruct((items, height, features), jnp.bfloat16),
            jax.ShapeDtypeStruct((items, height, features), jnp.bfloat16),
            jax.ShapeDtypeStruct((items, height, features), jnp.bfloat16),
        ],
    )(ktab, mtab, arrived, arrived, arrived, key_rows, value_rows)


def shards(queries, key_rows, values, outputs, out_grad, log_norm, rand_blocks):
    ctx_size = lax.axis_size("ctx")
    my_index = lax.axis_index("ctx")
    row_count, features = queries.shape
    heads = log_norm.shape[0]
    slot_count = 2 * PAIR
    height = row_count // slot_count
    block_total = slot_count * ctx_size
    first_dev = my_index == 0
    last_dev = my_index == ctx_size - 1

    delta = jnp.sum(
        (out_grad.astype(jnp.float32) * outputs.astype(jnp.float32)).reshape(
            row_count, heads, features // heads
        ),
        axis=-1,
    )
    delta = jnp.transpose(delta).astype(jnp.bfloat16)
    norm3 = log_norm.astype(jnp.float32).reshape(heads, 1, row_count)
    delta3 = delta.astype(jnp.float32).reshape(heads, 1, row_count)

    def block(array, slot):
        return array[slot * height : (slot + 1) * height]

    from_left = shift(jnp.stack([block(key_rows, 1), block(values, 1)]), "ctx", 1)
    from_right = shift(jnp.stack([block(key_rows, 2), block(values, 2)]), "ctx", -1)
    global_kv = spread_2(jnp.stack([block(key_rows, 0), block(values, 0)]), "ctx", 0)
    key_win = jnp.concatenate([key_rows, from_left[0], from_right[0]])
    value_win = jnp.concatenate([values, from_left[1], from_right[1]])

    within = jnp.arange(slot_count, dtype=jnp.int32)
    seq_blk = jnp.where(
        within < PAIR, PAIR * my_index + within, block_total - 1 - PAIR * my_index - (within - PAIR)
    )
    last_prev = jnp.where(last_dev, 1, slot_count + 1).astype(jnp.int32)
    first_prev = jnp.where(first_dev, 0, 1).astype(jnp.int32)
    def table(*items):
        return jnp.stack([jnp.asarray(x, jnp.int32) for x in items])

    dq_own, dk_own, dv_own = list_pairs(
        table(0, 1, 1, 2, 2, 3), table(0, 1, 1, 2, 2, 3), table(1, 1, 0, 1, 0, 1),
        table(0, 1, 0, 2, 3, 3), table(2, 2, 1, 2, 1, 2), slot_count,
        queries, out_grad, norm3, delta3, key_rows, values,
    )
    dk_own = dk_own.reshape(6, height, features)
    dv_own = dv_own.reshape(6, height, features)
    dq_rim, dk_rim, dv_rim = list_pairs(
        table(0, slot_count - 1), table(0, 1), table(1, 1),
        table(slot_count, last_prev), table(first_prev, 1), 2,
        queries, out_grad, norm3, delta3, key_win, value_win,
    )
    dq_rim = dq_rim.reshape(2, height, features)
    dk_rim = dk_rim.reshape(2, height, features)
    dv_rim = dv_rim.reshape(2, height, features)
    glob_mode = (seq_blk >= WINDOW).astype(jnp.int32)
    dq_glob, dk_glob, dv_glob = list_pairs(
        table(0, 1, 2, 3), table(0, 1, 2, 3), table(1, 1, 1, 1), table(0, 0, 0, 0), glob_mode,
        slot_count, queries, out_grad, norm3, delta3, global_kv[0], global_kv[1],
    )
    zero_blk = jnp.zeros((height, features), jnp.float32)
    dq_local = (
        dq_own + dq_glob
        + jnp.concatenate([dq_rim[0:1], zero_blk[None], zero_blk[None], dq_rim[1:2]]).reshape(
            row_count, features
        )
    )

    to_left = jnp.stack([dk_rim[0], dv_rim[0]]).astype(jnp.bfloat16)
    to_right = jnp.stack([dk_rim[1], dv_rim[1]]).astype(jnp.bfloat16)
    back_right = shift(to_left, "ctx", -1)
    back_left = shift(to_right, "ctx", 1)

    part = jnp.stack(
        [
            jnp.sum(dk_glob.reshape(slot_count, height, features), axis=0),
            jnp.sum(dv_glob.reshape(slot_count, height, features), axis=0),
        ]
    )
    total = gather_to_root(part, "ctx")

    ref_valid = rand_blocks >= 0
    in_front = rand_blocks < block_total // 2
    mirror = block_total - 1 - rand_blocks
    owner_dev = jnp.where(in_front, rand_blocks // PAIR, mirror // PAIR)
    owner_dev = jnp.where(ref_valid, owner_dev, ctx_size).reshape(-1)
    key_slot = jnp.where(in_front, rand_blocks % PAIR, PAIR + mirror % PAIR) + 1
    key_slot = jnp.where(ref_valid, key_slot, 0).reshape(-1)
    targets = jnp.arange(ctx_size, dtype=jnp.int32)
    matches = owner_dev[None, :] == targets[:, None]
    slot_send = jnp.sum(jnp.where(matches, key_slot[None, :], 0), axis=1)
    select = jnp.any(matches.reshape(ctx_size, slot_count, RANDOM), axis=2).astype(jnp.bfloat16)

    def per_slot_row(stat):
        return jnp.transpose(stat.reshape(heads, slot_count, height), (1, 0, 2)).reshape(
            slot_count, 1, features
        )

    packed = jnp.concatenate(
        [
            queries.reshape(slot_count, height, features),
            out_grad.reshape(slot_count, height, features),
            per_slot_row(log_norm),
            per_slot_row(delta),
            jnp.zeros((slot_count, STAT_ROWS - 2, features), jnp.bfloat16),
        ],
        axis=1,
    )
    pick = select > 0
    row_id = lax.broadcasted_iota(jnp.int32, (1, packed.shape[1], 1), 1)
    routed = jnp.where(
        row_id == 2 * height + 2, slot_send.astype(jnp.bfloat16)[:, None, None], jnp.bfloat16(0)
    )
    for slot in range(slot_count):
        routed = routed + jnp.where(pick[:, slot, None, None], packed[slot][None], jnp.bfloat16(0))
    arrived = lax.all_to_all(routed, "ctx", split_axis=0, concat_axis=0, tiled=True)
    slot_recv = arrived[:, 2 * height + 2, 0].astype(jnp.float32).astype(jnp.int32)
    ktab_r = jnp.maximum(slot_recv - 1, 0)
    mtab_r = (slot_recv > 0).astype(jnp.int32)
    dq_rand, dk_rand, dv_rand = rand_pairs(ktab_r, mtab_r, arrived, key_rows, values, heads)
    dq_rand, total, back_left, back_right = lax.optimization_barrier(
        (dq_rand, total, back_left, back_right)
    )
    back_left = back_left.astype(jnp.float32)
    back_right = back_right.astype(jnp.float32)
    returned = lax.all_to_all(dq_rand, "ctx", split_axis=0, concat_axis=0, tiled=True)
    select_f = select.astype(jnp.float32)
    rand_query = jnp.sum(
        select_f[:, :, None, None] * returned.astype(jnp.float32)[:, None], axis=0
    )
    choose = (slot_recv[:, None] == jnp.arange(1, slot_count + 1)[None, :]).astype(jnp.float32)
    rand_key = jnp.sum(choose[:, :, None, None] * dk_rand.astype(jnp.float32)[:, None], axis=0)
    rand_value = jnp.sum(choose[:, :, None, None] * dv_rand.astype(jnp.float32)[:, None], axis=0)

    own_tail = jnp.where(last_dev, 1.0, 0.0).astype(jnp.float32)

    owner_flag = jnp.where(first_dev, 1.0, 0.0).astype(jnp.float32)

    def assemble(own, rim, which, rand_part):
        slots = [
            own[0] + own[2] + total[which] * owner_flag,
            own[1] + rim[1] * own_tail + back_right[which],
            own[3] + back_left[which],
            own[5] + own[4],
        ]
        whole = jnp.stack(slots) + rand_part
        return whole.reshape(row_count, features).astype(jnp.bfloat16)

    query_total = (dq_local + rand_query.reshape(row_count, features)).astype(jnp.bfloat16)
    return (
        query_total,
        assemble(dk_own, dk_rim, 0, rand_key),
        assemble(dv_own, dv_rim, 1, rand_value),
    )


def solution(mesh):
    return jax.shard_map(
        shards,
        mesh=mesh,
        in_specs=(
            P("ctx", "head"),
            P("ctx", "head"),
            P("ctx", "head"),
            P("ctx", "head"),
            P("ctx", "head"),
            P("head", "ctx"),
            P("ctx", None),
        ),
        out_specs=(P("ctx", "head"), P("ctx", "head"), P("ctx", "head")),
        check_vma=False,
    )
```

```python
import functools

import jax
import jax.numpy as jnp
from jax import lax
from jax.experimental import pallas as pl
from jax.experimental.pallas import tpu as pltpu
from jax.sharding import PartitionSpec as P

PAIR = 2
WINDOW = 2
GLOBAL = 1
RANDOM = 3
STAT_ROWS = 16


RADIX = 4


def spread_2(array, axis, root):
    count = lax.axis_size(axis)
    mine = lax.axis_index(axis) == root
    array = jnp.where(mine, array, jnp.zeros_like(array))
    step = 1
    while step * RADIX < count:
        step *= RADIX
    while step >= 1:
        arrived = [
            lax.ppermute(array, axis, [(i, i + j * step) for i in range(0, count, RADIX * step) if i + j * step < count])
            for j in range(1, RADIX)
            if j * step < count
        ]
        for part in arrived:
            array = array + part
        step //= RADIX
    return array


def gather_to_root(array, axis, tie):
    count = lax.axis_size(axis)
    step = 1
    while step < count:
        if step == RADIX:
            array, tie = lax.optimization_barrier((array, tie))
        sent = array.astype(jnp.bfloat16)
        arrived = [
            lax.ppermute(sent, axis, [(i + j * step, i) for i in range(0, count, RADIX * step) if i + j * step < count])
            for j in range(1, RADIX)
            if j * step < count
        ]
        for part in arrived:
            array = array + part.astype(jnp.float32)
        step *= RADIX
    return array, tie


def shift(array, axis, offset):
    count = lax.axis_size(axis)
    pairs = [(i, i + offset) for i in range(count) if 0 <= i + offset < count]
    return lax.ppermute(array, axis, pairs)


def pair_math(q, do, k, v, nrm, dlt, mode):
    scale = q.shape[-1] ** (-0.5)
    nt = (((1,), (1,)), ((), ()))
    s_t = lax.dot_general(k, q, nt, preferred_element_type=jnp.float32) * scale
    rows = lax.broadcasted_iota(jnp.int32, s_t.shape, 0)
    cols = lax.broadcasted_iota(jnp.int32, s_t.shape, 1)
    full = (mode == 1).astype(jnp.float32)
    causal = (mode == 2).astype(jnp.float32)
    visible = full + causal * (rows <= cols).astype(jnp.float32)
    p_t = jnp.exp(s_t - nrm) * visible
    dv = jnp.dot(p_t.astype(jnp.bfloat16), do, preferred_element_type=jnp.float32)
    dp_t = lax.dot_general(v, do, nt, preferred_element_type=jnp.float32)
    ds_t = (p_t * (dp_t - dlt)).astype(jnp.bfloat16)
    dk = jnp.dot(ds_t, q, preferred_element_type=jnp.float32) * scale
    tn = (((0,), (0,)), ((), ()))
    dq = lax.dot_general(ds_t, k, tn, preferred_element_type=jnp.float32) * scale
    return dq, dk, dv


def list_kernel(qin, qout, first, ktab, mtab, q_ref, do_ref, nrm_ref, dlt_ref, k_ref, v_ref, dq_ref, dk_ref, dv_ref):
    p = pl.program_id(0)
    mode = mtab[p]
    lead = first[p]
    heads = nrm_ref.shape[0]
    width = q_ref.shape[1] // heads
    for h in range(heads):
        cols = slice(h * width, (h + 1) * width)
        dq, dk, dv = pair_math(
            q_ref[:, cols], do_ref[:, cols], k_ref[:, cols], v_ref[:, cols],
            nrm_ref[h], dlt_ref[h], mode,
        )

        @pl.when(lead == 1)
        def _():
            dq_ref[:, cols] = dq

        @pl.when(lead == 0)
        def _():
            dq_ref[:, cols] += dq

        dk_ref[:, cols] = dk
        dv_ref[:, cols] = dv


def rand_kernel(heads, ktab, mtab, q_ref, do_ref, st_ref, k_ref, v_ref, dq_ref, dk_ref, dv_ref):
    p = pl.program_id(0)
    mode = mtab[p]
    width = q_ref.shape[2] // heads

    @pl.when(mode == 0)
    def _():
        dq_ref[...] = jnp.zeros_like(dq_ref)
        dk_ref[...] = jnp.zeros_like(dk_ref)
        dv_ref[...] = jnp.zeros_like(dv_ref)

    @pl.when(mode > 0)
    def _():
        for h in range(heads):
            cols = slice(h * width, (h + 1) * width)
            stats = st_ref[0, :, cols].astype(jnp.float32)
            dq, dk, dv = pair_math(
                q_ref[0, :, cols], do_ref[0, :, cols], k_ref[:, cols], v_ref[:, cols],
                stats[0:1, :], stats[1:2, :], mode,
            )
            dq_ref[0, :, cols] = dq.astype(jnp.bfloat16)
            dk_ref[0, :, cols] = dk
            dv_ref[0, :, cols] = dv


def list_pairs(qin, qout, first, ktab, mtab, outs, queries, out_grad, norm3, delta3, key_src, value_src):
    rows, features = queries.shape
    heads = norm3.shape[0]
    height = rows // (2 * PAIR)
    count = ktab.shape[0]
    blk = (height, features)
    stat = (heads, 1, height)
    grid_spec = pltpu.PrefetchScalarGridSpec(
        num_scalar_prefetch=5,
        grid=(count,),
        in_specs=[
            pl.BlockSpec(blk, lambda p, qi, qo, f, kt, mt: (qi[p], 0)),
            pl.BlockSpec(blk, lambda p, qi, qo, f, kt, mt: (qi[p], 0)),
            pl.BlockSpec(stat, lambda p, qi, qo, f, kt, mt: (0, 0, qi[p])),
            pl.BlockSpec(stat, lambda p, qi, qo, f, kt, mt: (0, 0, qi[p])),
            pl.BlockSpec(blk, lambda p, qi, qo, f, kt, mt: (kt[p], 0)),
            pl.BlockSpec(blk, lambda p, qi, qo, f, kt, mt: (kt[p], 0)),
        ],
        out_specs=[
            pl.BlockSpec(blk, lambda p, qi, qo, f, kt, mt: (qo[p], 0)),
            pl.BlockSpec(blk, lambda p, qi, qo, f, kt, mt: (p, 0)),
            pl.BlockSpec(blk, lambda p, qi, qo, f, kt, mt: (p, 0)),
        ],
    )
    return pl.pallas_call(
        list_kernel,
        grid_spec=grid_spec,
        out_shape=[
            jax.ShapeDtypeStruct((outs * height, features), jnp.float32),
            jax.ShapeDtypeStruct((count * height, features), jnp.float32),
            jax.ShapeDtypeStruct((count * height, features), jnp.float32),
        ],
    )(qin, qout, first, ktab, mtab, queries, out_grad, norm3, delta3, key_src, value_src)


def rand_pairs(ktab, mtab, arrived, key_rows, value_rows, heads):
    items, packed_rows, features = arrived.shape
    height = (packed_rows - STAT_ROWS) // 2
    grid_spec = pltpu.PrefetchScalarGridSpec(
        num_scalar_prefetch=2,
        grid=(items,),
        in_specs=[
            pl.BlockSpec((1, height, features), lambda p, kt, mt: (p, 0, 0)),
            pl.BlockSpec((1, height, features), lambda p, kt, mt: (p, 1, 0)),
            pl.BlockSpec(
                (1, STAT_ROWS, features), lambda p, kt, mt: (p, 2 * height // STAT_ROWS, 0)
            ),
            pl.BlockSpec((height, features), lambda p, kt, mt: (kt[p], 0)),
            pl.BlockSpec((height, features), lambda p, kt, mt: (kt[p], 0)),
        ],
        out_specs=[
            pl.BlockSpec((1, height, features), lambda p, kt, mt: (p, 0, 0)),
            pl.BlockSpec((1, height, features), lambda p, kt, mt: (p, 0, 0)),
            pl.BlockSpec((1, height, features), lambda p, kt, mt: (p, 0, 0)),
        ],
    )
    return pl.pallas_call(
        functools.partial(rand_kernel, heads),
        grid_spec=grid_spec,
        out_shape=[
            jax.ShapeDtypeStruct((items, height, features), jnp.bfloat16),
            jax.ShapeDtypeStruct((items, height, features), jnp.float32),
            jax.ShapeDtypeStruct((items, height, features), jnp.float32),
        ],
    )(ktab, mtab, arrived, arrived, arrived, key_rows, value_rows)


def shards(queries, key_rows, values, outputs, out_grad, log_norm, rand_blocks):
    ctx_size = lax.axis_size("ctx")
    my_index = lax.axis_index("ctx")
    row_count, features = queries.shape
    heads = log_norm.shape[0]
    slot_count = 2 * PAIR
    height = row_count // slot_count
    block_total = slot_count * ctx_size
    first_dev = my_index == 0
    last_dev = my_index == ctx_size - 1

    delta = jnp.sum(
        (out_grad.astype(jnp.float32) * outputs.astype(jnp.float32)).reshape(
            row_count, heads, features // heads
        ),
        axis=-1,
    )
    delta = jnp.transpose(delta).astype(jnp.bfloat16)
    norm3 = log_norm.astype(jnp.float32).reshape(heads, 1, row_count)
    delta3 = delta.astype(jnp.float32).reshape(heads, 1, row_count)

    def block(array, slot):
        return array[slot * height : (slot + 1) * height]

    from_left = shift(jnp.stack([block(key_rows, 1), block(values, 1)]), "ctx", 1)
    from_right = shift(jnp.stack([block(key_rows, 2), block(values, 2)]), "ctx", -1)
    global_kv = spread_2(jnp.stack([block(key_rows, 0), block(values, 0)]), "ctx", 0)
    key_win = jnp.concatenate([key_rows, from_left[0], from_right[0]])
    value_win = jnp.concatenate([values, from_left[1], from_right[1]])

    within = jnp.arange(slot_count, dtype=jnp.int32)
    seq_blk = jnp.where(
        within < PAIR, PAIR * my_index + within, block_total - 1 - PAIR * my_index - (within - PAIR)
    )
    last_prev = jnp.where(last_dev, 1, slot_count + 1).astype(jnp.int32)
    first_prev = jnp.where(first_dev, 0, 1).astype(jnp.int32)
    def table(*items):
        return jnp.stack([jnp.asarray(x, jnp.int32) for x in items])

    dq_own, dk_own, dv_own = list_pairs(
        table(0, 1, 1, 2, 2, 3), table(0, 1, 1, 2, 2, 3), table(1, 1, 0, 1, 0, 1),
        table(0, 1, 0, 2, 3, 3), table(2, 2, 1, 2, 1, 2), slot_count,
        queries, out_grad, norm3, delta3, key_rows, values,
    )
    dk_own = dk_own.reshape(6, height, features)
    dv_own = dv_own.reshape(6, height, features)
    dq_rim, dk_rim, dv_rim = list_pairs(
        table(0, slot_count - 1), table(0, 1), table(1, 1),
        table(slot_count, last_prev), table(first_prev, 1), 2,
        queries, out_grad, norm3, delta3, key_win, value_win,
    )
    dq_rim = dq_rim.reshape(2, height, features)
    dk_rim = dk_rim.reshape(2, height, features)
    dv_rim = dv_rim.reshape(2, height, features)
    to_left = jnp.stack([dk_rim[0], dv_rim[0]]).astype(jnp.bfloat16)
    to_right = jnp.stack([dk_rim[1], dv_rim[1]]).astype(jnp.bfloat16)
    back_right = shift(to_left, "ctx", -1)
    back_left = shift(to_right, "ctx", 1)

    ref_valid = rand_blocks >= 0
    in_front = rand_blocks < block_total // 2
    mirror = block_total - 1 - rand_blocks
    owner_dev = jnp.where(in_front, rand_blocks // PAIR, mirror // PAIR)
    owner_dev = jnp.where(ref_valid, owner_dev, ctx_size).reshape(-1)
    key_slot = jnp.where(in_front, rand_blocks % PAIR, PAIR + mirror % PAIR) + 1
    key_slot = jnp.where(ref_valid, key_slot, 0).reshape(-1)
    targets = jnp.arange(ctx_size, dtype=jnp.int32)
    matches = owner_dev[None, :] == targets[:, None]
    slot_send = jnp.sum(jnp.where(matches, key_slot[None, :], 0), axis=1)
    select = jnp.any(matches.reshape(ctx_size, slot_count, RANDOM), axis=2).astype(jnp.bfloat16)

    def per_slot_row(stat):
        return jnp.transpose(stat.reshape(heads, slot_count, height), (1, 0, 2)).reshape(
            slot_count, 1, features
        )

    packed = jnp.concatenate(
        [
            queries.reshape(slot_count, height, features),
            out_grad.reshape(slot_count, height, features),
            per_slot_row(log_norm),
            per_slot_row(delta),
            jnp.zeros((slot_count, STAT_ROWS - 2, features), jnp.bfloat16),
        ],
        axis=1,
    )
    pick = select > 0
    row_id = lax.broadcasted_iota(jnp.int32, (1, packed.shape[1], 1), 1)
    routed = jnp.where(
        row_id == 2 * height + 2, slot_send.astype(jnp.bfloat16)[:, None, None], jnp.bfloat16(0)
    )
    for slot in range(slot_count):
        routed = routed + jnp.where(pick[:, slot, None, None], packed[slot][None], jnp.bfloat16(0))
    arrived = lax.all_to_all(routed, "ctx", split_axis=0, concat_axis=0, tiled=True)
    slot_recv = arrived[:, 2 * height + 2, 0].astype(jnp.float32).astype(jnp.int32)
    ktab_r = jnp.maximum(slot_recv - 1, 0)
    mtab_r = (slot_recv > 0).astype(jnp.int32)
    dq_rand, dk_rand, dv_rand = rand_pairs(ktab_r, mtab_r, arrived, key_rows, values, heads)
    glob_mode = (seq_blk >= WINDOW).astype(jnp.int32)
    dq_glob, dk_glob, dv_glob = list_pairs(
        table(0, 1, 2, 3), table(0, 1, 2, 3), table(1, 1, 1, 1), table(0, 0, 0, 0), glob_mode,
        slot_count, queries, out_grad, norm3, delta3, global_kv[0], global_kv[1],
    )
    part = jnp.stack(
        [
            jnp.sum(dk_glob.reshape(slot_count, height, features), axis=0),
            jnp.sum(dv_glob.reshape(slot_count, height, features), axis=0),
        ]
    )
    total, (dq_rand, dk_rand, dv_rand) = gather_to_root(part, "ctx", (dq_rand, dk_rand, dv_rand))

    zero_blk = jnp.zeros((height, features), jnp.float32)
    dq_local = (
        dq_own + dq_glob
        + jnp.concatenate([dq_rim[0:1], zero_blk[None], zero_blk[None], dq_rim[1:2]]).reshape(
            row_count, features
        )
    )

    dq_rand, back_left, back_right = lax.optimization_barrier((dq_rand, back_left, back_right))
    back_left = back_left.astype(jnp.float32)
    back_right = back_right.astype(jnp.float32)
    returned = lax.all_to_all(dq_rand, "ctx", split_axis=0, concat_axis=0, tiled=True)
    select_f = select.astype(jnp.float32)
    rand_query = jnp.sum(
        select_f[:, :, None, None] * returned.astype(jnp.float32)[:, None], axis=0
    )
    choose = (slot_recv[:, None] == jnp.arange(1, slot_count + 1)[None, :]).astype(jnp.float32)
    rand_key = jnp.sum(choose[:, :, None, None] * dk_rand[:, None], axis=0)
    rand_value = jnp.sum(choose[:, :, None, None] * dv_rand[:, None], axis=0)

    own_tail = jnp.where(last_dev, 1.0, 0.0).astype(jnp.float32)

    owner_flag = jnp.where(first_dev, 1.0, 0.0).astype(jnp.float32)

    def assemble(own, rim, which, rand_part):
        slots = [
            own[0] + own[2] + total[which] * owner_flag,
            own[1] + rim[1] * own_tail + back_right[which],
            own[3] + back_left[which],
            own[5] + own[4],
        ]
        whole = jnp.stack(slots) + rand_part
        return whole.reshape(row_count, features).astype(jnp.bfloat16)

    query_total = (dq_local + rand_query.reshape(row_count, features)).astype(jnp.bfloat16)
    return (
        query_total,
        assemble(dk_own, dk_rim, 0, rand_key),
        assemble(dv_own, dv_rim, 1, rand_value),
    )


def solution(mesh):
    return jax.shard_map(
        shards,
        mesh=mesh,
        in_specs=(
            P("ctx", "head"),
            P("ctx", "head"),
            P("ctx", "head"),
            P("ctx", "head"),
            P("ctx", "head"),
            P("head", "ctx"),
            P("ctx", None),
        ),
        out_specs=(P("ctx", "head"), P("ctx", "head"), P("ctx", "head")),
        check_vma=False,
    )
```

```python
import functools

import jax
import jax.numpy as jnp
from jax import lax
from jax.experimental import pallas as pl
from jax.experimental.pallas import tpu as pltpu
from jax.sharding import PartitionSpec as P

PAIR = 2
WINDOW = 2
GLOBAL = 1
RANDOM = 3
STAT_ROWS = 16


RADIX = 8


def spread_2(array, axis, root):
    count = lax.axis_size(axis)
    mine = lax.axis_index(axis) == root
    array = jnp.where(mine, array, jnp.zeros_like(array))
    step = 1
    while step * RADIX < count:
        step *= RADIX
    while step >= 1:
        arrived = [
            lax.ppermute(array, axis, [(i, i + j * step) for i in range(0, count, RADIX * step) if i + j * step < count])
            for j in range(1, RADIX)
            if j * step < count
        ]
        for part in arrived:
            array = array + part
        step //= RADIX
    return array


def gather_to_root(array, axis):
    count = lax.axis_size(axis)
    step = 1
    while step < count:
        sent = array.astype(jnp.bfloat16)
        arrived = [
            lax.ppermute(sent, axis, [(i + j * step, i) for i in range(0, count, RADIX * step) if i + j * step < count])
            for j in range(1, RADIX)
            if j * step < count
        ]
        for part in arrived:
            array = array + part.astype(jnp.float32)
        step *= RADIX
    return array


def shift(array, axis, offset):
    count = lax.axis_size(axis)
    pairs = [(i, i + offset) for i in range(count) if 0 <= i + offset < count]
    return lax.ppermute(array, axis, pairs)


def pair_math(q, do, k, v, nrm, dlt, mode):
    scale = q.shape[-1] ** (-0.5)
    nt = (((1,), (1,)), ((), ()))
    s_t = lax.dot_general(k, q, nt, preferred_element_type=jnp.float32) * scale
    rows = lax.broadcasted_iota(jnp.int32, s_t.shape, 0)
    cols = lax.broadcasted_iota(jnp.int32, s_t.shape, 1)
    full = (mode == 1).astype(jnp.float32)
    causal = (mode == 2).astype(jnp.float32)
    visible = full + causal * (rows <= cols).astype(jnp.float32)
    p_t = jnp.exp(s_t - nrm) * visible
    dv = jnp.dot(p_t.astype(jnp.bfloat16), do, preferred_element_type=jnp.float32)
    dp_t = lax.dot_general(v, do, nt, preferred_element_type=jnp.float32)
    ds_t = (p_t * (dp_t - dlt)).astype(jnp.bfloat16)
    dk = jnp.dot(ds_t, q, preferred_element_type=jnp.float32) * scale
    tn = (((0,), (0,)), ((), ()))
    dq = lax.dot_general(ds_t, k, tn, preferred_element_type=jnp.float32) * scale
    return dq, dk, dv


def list_kernel(qin, qout, first, ktab, mtab, q_ref, do_ref, nrm_ref, dlt_ref, k_ref, v_ref, dq_ref, dk_ref, dv_ref):
    p = pl.program_id(0)
    mode = mtab[p]
    lead = first[p]
    heads = nrm_ref.shape[0]
    width = q_ref.shape[1] // heads
    for h in range(heads):
        cols = slice(h * width, (h + 1) * width)
        dq, dk, dv = pair_math(
            q_ref[:, cols], do_ref[:, cols], k_ref[:, cols], v_ref[:, cols],
            nrm_ref[h], dlt_ref[h], mode,
        )

        @pl.when(lead == 1)
        def _():
            dq_ref[:, cols] = dq

        @pl.when(lead == 0)
        def _():
            dq_ref[:, cols] += dq

        dk_ref[:, cols] = dk
        dv_ref[:, cols] = dv


def rand_kernel(heads, ktab, mtab, q_ref, do_ref, st_ref, k_ref, v_ref, dq_ref, dk_ref, dv_ref):
    p = pl.program_id(0)
    mode = mtab[p]
    width = q_ref.shape[2] // heads

    @pl.when(mode == 0)
    def _():
        dq_ref[...] = jnp.zeros_like(dq_ref)
        dk_ref[...] = jnp.zeros_like(dk_ref)
        dv_ref[...] = jnp.zeros_like(dv_ref)

    @pl.when(mode > 0)
    def _():
        for h in range(heads):
            cols = slice(h * width, (h + 1) * width)
            stats = st_ref[0, :, cols].astype(jnp.float32)
            dq, dk, dv = pair_math(
                q_ref[0, :, cols], do_ref[0, :, cols], k_ref[:, cols], v_ref[:, cols],
                stats[0:1, :], stats[1:2, :], mode,
            )
            dq_ref[0, :, cols] = dq.astype(jnp.bfloat16)
            dk_ref[0, :, cols] = dk
            dv_ref[0, :, cols] = dv


def list_pairs(qin, qout, first, ktab, mtab, outs, queries, out_grad, norm3, delta3, key_src, value_src):
    rows, features = queries.shape
    heads = norm3.shape[0]
    height = rows // (2 * PAIR)
    count = ktab.shape[0]
    blk = (height, features)
    stat = (heads, 1, height)
    grid_spec = pltpu.PrefetchScalarGridSpec(
        num_scalar_prefetch=5,
        grid=(count,),
        in_specs=[
            pl.BlockSpec(blk, lambda p, qi, qo, f, kt, mt: (qi[p], 0)),
            pl.BlockSpec(blk, lambda p, qi, qo, f, kt, mt: (qi[p], 0)),
            pl.BlockSpec(stat, lambda p, qi, qo, f, kt, mt: (0, 0, qi[p])),
            pl.BlockSpec(stat, lambda p, qi, qo, f, kt, mt: (0, 0, qi[p])),
            pl.BlockSpec(blk, lambda p, qi, qo, f, kt, mt: (kt[p], 0)),
            pl.BlockSpec(blk, lambda p, qi, qo, f, kt, mt: (kt[p], 0)),
        ],
        out_specs=[
            pl.BlockSpec(blk, lambda p, qi, qo, f, kt, mt: (qo[p], 0)),
            pl.BlockSpec(blk, lambda p, qi, qo, f, kt, mt: (p, 0)),
            pl.BlockSpec(blk, lambda p, qi, qo, f, kt, mt: (p, 0)),
        ],
    )
    return pl.pallas_call(
        list_kernel,
        grid_spec=grid_spec,
        out_shape=[
            jax.ShapeDtypeStruct((outs * height, features), jnp.float32),
            jax.ShapeDtypeStruct((count * height, features), jnp.float32),
            jax.ShapeDtypeStruct((count * height, features), jnp.float32),
        ],
    )(qin, qout, first, ktab, mtab, queries, out_grad, norm3, delta3, key_src, value_src)


def rand_pairs(ktab, mtab, arrived, key_rows, value_rows, heads):
    items, packed_rows, features = arrived.shape
    height = (packed_rows - STAT_ROWS) // 2
    grid_spec = pltpu.PrefetchScalarGridSpec(
        num_scalar_prefetch=2,
        grid=(items,),
        in_specs=[
            pl.BlockSpec((1, height, features), lambda p, kt, mt: (p, 0, 0)),
            pl.BlockSpec((1, height, features), lambda p, kt, mt: (p, 1, 0)),
            pl.BlockSpec(
                (1, STAT_ROWS, features), lambda p, kt, mt: (p, 2 * height // STAT_ROWS, 0)
            ),
            pl.BlockSpec((height, features), lambda p, kt, mt: (kt[p], 0)),
            pl.BlockSpec((height, features), lambda p, kt, mt: (kt[p], 0)),
        ],
        out_specs=[
            pl.BlockSpec((1, height, features), lambda p, kt, mt: (p, 0, 0)),
            pl.BlockSpec((1, height, features), lambda p, kt, mt: (p, 0, 0)),
            pl.BlockSpec((1, height, features), lambda p, kt, mt: (p, 0, 0)),
        ],
    )
    return pl.pallas_call(
        functools.partial(rand_kernel, heads),
        grid_spec=grid_spec,
        out_shape=[
            jax.ShapeDtypeStruct((items, height, features), jnp.bfloat16),
            jax.ShapeDtypeStruct((items, height, features), jnp.float32),
            jax.ShapeDtypeStruct((items, height, features), jnp.float32),
        ],
    )(ktab, mtab, arrived, arrived, arrived, key_rows, value_rows)


def shards(queries, key_rows, values, outputs, out_grad, log_norm, rand_blocks):
    ctx_size = lax.axis_size("ctx")
    my_index = lax.axis_index("ctx")
    row_count, features = queries.shape
    heads = log_norm.shape[0]
    slot_count = 2 * PAIR
    height = row_count // slot_count
    block_total = slot_count * ctx_size
    first_dev = my_index == 0
    last_dev = my_index == ctx_size - 1

    delta = jnp.sum(
        (out_grad.astype(jnp.float32) * outputs.astype(jnp.float32)).reshape(
            row_count, heads, features // heads
        ),
        axis=-1,
    )
    delta = jnp.transpose(delta).astype(jnp.bfloat16)
    norm3 = log_norm.astype(jnp.float32).reshape(heads, 1, row_count)
    delta3 = delta.astype(jnp.float32).reshape(heads, 1, row_count)

    def block(array, slot):
        return array[slot * height : (slot + 1) * height]

    from_left = shift(jnp.stack([block(key_rows, 1), block(values, 1)]), "ctx", 1)
    from_right = shift(jnp.stack([block(key_rows, 2), block(values, 2)]), "ctx", -1)
    global_kv = spread_2(jnp.stack([block(key_rows, 0), block(values, 0)]), "ctx", 0)
    key_win = jnp.concatenate([key_rows, from_left[0], from_right[0]])
    value_win = jnp.concatenate([values, from_left[1], from_right[1]])

    within = jnp.arange(slot_count, dtype=jnp.int32)
    seq_blk = jnp.where(
        within < PAIR, PAIR * my_index + within, block_total - 1 - PAIR * my_index - (within - PAIR)
    )
    last_prev = jnp.where(last_dev, 1, slot_count + 1).astype(jnp.int32)
    first_prev = jnp.where(first_dev, 0, 1).astype(jnp.int32)
    def table(*items):
        return jnp.stack([jnp.asarray(x, jnp.int32) for x in items])

    dq_own, dk_own, dv_own = list_pairs(
        table(0, 1, 1, 2, 2, 3), table(0, 1, 1, 2, 2, 3), table(1, 1, 0, 1, 0, 1),
        table(0, 1, 0, 2, 3, 3), table(2, 2, 1, 2, 1, 2), slot_count,
        queries, out_grad, norm3, delta3, key_rows, values,
    )
    dk_own = dk_own.reshape(6, height, features)
    dv_own = dv_own.reshape(6, height, features)
    dq_rim, dk_rim, dv_rim = list_pairs(
        table(0, slot_count - 1), table(0, 1), table(1, 1),
        table(slot_count, last_prev), table(first_prev, 1), 2,
        queries, out_grad, norm3, delta3, key_win, value_win,
    )
    dq_rim = dq_rim.reshape(2, height, features)
    dk_rim = dk_rim.reshape(2, height, features)
    dv_rim = dv_rim.reshape(2, height, features)
    glob_mode = (seq_blk >= WINDOW).astype(jnp.int32)
    dq_glob, dk_glob, dv_glob = list_pairs(
        table(0, 1, 2, 3), table(0, 1, 2, 3), table(1, 1, 1, 1), table(0, 0, 0, 0), glob_mode,
        slot_count, queries, out_grad, norm3, delta3, global_kv[0], global_kv[1],
    )
    zero_blk = jnp.zeros((height, features), jnp.float32)
    dq_local = (
        dq_own + dq_glob
        + jnp.concatenate([dq_rim[0:1], zero_blk[None], zero_blk[None], dq_rim[1:2]]).reshape(
            row_count, features
        )
    )

    to_left = jnp.stack([dk_rim[0], dv_rim[0]]).astype(jnp.bfloat16)
    to_right = jnp.stack([dk_rim[1], dv_rim[1]]).astype(jnp.bfloat16)
    back_right = shift(to_left, "ctx", -1)
    back_left = shift(to_right, "ctx", 1)

    part = jnp.stack(
        [
            jnp.sum(dk_glob.reshape(slot_count, height, features), axis=0),
            jnp.sum(dv_glob.reshape(slot_count, height, features), axis=0),
        ]
    )
    total = gather_to_root(part, "ctx")

    ref_valid = rand_blocks >= 0
    in_front = rand_blocks < block_total // 2
    mirror = block_total - 1 - rand_blocks
    owner_dev = jnp.where(in_front, rand_blocks // PAIR, mirror // PAIR)
    owner_dev = jnp.where(ref_valid, owner_dev, ctx_size).reshape(-1)
    key_slot = jnp.where(in_front, rand_blocks % PAIR, PAIR + mirror % PAIR) + 1
    key_slot = jnp.where(ref_valid, key_slot, 0).reshape(-1)
    targets = jnp.arange(ctx_size, dtype=jnp.int32)
    matches = owner_dev[None, :] == targets[:, None]
    slot_send = jnp.sum(jnp.where(matches, key_slot[None, :], 0), axis=1)
    select = jnp.any(matches.reshape(ctx_size, slot_count, RANDOM), axis=2).astype(jnp.bfloat16)

    def per_slot_row(stat):
        return jnp.transpose(stat.reshape(heads, slot_count, height), (1, 0, 2)).reshape(
            slot_count, 1, features
        )

    packed = jnp.concatenate(
        [
            queries.reshape(slot_count, height, features),
            out_grad.reshape(slot_count, height, features),
            per_slot_row(log_norm),
            per_slot_row(delta),
            jnp.zeros((slot_count, STAT_ROWS - 2, features), jnp.bfloat16),
        ],
        axis=1,
    )
    pick = select > 0
    row_id = lax.broadcasted_iota(jnp.int32, (1, packed.shape[1], 1), 1)
    routed = jnp.where(
        row_id == 2 * height + 2, slot_send.astype(jnp.bfloat16)[:, None, None], jnp.bfloat16(0)
    )
    for slot in range(slot_count):
        routed = routed + jnp.where(pick[:, slot, None, None], packed[slot][None], jnp.bfloat16(0))
    arrived = lax.all_to_all(routed, "ctx", split_axis=0, concat_axis=0, tiled=True)
    slot_recv = arrived[:, 2 * height + 2, 0].astype(jnp.float32).astype(jnp.int32)
    ktab_r = jnp.maximum(slot_recv - 1, 0)
    mtab_r = (slot_recv > 0).astype(jnp.int32)
    dq_rand, dk_rand, dv_rand = rand_pairs(ktab_r, mtab_r, arrived, key_rows, values, heads)
    dq_rand, total, back_left, back_right = lax.optimization_barrier(
        (dq_rand, total, back_left, back_right)
    )
    back_left = back_left.astype(jnp.float32)
    back_right = back_right.astype(jnp.float32)
    returned = lax.all_to_all(dq_rand, "ctx", split_axis=0, concat_axis=0, tiled=True)
    select_f = select.astype(jnp.float32)
    rand_query = jnp.sum(
        select_f[:, :, None, None] * returned.astype(jnp.float32)[:, None], axis=0
    )
    choose = (slot_recv[:, None] == jnp.arange(1, slot_count + 1)[None, :]).astype(jnp.float32)
    rand_key = jnp.sum(choose[:, :, None, None] * dk_rand[:, None], axis=0)
    rand_value = jnp.sum(choose[:, :, None, None] * dv_rand[:, None], axis=0)

    own_tail = jnp.where(last_dev, 1.0, 0.0).astype(jnp.float32)

    owner_flag = jnp.where(first_dev, 1.0, 0.0).astype(jnp.float32)

    def assemble(own, rim, which, rand_part):
        slots = [
            own[0] + own[2] + total[which] * owner_flag,
            own[1] + rim[1] * own_tail + back_right[which],
            own[3] + back_left[which],
            own[5] + own[4],
        ]
        whole = jnp.stack(slots) + rand_part
        return whole.reshape(row_count, features).astype(jnp.bfloat16)

    query_total = (dq_local + rand_query.reshape(row_count, features)).astype(jnp.bfloat16)
    return (
        query_total,
        assemble(dk_own, dk_rim, 0, rand_key),
        assemble(dv_own, dv_rim, 1, rand_value),
    )


def solution(mesh):
    return jax.shard_map(
        shards,
        mesh=mesh,
        in_specs=(
            P("ctx", "head"),
            P("ctx", "head"),
            P("ctx", "head"),
            P("ctx", "head"),
            P("ctx", "head"),
            P("head", "ctx"),
            P("ctx", None),
        ),
        out_specs=(P("ctx", "head"), P("ctx", "head"), P("ctx", "head")),
        check_vma=False,
    )
```

```python
import functools

import jax
import jax.numpy as jnp
from jax import lax
from jax.experimental import pallas as pl
from jax.experimental.pallas import tpu as pltpu
from jax.sharding import PartitionSpec as P

PAIR = 2
WINDOW = 2
GLOBAL = 1
RANDOM = 3
STAT_ROWS = 16


RADIX = 4


def spread_2(array, axis, root):
    count = lax.axis_size(axis)
    mine = lax.axis_index(axis) == root
    array = jnp.where(mine, array, jnp.zeros_like(array))
    step = 1
    while step * RADIX < count:
        step *= RADIX
    while step >= 1:
        arrived = [
            lax.ppermute(array, axis, [(i, i + j * step) for i in range(0, count, RADIX * step) if i + j * step < count])
            for j in range(1, RADIX)
            if j * step < count
        ]
        for part in arrived:
            array = array + part
        step //= RADIX
    return array


def gather_to_root(array, axis):
    count = lax.axis_size(axis)
    step = 1
    while step < count:
        sent = array.astype(jnp.bfloat16)
        arrived = [
            lax.ppermute(sent, axis, [(i + j * step, i) for i in range(0, count, RADIX * step) if i + j * step < count])
            for j in range(1, RADIX)
            if j * step < count
        ]
        for part in arrived:
            array = array + part.astype(jnp.float32)
        step *= RADIX
    return array


def shift(array, axis, offset):
    count = lax.axis_size(axis)
    pairs = [(i, i + offset) for i in range(count) if 0 <= i + offset < count]
    return lax.ppermute(array, axis, pairs)


def pair_math(q, do, k, v, nrm, dlt, mode):
    scale = q.shape[-1] ** (-0.5)
    nt = (((1,), (1,)), ((), ()))
    s_t = lax.dot_general(k, q, nt, preferred_element_type=jnp.float32) * scale
    rows = lax.broadcasted_iota(jnp.int32, s_t.shape, 0)
    cols = lax.broadcasted_iota(jnp.int32, s_t.shape, 1)
    full = (mode == 1).astype(jnp.float32)
    causal = (mode == 2).astype(jnp.float32)
    visible = full + causal * (rows <= cols).astype(jnp.float32)
    p_t = jnp.exp(s_t - nrm) * visible
    dv = jnp.dot(p_t.astype(jnp.bfloat16), do, preferred_element_type=jnp.float32)
    dp_t = lax.dot_general(v, do, nt, preferred_element_type=jnp.float32)
    ds_t = (p_t * (dp_t - dlt)).astype(jnp.bfloat16)
    dk = jnp.dot(ds_t, q, preferred_element_type=jnp.float32) * scale
    tn = (((0,), (0,)), ((), ()))
    dq = lax.dot_general(ds_t, k, tn, preferred_element_type=jnp.float32) * scale
    return dq, dk, dv


def list_kernel(qin, qout, first, ktab, mtab, q_ref, do_ref, nrm_ref, dlt_ref, k_ref, v_ref, dq_ref, dk_ref, dv_ref):
    p = pl.program_id(0)
    mode = mtab[p]
    lead = first[p]
    heads = nrm_ref.shape[0]
    width = q_ref.shape[1] // heads
    for h in range(heads):
        cols = slice(h * width, (h + 1) * width)
        dq, dk, dv = pair_math(
            q_ref[:, cols], do_ref[:, cols], k_ref[:, cols], v_ref[:, cols],
            nrm_ref[h], dlt_ref[h], mode,
        )

        @pl.when(lead == 1)
        def _():
            dq_ref[:, cols] = dq

        @pl.when(lead == 0)
        def _():
            dq_ref[:, cols] += dq

        dk_ref[:, cols] = dk
        dv_ref[:, cols] = dv


def rand_kernel(heads, ftab, ktab, mtab, q_ref, do_ref, st_ref, k_ref, v_ref, dq_ref, dk_ref, dv_ref):
    p = pl.program_id(0)
    mode = mtab[p]
    width = q_ref.shape[2] // heads

    @pl.when(mode == 0)
    def _():
        dq_ref[...] = jnp.zeros_like(dq_ref)
        dk_ref[...] = jnp.zeros_like(dk_ref)
        dv_ref[...] = jnp.zeros_like(dv_ref)

    @pl.when(mode > 0)
    def _():
        for h in range(heads):
            cols = slice(h * width, (h + 1) * width)
            stats = st_ref[0, :, cols].astype(jnp.float32)
            dq, dk, dv = pair_math(
                q_ref[0, :, cols], do_ref[0, :, cols], k_ref[:, cols], v_ref[:, cols],
                stats[0:1, :], stats[1:2, :], mode,
            )
            dq_ref[0, :, cols] = dq.astype(jnp.bfloat16)
            dk_ref[0, :, cols] = dk
            dv_ref[0, :, cols] = dv


def list_pairs(qin, qout, first, ktab, mtab, outs, queries, out_grad, norm3, delta3, key_src, value_src):
    rows, features = queries.shape
    heads = norm3.shape[0]
    height = rows // (2 * PAIR)
    count = ktab.shape[0]
    blk = (height, features)
    stat = (heads, 1, height)
    grid_spec = pltpu.PrefetchScalarGridSpec(
        num_scalar_prefetch=5,
        grid=(count,),
        in_specs=[
            pl.BlockSpec(blk, lambda p, qi, qo, f, kt, mt: (qi[p], 0)),
            pl.BlockSpec(blk, lambda p, qi, qo, f, kt, mt: (qi[p], 0)),
            pl.BlockSpec(stat, lambda p, qi, qo, f, kt, mt: (0, 0, qi[p])),
            pl.BlockSpec(stat, lambda p, qi, qo, f, kt, mt: (0, 0, qi[p])),
            pl.BlockSpec(blk, lambda p, qi, qo, f, kt, mt: (kt[p], 0)),
            pl.BlockSpec(blk, lambda p, qi, qo, f, kt, mt: (kt[p], 0)),
        ],
        out_specs=[
            pl.BlockSpec(blk, lambda p, qi, qo, f, kt, mt: (qo[p], 0)),
            pl.BlockSpec(blk, lambda p, qi, qo, f, kt, mt: (p, 0)),
            pl.BlockSpec(blk, lambda p, qi, qo, f, kt, mt: (p, 0)),
        ],
    )
    return pl.pallas_call(
        list_kernel,
        grid_spec=grid_spec,
        out_shape=[
            jax.ShapeDtypeStruct((outs * height, features), jnp.float32),
            jax.ShapeDtypeStruct((count * height, features), jnp.float32),
            jax.ShapeDtypeStruct((count * height, features), jnp.float32),
        ],
    )(qin, qout, first, ktab, mtab, queries, out_grad, norm3, delta3, key_src, value_src)


def rand_pairs(ftab, ktab, mtab, arrived, key_rows, value_rows, heads):
    items, packed_rows, features = arrived.shape
    height = (packed_rows - STAT_ROWS) // 2
    grid_spec = pltpu.PrefetchScalarGridSpec(
        num_scalar_prefetch=3,
        grid=(items,),
        in_specs=[
            pl.BlockSpec((1, height, features), lambda p, ft, kt, mt: (ft[p], 0, 0)),
            pl.BlockSpec((1, height, features), lambda p, ft, kt, mt: (ft[p], 1, 0)),
            pl.BlockSpec(
                (1, STAT_ROWS, features), lambda p, ft, kt, mt: (ft[p], 2 * height // STAT_ROWS, 0)
            ),
            pl.BlockSpec((height, features), lambda p, ft, kt, mt: (kt[p], 0)),
            pl.BlockSpec((height, features), lambda p, ft, kt, mt: (kt[p], 0)),
        ],
        out_specs=[
            pl.BlockSpec((1, height, features), lambda p, ft, kt, mt: (p, 0, 0)),
            pl.BlockSpec((1, height, features), lambda p, ft, kt, mt: (p, 0, 0)),
            pl.BlockSpec((1, height, features), lambda p, ft, kt, mt: (p, 0, 0)),
        ],
    )
    return pl.pallas_call(
        functools.partial(rand_kernel, heads),
        grid_spec=grid_spec,
        out_shape=[
            jax.ShapeDtypeStruct((items, height, features), jnp.bfloat16),
            jax.ShapeDtypeStruct((items, height, features), jnp.float32),
            jax.ShapeDtypeStruct((items, height, features), jnp.float32),
        ],
    )(ftab, ktab, mtab, arrived, arrived, arrived, key_rows, value_rows)


def shards(queries, key_rows, values, outputs, out_grad, log_norm, rand_blocks):
    ctx_size = lax.axis_size("ctx")
    my_index = lax.axis_index("ctx")
    row_count, features = queries.shape
    heads = log_norm.shape[0]
    slot_count = 2 * PAIR
    height = row_count // slot_count
    block_total = slot_count * ctx_size
    first_dev = my_index == 0
    last_dev = my_index == ctx_size - 1

    delta = jnp.sum(
        (out_grad.astype(jnp.float32) * outputs.astype(jnp.float32)).reshape(
            row_count, heads, features // heads
        ),
        axis=-1,
    )
    delta = jnp.transpose(delta).astype(jnp.bfloat16)
    norm3 = log_norm.astype(jnp.float32).reshape(heads, 1, row_count)
    delta3 = delta.astype(jnp.float32).reshape(heads, 1, row_count)

    def block(array, slot):
        return array[slot * height : (slot + 1) * height]

    from_left = shift(jnp.stack([block(key_rows, 1), block(values, 1)]), "ctx", 1)
    from_right = shift(jnp.stack([block(key_rows, 2), block(values, 2)]), "ctx", -1)
    global_kv = spread_2(jnp.stack([block(key_rows, 0), block(values, 0)]), "ctx", 0)
    key_win = jnp.concatenate([key_rows, from_left[0], from_right[0]])
    value_win = jnp.concatenate([values, from_left[1], from_right[1]])

    within = jnp.arange(slot_count, dtype=jnp.int32)
    seq_blk = jnp.where(
        within < PAIR, PAIR * my_index + within, block_total - 1 - PAIR * my_index - (within - PAIR)
    )
    last_prev = jnp.where(last_dev, 1, slot_count + 1).astype(jnp.int32)
    first_prev = jnp.where(first_dev, 0, 1).astype(jnp.int32)
    def table(*items):
        return jnp.stack([jnp.asarray(x, jnp.int32) for x in items])

    dq_own, dk_own, dv_own = list_pairs(
        table(0, 1, 1, 2, 2, 3), table(0, 1, 1, 2, 2, 3), table(1, 1, 0, 1, 0, 1),
        table(0, 1, 0, 2, 3, 3), table(2, 2, 1, 2, 1, 2), slot_count,
        queries, out_grad, norm3, delta3, key_rows, values,
    )
    dk_own = dk_own.reshape(6, height, features)
    dv_own = dv_own.reshape(6, height, features)
    dq_rim, dk_rim, dv_rim = list_pairs(
        table(0, slot_count - 1), table(0, 1), table(1, 1),
        table(slot_count, last_prev), table(first_prev, 1), 2,
        queries, out_grad, norm3, delta3, key_win, value_win,
    )
    dq_rim = dq_rim.reshape(2, height, features)
    dk_rim = dk_rim.reshape(2, height, features)
    dv_rim = dv_rim.reshape(2, height, features)
    glob_mode = (seq_blk >= WINDOW).astype(jnp.int32)
    dq_glob, dk_glob, dv_glob = list_pairs(
        table(0, 1, 2, 3), table(0, 1, 2, 3), table(1, 1, 1, 1), table(0, 0, 0, 0), glob_mode,
        slot_count, queries, out_grad, norm3, delta3, global_kv[0], global_kv[1],
    )
    zero_blk = jnp.zeros((height, features), jnp.float32)
    dq_local = (
        dq_own + dq_glob
        + jnp.concatenate([dq_rim[0:1], zero_blk[None], zero_blk[None], dq_rim[1:2]]).reshape(
            row_count, features
        )
    )

    to_left = jnp.stack([dk_rim[0], dv_rim[0]]).astype(jnp.bfloat16)
    to_right = jnp.stack([dk_rim[1], dv_rim[1]]).astype(jnp.bfloat16)
    back_right = shift(to_left, "ctx", -1)
    back_left = shift(to_right, "ctx", 1)

    part = jnp.stack(
        [
            jnp.sum(dk_glob.reshape(slot_count, height, features), axis=0),
            jnp.sum(dv_glob.reshape(slot_count, height, features), axis=0),
        ]
    )
    total = gather_to_root(part, "ctx")

    ref_valid = rand_blocks >= 0
    in_front = rand_blocks < block_total // 2
    mirror = block_total - 1 - rand_blocks
    owner_dev = jnp.where(in_front, rand_blocks // PAIR, mirror // PAIR)
    owner_dev = jnp.where(ref_valid, owner_dev, ctx_size).reshape(-1)
    key_slot = jnp.where(in_front, rand_blocks % PAIR, PAIR + mirror % PAIR) + 1
    key_slot = jnp.where(ref_valid, key_slot, 0).reshape(-1)
    targets = jnp.arange(ctx_size, dtype=jnp.int32)
    matches = owner_dev[None, :] == targets[:, None]
    slot_send = jnp.sum(jnp.where(matches, key_slot[None, :], 0), axis=1)
    select = jnp.any(matches.reshape(ctx_size, slot_count, RANDOM), axis=2).astype(jnp.bfloat16)

    def per_slot_row(stat):
        return jnp.transpose(stat.reshape(heads, slot_count, height), (1, 0, 2)).reshape(
            slot_count, 1, features
        )

    packed = jnp.concatenate(
        [
            queries.reshape(slot_count, height, features),
            out_grad.reshape(slot_count, height, features),
            per_slot_row(log_norm),
            per_slot_row(delta),
            jnp.zeros((slot_count, STAT_ROWS - 2, features), jnp.bfloat16),
        ],
        axis=1,
    )
    pick = select > 0
    row_id = lax.broadcasted_iota(jnp.int32, (1, packed.shape[1], 1), 1)
    routed = jnp.where(
        row_id == 2 * height + 2, slot_send.astype(jnp.bfloat16)[:, None, None], jnp.bfloat16(0)
    )
    for slot in range(slot_count):
        routed = routed + jnp.where(pick[:, slot, None, None], packed[slot][None], jnp.bfloat16(0))
    arrived = lax.all_to_all(routed, "ctx", split_axis=0, concat_axis=0, tiled=True)
    slot_recv = arrived[:, 2 * height + 2, 0].astype(jnp.float32).astype(jnp.int32)
    ktab_r = jnp.maximum(slot_recv - 1, 0)
    mtab_r = (slot_recv > 0).astype(jnp.int32)
    item_ids = jnp.arange(ctx_size, dtype=jnp.int32)
    ftab_r = lax.cummax(jnp.where(mtab_r > 0, item_ids, 0), axis=0)
    dq_rand, dk_rand, dv_rand = rand_pairs(ftab_r, ktab_r, mtab_r, arrived, key_rows, values, heads)
    dq_rand, total, back_left, back_right = lax.optimization_barrier(
        (dq_rand, total, back_left, back_right)
    )
    back_left = back_left.astype(jnp.float32)
    back_right = back_right.astype(jnp.float32)
    returned = lax.all_to_all(dq_rand, "ctx", split_axis=0, concat_axis=0, tiled=True)
    select_f = select.astype(jnp.float32)
    rand_query = jnp.sum(
        select_f[:, :, None, None] * returned.astype(jnp.float32)[:, None], axis=0
    )
    choose = (slot_recv[:, None] == jnp.arange(1, slot_count + 1)[None, :]).astype(jnp.float32)
    rand_key = jnp.sum(choose[:, :, None, None] * dk_rand[:, None], axis=0)
    rand_value = jnp.sum(choose[:, :, None, None] * dv_rand[:, None], axis=0)

    own_tail = jnp.where(last_dev, 1.0, 0.0).astype(jnp.float32)

    owner_flag = jnp.where(first_dev, 1.0, 0.0).astype(jnp.float32)

    def assemble(own, rim, which, rand_part):
        slots = [
            own[0] + own[2] + total[which] * owner_flag,
            own[1] + rim[1] * own_tail + back_right[which],
            own[3] + back_left[which],
            own[5] + own[4],
        ]
        whole = jnp.stack(slots) + rand_part
        return whole.reshape(row_count, features).astype(jnp.bfloat16)

    query_total = (dq_local + rand_query.reshape(row_count, features)).astype(jnp.bfloat16)
    return (
        query_total,
        assemble(dk_own, dk_rim, 0, rand_key),
        assemble(dv_own, dv_rim, 1, rand_value),
    )


def solution(mesh):
    return jax.shard_map(
        shards,
        mesh=mesh,
        in_specs=(
            P("ctx", "head"),
            P("ctx", "head"),
            P("ctx", "head"),
            P("ctx", "head"),
            P("ctx", "head"),
            P("head", "ctx"),
            P("ctx", None),
        ),
        out_specs=(P("ctx", "head"), P("ctx", "head"), P("ctx", "head")),
        check_vma=False,
    )
```

```python
import functools

import jax
import jax.numpy as jnp
from jax import lax
from jax.experimental import pallas as pl
from jax.experimental.pallas import tpu as pltpu
from jax.sharding import PartitionSpec as P

PAIR = 2
WINDOW = 2
GLOBAL = 1
RANDOM = 3
STAT_ROWS = 8


RADIX = 4


def spread_2(array, axis, root):
    count = lax.axis_size(axis)
    mine = lax.axis_index(axis) == root
    array = jnp.where(mine, array, jnp.zeros_like(array))
    step = 1
    while step * RADIX < count:
        step *= RADIX
    while step >= 1:
        arrived = [
            lax.ppermute(array, axis, [(i, i + j * step) for i in range(0, count, RADIX * step) if i + j * step < count])
            for j in range(1, RADIX)
            if j * step < count
        ]
        for part in arrived:
            array = array + part
        step //= RADIX
    return array


def gather_to_root(array, axis):
    count = lax.axis_size(axis)
    step = 1
    while step < count:
        sent = array.astype(jnp.bfloat16)
        arrived = [
            lax.ppermute(sent, axis, [(i + j * step, i) for i in range(0, count, RADIX * step) if i + j * step < count])
            for j in range(1, RADIX)
            if j * step < count
        ]
        for part in arrived:
            array = array + part.astype(jnp.float32)
        step *= RADIX
    return array


def shift(array, axis, offset):
    count = lax.axis_size(axis)
    pairs = [(i, i + offset) for i in range(count) if 0 <= i + offset < count]
    return lax.ppermute(array, axis, pairs)


def pair_math(q, do, k, v, nrm, dlt, mode):
    scale = q.shape[-1] ** (-0.5)
    nt = (((1,), (1,)), ((), ()))
    s_t = lax.dot_general(k, q, nt, preferred_element_type=jnp.float32) * scale
    rows = lax.broadcasted_iota(jnp.int32, s_t.shape, 0)
    cols = lax.broadcasted_iota(jnp.int32, s_t.shape, 1)
    full = (mode == 1).astype(jnp.float32)
    causal = (mode == 2).astype(jnp.float32)
    visible = full + causal * (rows <= cols).astype(jnp.float32)
    p_t = jnp.exp(s_t - nrm) * visible
    dv = jnp.dot(p_t.astype(jnp.bfloat16), do, preferred_element_type=jnp.float32)
    dp_t = lax.dot_general(v, do, nt, preferred_element_type=jnp.float32)
    ds_t = (p_t * (dp_t - dlt)).astype(jnp.bfloat16)
    dk = jnp.dot(ds_t, q, preferred_element_type=jnp.float32) * scale
    tn = (((0,), (0,)), ((), ()))
    dq = lax.dot_general(ds_t, k, tn, preferred_element_type=jnp.float32) * scale
    return dq, dk, dv


def list_kernel(qin, qout, first, ktab, mtab, q_ref, do_ref, nrm_ref, dlt_ref, k_ref, v_ref, dq_ref, dk_ref, dv_ref):
    p = pl.program_id(0)
    mode = mtab[p]
    lead = first[p]
    heads = nrm_ref.shape[0]
    width = q_ref.shape[1] // heads
    for h in range(heads):
        cols = slice(h * width, (h + 1) * width)
        dq, dk, dv = pair_math(
            q_ref[:, cols], do_ref[:, cols], k_ref[:, cols], v_ref[:, cols],
            nrm_ref[h], dlt_ref[h], mode,
        )

        @pl.when(lead == 1)
        def _():
            dq_ref[:, cols] = dq

        @pl.when(lead == 0)
        def _():
            dq_ref[:, cols] += dq

        dk_ref[:, cols] = dk
        dv_ref[:, cols] = dv


def rand_kernel(heads, ktab, mtab, q_ref, do_ref, st_ref, k_ref, v_ref, dq_ref, dk_ref, dv_ref):
    p = pl.program_id(0)
    mode = mtab[p]
    width = q_ref.shape[2] // heads

    @pl.when(mode == 0)
    def _():
        dq_ref[...] = jnp.zeros_like(dq_ref)
        dk_ref[...] = jnp.zeros_like(dk_ref)
        dv_ref[...] = jnp.zeros_like(dv_ref)

    @pl.when(mode > 0)
    def _():
        for h in range(heads):
            cols = slice(h * width, (h + 1) * width)
            stats = st_ref[0, :, cols].astype(jnp.float32)
            dq, dk, dv = pair_math(
                q_ref[0, :, cols], do_ref[0, :, cols], k_ref[:, cols], v_ref[:, cols],
                stats[0:1, :], stats[1:2, :], mode,
            )
            dq_ref[0, :, cols] = dq.astype(jnp.bfloat16)
            dk_ref[0, :, cols] = dk
            dv_ref[0, :, cols] = dv


def list_pairs(qin, qout, first, ktab, mtab, outs, queries, out_grad, norm3, delta3, key_src, value_src):
    rows, features = queries.shape
    heads = norm3.shape[0]
    height = rows // (2 * PAIR)
    count = ktab.shape[0]
    blk = (height, features)
    stat = (heads, 1, height)
    grid_spec = pltpu.PrefetchScalarGridSpec(
        num_scalar_prefetch=5,
        grid=(count,),
        in_specs=[
            pl.BlockSpec(blk, lambda p, qi, qo, f, kt, mt: (qi[p], 0)),
            pl.BlockSpec(blk, lambda p, qi, qo, f, kt, mt: (qi[p], 0)),
            pl.BlockSpec(stat, lambda p, qi, qo, f, kt, mt: (0, 0, qi[p])),
            pl.BlockSpec(stat, lambda p, qi, qo, f, kt, mt: (0, 0, qi[p])),
            pl.BlockSpec(blk, lambda p, qi, qo, f, kt, mt: (kt[p], 0)),
            pl.BlockSpec(blk, lambda p, qi, qo, f, kt, mt: (kt[p], 0)),
        ],
        out_specs=[
            pl.BlockSpec(blk, lambda p, qi, qo, f, kt, mt: (qo[p], 0)),
            pl.BlockSpec(blk, lambda p, qi, qo, f, kt, mt: (p, 0)),
            pl.BlockSpec(blk, lambda p, qi, qo, f, kt, mt: (p, 0)),
        ],
    )
    return pl.pallas_call(
        list_kernel,
        grid_spec=grid_spec,
        out_shape=[
            jax.ShapeDtypeStruct((outs * height, features), jnp.float32),
            jax.ShapeDtypeStruct((count * height, features), jnp.float32),
            jax.ShapeDtypeStruct((count * height, features), jnp.float32),
        ],
    )(qin, qout, first, ktab, mtab, queries, out_grad, norm3, delta3, key_src, value_src)


def rand_pairs(ktab, mtab, arrived, key_rows, value_rows, heads):
    items, packed_rows, features = arrived.shape
    height = (packed_rows - STAT_ROWS) // 2
    grid_spec = pltpu.PrefetchScalarGridSpec(
        num_scalar_prefetch=2,
        grid=(items,),
        in_specs=[
            pl.BlockSpec((1, height, features), lambda p, kt, mt: (p, 0, 0)),
            pl.BlockSpec((1, height, features), lambda p, kt, mt: (p, 1, 0)),
            pl.BlockSpec(
                (1, STAT_ROWS, features), lambda p, kt, mt: (p, 2 * height // STAT_ROWS, 0)
            ),
            pl.BlockSpec((height, features), lambda p, kt, mt: (kt[p], 0)),
            pl.BlockSpec((height, features), lambda p, kt, mt: (kt[p], 0)),
        ],
        out_specs=[
            pl.BlockSpec((1, height, features), lambda p, kt, mt: (p, 0, 0)),
            pl.BlockSpec((1, height, features), lambda p, kt, mt: (p, 0, 0)),
            pl.BlockSpec((1, height, features), lambda p, kt, mt: (p, 0, 0)),
        ],
    )
    return pl.pallas_call(
        functools.partial(rand_kernel, heads),
        grid_spec=grid_spec,
        out_shape=[
            jax.ShapeDtypeStruct((items, height, features), jnp.bfloat16),
            jax.ShapeDtypeStruct((items, height, features), jnp.float32),
            jax.ShapeDtypeStruct((items, height, features), jnp.float32),
        ],
    )(ktab, mtab, arrived, arrived, arrived, key_rows, value_rows)


def shards(queries, key_rows, values, outputs, out_grad, log_norm, rand_blocks):
    ctx_size = lax.axis_size("ctx")
    my_index = lax.axis_index("ctx")
    row_count, features = queries.shape
    heads = log_norm.shape[0]
    slot_count = 2 * PAIR
    height = row_count // slot_count
    block_total = slot_count * ctx_size
    first_dev = my_index == 0
    last_dev = my_index == ctx_size - 1

    delta = jnp.sum(
        (out_grad.astype(jnp.float32) * outputs.astype(jnp.float32)).reshape(
            row_count, heads, features // heads
        ),
        axis=-1,
    )
    delta = jnp.transpose(delta).astype(jnp.bfloat16)
    norm3 = log_norm.astype(jnp.float32).reshape(heads, 1, row_count)
    delta3 = delta.astype(jnp.float32).reshape(heads, 1, row_count)

    def block(array, slot):
        return array[slot * height : (slot + 1) * height]

    from_left = shift(jnp.stack([block(key_rows, 1), block(values, 1)]), "ctx", 1)
    from_right = shift(jnp.stack([block(key_rows, 2), block(values, 2)]), "ctx", -1)
    global_kv = spread_2(jnp.stack([block(key_rows, 0), block(values, 0)]), "ctx", 0)
    key_win = jnp.concatenate([key_rows, from_left[0], from_right[0]])
    value_win = jnp.concatenate([values, from_left[1], from_right[1]])

    within = jnp.arange(slot_count, dtype=jnp.int32)
    seq_blk = jnp.where(
        within < PAIR, PAIR * my_index + within, block_total - 1 - PAIR * my_index - (within - PAIR)
    )
    last_prev = jnp.where(last_dev, 1, slot_count + 1).astype(jnp.int32)
    first_prev = jnp.where(first_dev, 0, 1).astype(jnp.int32)
    def table(*items):
        return jnp.stack([jnp.asarray(x, jnp.int32) for x in items])

    dq_own, dk_own, dv_own = list_pairs(
        table(0, 1, 1, 2, 2, 3), table(0, 1, 1, 2, 2, 3), table(1, 1, 0, 1, 0, 1),
        table(0, 1, 0, 2, 3, 3), table(2, 2, 1, 2, 1, 2), slot_count,
        queries, out_grad, norm3, delta3, key_rows, values,
    )
    dk_own = dk_own.reshape(6, height, features)
    dv_own = dv_own.reshape(6, height, features)
    dq_rim, dk_rim, dv_rim = list_pairs(
        table(0, slot_count - 1), table(0, 1), table(1, 1),
        table(slot_count, last_prev), table(first_prev, 1), 2,
        queries, out_grad, norm3, delta3, key_win, value_win,
    )
    dq_rim = dq_rim.reshape(2, height, features)
    dk_rim = dk_rim.reshape(2, height, features)
    dv_rim = dv_rim.reshape(2, height, features)
    glob_mode = (seq_blk >= WINDOW).astype(jnp.int32)
    dq_glob, dk_glob, dv_glob = list_pairs(
        table(0, 1, 2, 3), table(0, 1, 2, 3), table(1, 1, 1, 1), table(0, 0, 0, 0), glob_mode,
        slot_count, queries, out_grad, norm3, delta3, global_kv[0], global_kv[1],
    )
    zero_blk = jnp.zeros((height, features), jnp.float32)
    dq_local = (
        dq_own + dq_glob
        + jnp.concatenate([dq_rim[0:1], zero_blk[None], zero_blk[None], dq_rim[1:2]]).reshape(
            row_count, features
        )
    )

    to_left = jnp.stack([dk_rim[0], dv_rim[0]]).astype(jnp.bfloat16)
    to_right = jnp.stack([dk_rim[1], dv_rim[1]]).astype(jnp.bfloat16)
    back_right = shift(to_left, "ctx", -1)
    back_left = shift(to_right, "ctx", 1)

    part = jnp.stack(
        [
            jnp.sum(dk_glob.reshape(slot_count, height, features), axis=0),
            jnp.sum(dv_glob.reshape(slot_count, height, features), axis=0),
        ]
    )
    total = gather_to_root(part, "ctx")

    ref_valid = rand_blocks >= 0
    in_front = rand_blocks < block_total // 2
    mirror = block_total - 1 - rand_blocks
    owner_dev = jnp.where(in_front, rand_blocks // PAIR, mirror // PAIR)
    owner_dev = jnp.where(ref_valid, owner_dev, ctx_size).reshape(-1)
    key_slot = jnp.where(in_front, rand_blocks % PAIR, PAIR + mirror % PAIR) + 1
    key_slot = jnp.where(ref_valid, key_slot, 0).reshape(-1)
    targets = jnp.arange(ctx_size, dtype=jnp.int32)
    matches = owner_dev[None, :] == targets[:, None]
    slot_send = jnp.sum(jnp.where(matches, key_slot[None, :], 0), axis=1)
    select = jnp.any(matches.reshape(ctx_size, slot_count, RANDOM), axis=2).astype(jnp.bfloat16)

    def per_slot_row(stat):
        return jnp.transpose(stat.reshape(heads, slot_count, height), (1, 0, 2)).reshape(
            slot_count, 1, features
        )

    packed = jnp.concatenate(
        [
            queries.reshape(slot_count, height, features),
            out_grad.reshape(slot_count, height, features),
            per_slot_row(log_norm),
            per_slot_row(delta),
            jnp.zeros((slot_count, STAT_ROWS - 2, features), jnp.bfloat16),
        ],
        axis=1,
    )
    pick = select > 0
    row_id = lax.broadcasted_iota(jnp.int32, (1, packed.shape[1], 1), 1)
    routed = jnp.where(
        row_id == 2 * height + 2, slot_send.astype(jnp.bfloat16)[:, None, None], jnp.bfloat16(0)
    )
    for slot in range(slot_count):
        routed = routed + jnp.where(pick[:, slot, None, None], packed[slot][None], jnp.bfloat16(0))
    arrived = lax.all_to_all(routed, "ctx", split_axis=0, concat_axis=0, tiled=True)
    slot_recv = arrived[:, 2 * height + 2, 0].astype(jnp.float32).astype(jnp.int32)
    ktab_r = jnp.maximum(slot_recv - 1, 0)
    mtab_r = (slot_recv > 0).astype(jnp.int32)
    dq_rand, dk_rand, dv_rand = rand_pairs(ktab_r, mtab_r, arrived, key_rows, values, heads)
    dq_rand, total, back_left, back_right = lax.optimization_barrier(
        (dq_rand, total, back_left, back_right)
    )
    back_left = back_left.astype(jnp.float32)
    back_right = back_right.astype(jnp.float32)
    returned = lax.all_to_all(dq_rand, "ctx", split_axis=0, concat_axis=0, tiled=True)
    select_f = select.astype(jnp.float32)
    rand_query = jnp.sum(
        select_f[:, :, None, None] * returned.astype(jnp.float32)[:, None], axis=0
    )
    choose = (slot_recv[:, None] == jnp.arange(1, slot_count + 1)[None, :]).astype(jnp.float32)
    rand_key = jnp.sum(choose[:, :, None, None] * dk_rand[:, None], axis=0)
    rand_value = jnp.sum(choose[:, :, None, None] * dv_rand[:, None], axis=0)

    own_tail = jnp.where(last_dev, 1.0, 0.0).astype(jnp.float32)

    owner_flag = jnp.where(first_dev, 1.0, 0.0).astype(jnp.float32)

    def assemble(own, rim, which, rand_part):
        slots = [
            own[0] + own[2] + total[which] * owner_flag,
            own[1] + rim[1] * own_tail + back_right[which],
            own[3] + back_left[which],
            own[5] + own[4],
        ]
        whole = jnp.stack(slots) + rand_part
        return whole.reshape(row_count, features).astype(jnp.bfloat16)

    query_total = (dq_local + rand_query.reshape(row_count, features)).astype(jnp.bfloat16)
    return (
        query_total,
        assemble(dk_own, dk_rim, 0, rand_key),
        assemble(dv_own, dv_rim, 1, rand_value),
    )


def solution(mesh):
    return jax.shard_map(
        shards,
        mesh=mesh,
        in_specs=(
            P("ctx", "head"),
            P("ctx", "head"),
            P("ctx", "head"),
            P("ctx", "head"),
            P("ctx", "head"),
            P("head", "ctx"),
            P("ctx", None),
        ),
        out_specs=(P("ctx", "head"), P("ctx", "head"), P("ctx", "head")),
        check_vma=False,
    )
```
